128 devices in a mesh: req: 8 (over y, core), exp: 16 (over z, x).
Axes of the slice: x: 4, y: 4, z: 4, core: 2. Of those that a mesh axis runs over, the one named last changes fastest.
Arguments:
- hidden: bfloat16 [16384, 2560], P(('req', 'exp')), may hold values from -1.5 to 1.5
- queries: bfloat16 [16384, 1280], P(('req', 'exp')), may hold values from -100 to 100
- suffix_kv: bfloat16 [16384, 512], P(('req', 'exp')), may hold values from -24 to 24
- lengths: int32 [8, 4], P('req'), may hold values from 1 to 1024, 2048 in all within a row
- page_table: int32 [8, 4, 32], P('req'), may hold values from 0 to 55
- page_pool: bfloat16 [56, 128, 512], P('req'), may hold values from -24 to 24
- w_out: bfloat16 [1280, 2560], replicated, may hold values from -0.15625 to 0.15625
- w_router: bfloat16 [2560, 64], replicated, may hold values from -5 to 5
- routes: int32 [16384, 6], P(('req', 'exp')), may hold values from 0 to 63, all different within a row; in each aligned block of 128 rows (0 to 127, 128 to 255, ...) at most 15 rows name the same one
- w_gate: bfloat16 [128, 2560, 768], P(('req', 'exp')), may hold values from -0.125 to 0.125
- w_up: bfloat16 [128, 2560, 768], P(('req', 'exp')), may hold values from -0.125 to 0.125
- w_down: bfloat16 [128, 768, 2560], P(('req', 'exp')), may hold values from -0.4375 to 0.4375
Outputs:
- layer_out: bfloat16 [16384, 2560], P(('req', 'exp'))
The draws below stay inside these ranges and needn't reach their ends.
Inputs may be any that keep to these rules, and one draw needn't show every extreme that they name: `lengths`: each row sums to 2048; its largest entry is exactly 1024. `page_table`: a page may appear in several prefixes and more than once in one. `routes`: the 6 experts of a token are distinct; among the rows of one device no expert is named more than 15 times, a bound that some block reaches.
All inputs are finite; a program needn't handle non-finite values.
Results may differ from the reference program's by a relative error of at most 0.022.
Values may be sent and summed in bfloat16 or wider, within the bound.
No kernel may reach another device: no remote copies, remote signals or barrier semaphores. Data moves between devices by JAX's collectives and lax.ppermute only.
A program may use at most 192 MiB of HBM per device.

```python
import math
import jax
import jax.numpy as jnp
import numpy as np
from jax import lax

D = 2560
QUERY_HEADS = 10
KEY_VALUE_HEADS = 2
HEAD_SIZE = 128
FF_E = 1536
TOP = 6
PAGE_TOKENS = 128
REQS = 4
PREFIX_PAGES = 32
TOK_DEV = 128
FF_HALF = 768
EXPERTS = 64
GROUP_TOKENS = 2048
SUFFIX_TOKENS = 16384
POOL_PAGES_COUNT = 56
MOST_LEN = 1024
CAP = 15
N_REQ = 8
N_EXP = 16


def suffix_pair(key):
    key_portion = jax.random.normal(jax.random.fold_in(key, 1), (SUFFIX_TOKENS, KEY_VALUE_HEADS * HEAD_SIZE), jnp.float32)
    value_portion = 6.0 * jax.random.normal(jax.random.fold_in(key, 2), (SUFFIX_TOKENS, KEY_VALUE_HEADS * HEAD_SIZE), jnp.float32)
    return (jnp.clip(key_portion, -4.0, 4.0), jnp.clip(value_portion, -24.0, 24.0))


def draw_suffix_kv(key, part):
    key_portion, value_portion = suffix_pair(jax.random.fold_in(key, 7))
    return jnp.concatenate([key_portion, value_portion], axis=1).astype(jnp.bfloat16)


def draw_queries(key, part):
    base = jnp.clip(2.0 * jax.random.normal(jax.random.fold_in(key, 3), (SUFFIX_TOKENS, QUERY_HEADS * HEAD_SIZE), jnp.float32), -12.0, 12.0)
    return jnp.clip(base, -100.0, 100.0).astype(jnp.bfloat16)


def draw_page_pool(key, part):
    array_shape = (POOL_PAGES_COUNT, PAGE_TOKENS, KEY_VALUE_HEADS * HEAD_SIZE)
    key_portion = jax.random.normal(jax.random.fold_in(key, 21), array_shape, jnp.float32)
    value_portion = 6.0 * jax.random.normal(jax.random.fold_in(key, 22), array_shape, jnp.float32)
    key_portion = jnp.clip(key_portion, -4.0, 4.0)
    value_portion = jnp.clip(value_portion, -24.0, 24.0)
    return jnp.concatenate([key_portion, value_portion], axis=2).astype(jnp.bfloat16)


def draw_w_router(key, part):
    noise = jax.random.normal(jax.random.fold_in(key, 31), (D, EXPERTS), jnp.float32)
    value_rows = 0.5 / math.sqrt(D) * noise
    return jnp.clip(value_rows, -5.0, 5.0).astype(jnp.bfloat16)


def touch_ends(values, rng, smallest, high):
    spot = [jax.random.randint(jax.random.fold_in(rng, axis), (), 0, length) for axis, length in enumerate(values.shape)]
    longest = values.shape.index(max(values.shape))
    beside = spot[:longest] + [(spot[longest] + 1) % values.shape[longest]] + spot[longest + 1:]
    return values.at[tuple(spot)].set(smallest).at[tuple(beside)].set(high)


def steps_of(own_key, shape, cuts, least, largest):
    loudness, own = 1.0, jax.random.fold_in(own_key, 6)
    for axis_at, shards_of in cuts:
        heights = jnp.exp(jax.random.uniform(jax.random.fold_in(own, axis_at), (shards_of,), jnp.float32, least / len(cuts), largest / len(cuts)))
        loudness = loudness * jnp.repeat(heights, shape[axis_at] // shards_of).reshape([-1 if axis == axis_at else 1 for axis in range(len(shape))])
    return loudness


def split_up(amount, total, most, slope):
    loads = [(1 << 20) // math.isqrt(standing ** slope) + 1 for standing in range(2, amount + 1)]
    surplus, holding = total - most - (amount - 1), [1] * (amount - 1)
    while surplus > 0:
        movable = [i for i in range(amount - 1) if holding[i] < most]
        pool, budget = sum([loads[i] for i in movable]), surplus
        for i in movable:
            addition = min(most - holding[i], max(1, budget * loads[i] // pool), surplus)
            holding[i] = holding[i] + addition
            surplus = surplus - addition
    return np.array([most] + holding)


def ragged_sizes(stream_key, amount, total, limit, skew):
    if amount == 2:
        one = jax.random.randint(stream_key, (), max(1, total - limit), min(limit, total - 1) + 1)
        return jnp.stack([one, total - one])
    tallies = jnp.asarray(split_up(amount, total, limit, skew), jnp.int32)
    couples = (amount - 1) // 2
    source_of, taker = tallies[1:1 + 2 * couples:2], tallies[2:2 + 2 * couples:2]
    margin = jnp.minimum(source_of - 1, limit - taker)
    passed = jax.random.randint(jax.random.fold_in(stream_key, 1), (couples,), 0, 1 << 20) % (margin + 1)
    tallies = tallies.at[1:1 + 2 * couples:2].set(source_of - passed).at[2:2 + 2 * couples:2].set(taker + passed)
    return tallies[jax.random.permutation(jax.random.fold_in(stream_key, 2), amount)]


def shared_out(stream_key, own, number, rows, amount, top, reach, lean):
    ranking = jax.random.permutation(stream_key, amount)
    heavy_load, usual = load_shares(amount, rows * top, reach, lean, True), load_shares(amount, rows * top, reach, lean, False)
    places = jnp.arange(amount)

    def named(tallies, offset_by):
        used = int((tallies > 0).sum())
        fixed = max(1, used // 4)
        moved = fixed + (places - fixed + offset_by * (used - fixed)) % max(1, amount - fixed)
        return jnp.zeros((amount,), jnp.int32).at[ranking[jnp.where(places < fixed, places, moved)]].set(jnp.asarray(tallies, jnp.int32))

    tallies = jnp.where(number % 4 == 0, named(heavy_load, number // 4), named(usual, number - number // 4 - 1))
    mixed = jax.random.permutation(jax.random.fold_in(own, 3), amount)
    source_of, receiver = mixed[0:amount // 2 * 2:2], mixed[1:amount // 2 * 2:2]
    room = jnp.minimum(tallies[source_of] - 1, reach - tallies[receiver]) // 2
    room = jnp.where((source_of == ranking[0]) | (receiver == ranking[0]) | (tallies[receiver] == 0), 0, jnp.maximum(room, 0))
    moved = jax.random.randint(jax.random.fold_in(own, 4), (amount // 2,), 0, 1 << 20) % (room + 1)
    tallies = tallies.at[source_of].add(-moved).at[receiver].add(moved)
    items = jnp.searchsorted(jnp.cumsum(tallies), jnp.arange(rows * top), side="right").astype(jnp.int32)
    listing = items.reshape(top, rows).T
    listing = listing[jax.random.permutation(jax.random.fold_in(own, 1), rows)]
    offset_by = jax.random.randint(jax.random.fold_in(own, 2), (rows, 1), 0, top)
    return jnp.take_along_axis(listing, (jnp.arange(top)[None, :] + offset_by) % top, axis=1)


def load_shares(number_of, total, most, skew, full):
    weights = [(1 << 20) // math.isqrt(standing ** skew) + 1 for standing in range(1, number_of + 1)]
    largest = most if full else min(most, max(-(-total // number_of), total * weights[0] // sum(weights)))
    least = 1 if total - largest >= number_of - 1 else 0
    given, rest = [largest] + [least] * (number_of - 1), total - largest - least * (number_of - 1)
    while rest > 0:
        free = [i for i in range(1, number_of) if given[i] < largest] or [i for i in range(1, number_of) if given[i] < most]
        pool, remaining = sum([weights[i] for i in free]), rest
        for i in free:
            extra = min(most - given[i], max(1, remaining * weights[i] // pool), rest)
            given[i] = given[i] + extra
            rest = rest - extra
    return np.array(given)


def normal_values(stream_key, shape, scale, reach, pieces=(), kind=jnp.bfloat16):
    factor_of = steps_of(stream_key, shape, pieces, -0.22, 0.18) if pieces else 1.0
    values = jax.random.normal(stream_key, shape, jnp.float32) * scale * factor_of
    return jnp.minimum(jnp.maximum(values, -reach), reach).astype(kind)


def setup_inputs(seed: int = 0) -> dict:
    keys = jax.random.split(jax.random.key(seed), 13)
    hidden = normal_values(keys[0], (SUFFIX_TOKENS, D), 0.25, 1.5, ((0, 128),))
    queries = draw_queries(jax.random.fold_in(keys[12], 71), 0)
    suffix_kv = draw_suffix_kv(jax.random.fold_in(keys[12], 71), 0)
    lengths = jax.vmap(lambda own: ragged_sizes(own, REQS, GROUP_TOKENS, MOST_LEN, 2))(jax.random.split(keys[3], N_REQ)).reshape((N_REQ, REQS)).astype(jnp.int32)
    page_table = touch_ends(jax.random.randint(keys[4], (N_REQ, REQS, PREFIX_PAGES), 0, POOL_PAGES_COUNT), jax.random.fold_in(keys[4], 1), 0, POOL_PAGES_COUNT - 1).astype(jnp.int32)
    page_pool = draw_page_pool(jax.random.fold_in(keys[12], 71), 0)
    w_out = normal_values(keys[6], (QUERY_HEADS * HEAD_SIZE, D), (QUERY_HEADS * HEAD_SIZE) ** -0.5, 0.15625)
    w_router = draw_w_router(jax.random.fold_in(keys[12], 71), 0)
    routes_keys = jax.random.split(jax.random.fold_in(keys[8], 1), SUFFIX_TOKENS // TOK_DEV)
    routes_turns = jax.random.permutation(jax.random.fold_in(keys[8], 3), SUFFIX_TOKENS // TOK_DEV)
    routes = jax.vmap(lambda own, number: shared_out(jax.random.fold_in(keys[8], 2), own, number, TOK_DEV, EXPERTS, TOP, CAP, 1))(routes_keys, routes_turns).reshape((SUFFIX_TOKENS, TOP))
    w_gate = normal_values(keys[9], (2 * EXPERTS, D, FF_HALF), D ** -0.5, 0.125, ((0, 128),))
    w_up = normal_values(keys[10], (2 * EXPERTS, D, FF_HALF), D ** -0.5, 0.125, ((0, 128),))
    w_down = normal_values(keys[11], (2 * EXPERTS, FF_HALF, D), (FF_E // 8) ** -0.5, 0.4375, ((0, 128),))
    return {"hidden": hidden, "queries": queries, "suffix_kv": suffix_kv, "lengths": lengths, "page_table": page_table, "page_pool": page_pool, "w_out": w_out, "w_router": w_router, "routes": routes, "w_gate": w_gate, "w_up": w_up, "w_down": w_down}


NEGATIVE_MASK = -1e+30
EPS = 1e-06

def weighted_softmax(scores, weights, value_rows):
    live = weights[:, None, None, :] > 0
    running_maximum = lax.optimization_barrier(jnp.max(jnp.where(live, scores, NEGATIVE_MASK), axis=-1, keepdims=True))
    expo = jnp.where(live, jnp.exp(scores - running_maximum), 0.0) * weights[:, None, None, :]
    grand_total = lax.optimization_barrier(jnp.sum(expo, axis=-1))
    rounded = lax.optimization_barrier(expo.astype(jnp.bfloat16)).astype(jnp.float32)
    summed_output = jnp.einsum('tgrk,kgd->tgrd', rounded, value_rows.astype(jnp.float32))
    return summed_output / grand_total[..., None]

def reference(hidden, queries, suffix_kv, lengths, page_table, page_pool, w_out, w_router, routes, w_gate, w_up, w_down):
    row_width = KEY_VALUE_HEADS * HEAD_SIZE
    flattened_pool = page_pool.reshape(POOL_PAGES_COUNT * PAGE_TOKENS, 2 * row_width)
    pooled_keys = flattened_pool[:, :row_width].reshape(POOL_PAGES_COUNT * PAGE_TOKENS, KEY_VALUE_HEADS, HEAD_SIZE)
    pooled_values = flattened_pool[:, row_width:].reshape(POOL_PAGES_COUNT * PAGE_TOKENS, KEY_VALUE_HEADS, HEAD_SIZE)
    query_block = min(512, GROUP_TOKENS)

    def group_attention(xs):
        query_group, key_value_group, lens, table = xs
        positions = jnp.arange(GROUP_TOKENS, dtype=jnp.int32)
        ends = jnp.cumsum(lens).astype(jnp.int32)
        starts = (ends - lens).astype(jnp.int32)
        req_of = lax.optimization_barrier(jnp.sum((positions[:, None] >= ends[None, :]).astype(jnp.int32), axis=1))
        pick = req_of[:, None] == jnp.arange(REQS, dtype=jnp.int32)[None, :]
        first = lax.optimization_barrier(jnp.sum(jnp.where(pick, starts[None, :], 0), axis=1)).astype(jnp.int32)
        counts = lax.optimization_barrier(jnp.sum((table[:, :, None] == jnp.arange(POOL_PAGES_COUNT, dtype=jnp.int32)[None, None, :]).astype(jnp.float32), axis=1))
        query_counts = jnp.dot(pick.astype(jnp.float32), counts, precision=lax.Precision.HIGHEST)
        page_weights = jnp.repeat(query_counts, PAGE_TOKENS, axis=1)
        key_rows = jnp.concatenate([pooled_keys, key_value_group[:, :row_width].reshape(GROUP_TOKENS, KEY_VALUE_HEADS, HEAD_SIZE)], axis=0)
        value_rows = jnp.concatenate([pooled_values, key_value_group[:, row_width:].reshape(GROUP_TOKENS, KEY_VALUE_HEADS, HEAD_SIZE)], axis=0)

        def one_block(index):
            start_offset = (index * query_block).astype(jnp.int32)
            rows = start_offset + jnp.arange(query_block, dtype=jnp.int32)
            query_block_size = lax.dynamic_slice_in_dim(query_group, start_offset, query_block, 0).reshape(query_block, KEY_VALUE_HEADS, QUERY_HEADS // KEY_VALUE_HEADS, HEAD_SIZE)
            scores = jnp.einsum('tgrd,kgd->tgrk', query_block_size.astype(jnp.float32), key_rows.astype(jnp.float32)) * (1.0 / math.sqrt(HEAD_SIZE))
            first_blk = lax.dynamic_slice_in_dim(first, start_offset, query_block, 0)
            suffix_w = ((positions[None, :] <= rows[:, None]) & (positions[None, :] >= first_blk[:, None])).astype(jnp.float32)
            weights = jnp.concatenate([lax.dynamic_slice_in_dim(page_weights, start_offset, query_block, 0), suffix_w], axis=1)
            return weighted_softmax(scores, weights, value_rows).reshape(query_block, QUERY_HEADS * HEAD_SIZE)
        return lax.map(one_block, jnp.arange(GROUP_TOKENS // query_block, dtype=jnp.int32)).reshape(GROUP_TOKENS, QUERY_HEADS * HEAD_SIZE)
    attended = lax.map(group_attention, (queries.reshape(N_REQ, GROUP_TOKENS, QUERY_HEADS * HEAD_SIZE), suffix_kv.reshape(N_REQ, GROUP_TOKENS, 2 * row_width), lengths, page_table))
    attended = attended.reshape(SUFFIX_TOKENS, QUERY_HEADS * HEAD_SIZE).astype(jnp.bfloat16)
    projected = jnp.dot(attended, w_out, preferred_element_type=jnp.float32)
    resid = lax.optimization_barrier((hidden.astype(jnp.float32) + projected).astype(jnp.bfloat16))
    resid_f = resid.astype(jnp.float32)
    normed = (resid_f * lax.rsqrt(lax.optimization_barrier(jnp.mean(resid_f * resid_f, axis=1, keepdims=True)) + EPS)).astype(jnp.bfloat16)
    logits = jnp.dot(normed, w_router, preferred_element_type=jnp.float32)
    gates = jax.nn.softmax(jnp.take_along_axis(logits, routes, axis=1), axis=1)
    rows_cap = N_REQ * N_EXP * CAP
    flattened = routes.reshape(-1)
    padded_rows = jnp.concatenate([normed, jnp.zeros((1, D), jnp.bfloat16)], axis=0)
    padded_gates = jnp.concatenate([gates.reshape(-1), jnp.zeros((1,), jnp.float32)], axis=0)

    def one_expert(grand_total, expert):
        picked = jnp.nonzero(flattened == expert, size=rows_cap, fill_value=SUFFIX_TOKENS * TOP)[0].astype(jnp.int32)
        token = (picked // TOP).astype(jnp.int32)
        rows = padded_rows[token]
        summed_output = jnp.zeros((rows_cap, D), jnp.float32)
        for half in range(2):
            slot = 2 * expert + half
            gate_w = lax.dynamic_index_in_dim(w_gate, slot, 0, keepdims=False)
            up_w = lax.dynamic_index_in_dim(w_up, slot, 0, keepdims=False)
            down_w = lax.dynamic_index_in_dim(w_down, slot, 0, keepdims=False)
            gate_part = jnp.dot(rows, gate_w, preferred_element_type=jnp.float32)
            up_part = jnp.dot(rows, up_w, preferred_element_type=jnp.float32)
            inner = (jax.nn.silu(gate_part) * up_part).astype(jnp.bfloat16)
            part = lax.optimization_barrier(jnp.dot(inner, down_w, preferred_element_type=jnp.float32).astype(jnp.bfloat16))
            summed_output = summed_output + part.astype(jnp.float32)
        weighted = summed_output * padded_gates[picked][:, None]
        return (grand_total.at[token].add(weighted, mode='drop'), None)
    moe, _ = lax.scan(one_expert, jnp.zeros((SUFFIX_TOKENS, D), jnp.float32), jnp.arange(EXPERTS, dtype=jnp.int32))
    return (resid_f + moe).astype(jnp.bfloat16)
```

```python
import math

import jax
import jax.numpy as jnp
from jax import lax
from jax.sharding import PartitionSpec as P

D = 2560
QUERY_HEADS = 10
KEY_VALUE_HEADS = 2
HEAD_SIZE = 128
TOP = 6
PAGE_TOKENS = 128


NEGATIVE_MASK = -1e30
EPS = 1e-06


def fold_scores(carry, query_matrix, key_rows, value_rows, weights):
    scores = jnp.einsum(
        "tgrd,kgd->tgrk", query_matrix, key_rows, preferred_element_type=jnp.float32
    ) * (1.0 / math.sqrt(HEAD_SIZE))
    running_maximum, grand_total, summed_output = carry
    live = weights[:, None, None, :] > 0
    fresh = jnp.maximum(running_maximum, jnp.max(jnp.where(live, scores, NEGATIVE_MASK), axis=-1))
    expo = jnp.where(live, jnp.exp(scores - fresh[..., None]), 0.0) * weights[:, None, None, :]
    decay = jnp.exp(running_maximum - fresh)
    grand_total = decay * grand_total + jnp.sum(expo, axis=-1)
    summed_output = decay[..., None] * summed_output + jnp.einsum(
        "tgrk,kgd->tgrd", expo.astype(jnp.bfloat16), value_rows, preferred_element_type=jnp.float32
    )
    return (fresh, grand_total, summed_output)


def empty_carry(token_count, request_groups):
    return (
        jnp.full((token_count, KEY_VALUE_HEADS, request_groups), NEGATIVE_MASK, jnp.float32),
        jnp.zeros((token_count, KEY_VALUE_HEADS, request_groups), jnp.float32),
        jnp.zeros((token_count, KEY_VALUE_HEADS, request_groups, HEAD_SIZE), jnp.float32),
    )


def on_device(
    hidden,
    queries,
    suffix_kv,
    lengths,
    page_table,
    page_pool,
    w_out,
    w_router,
    routes,
    w_gate,
    w_up,
    w_down,
):
    token_index = hidden.shape[0]
    row_width = KEY_VALUE_HEADS * HEAD_SIZE
    request_groups = QUERY_HEADS // KEY_VALUE_HEADS
    request_count = lax.axis_size("req")
    pool_per_shard = page_pool.shape[0]
    pool_all = pool_per_shard * request_count
    query_matrix = queries.reshape(token_index, KEY_VALUE_HEADS, request_groups, HEAD_SIZE)
    positions = lax.axis_index("exp") * token_index + jnp.arange(token_index, dtype=jnp.int32)
    lens = lengths[0]
    ends = jnp.cumsum(lens)
    starts = ends - lens
    req_of = jnp.sum((positions[:, None] >= ends[None, :]).astype(jnp.int32), axis=1)
    pick = req_of[:, None] == jnp.arange(lens.shape[0], dtype=jnp.int32)[None, :]
    first = jnp.sum(jnp.where(pick, starts[None, :], 0), axis=1)
    counts = jnp.sum(
        (page_table[0][:, :, None] == jnp.arange(pool_all, dtype=jnp.int32)[None, None, :]).astype(
            jnp.float32
        ),
        axis=1,
    )
    query_counts = jnp.dot(pick.astype(jnp.float32), counts, precision=lax.Precision.HIGHEST)
    query_total_set, every_count = (
        lax.all_gather(queries, "req", axis=0, tiled=True),
        lax.all_gather(query_counts.astype(jnp.bfloat16), "req", axis=0, tiled=True),
    )
    query_total_count = query_total_set.shape[0]
    local = lax.dynamic_slice_in_dim(
        every_count, lax.axis_index("req") * pool_per_shard, pool_per_shard, 1
    ).astype(jnp.float32)
    weights = jnp.repeat(local, PAGE_TOKENS, axis=1)
    flattened = page_pool.reshape(pool_per_shard * PAGE_TOKENS, 2 * row_width)
    key_rows = flattened[:, :row_width].reshape(
        pool_per_shard * PAGE_TOKENS, KEY_VALUE_HEADS, HEAD_SIZE
    )
    value_rows = flattened[:, row_width:].reshape(
        pool_per_shard * PAGE_TOKENS, KEY_VALUE_HEADS, HEAD_SIZE
    )
    running_maximum, grand_total, summed_output = fold_scores(
        empty_carry(query_total_count, request_groups),
        query_total_set.reshape(query_total_count, KEY_VALUE_HEADS, request_groups, HEAD_SIZE),
        key_rows,
        value_rows,
        weights,
    )
    peaks, totals, sums = (
        lax.all_to_all(
            running_maximum.reshape(request_count, token_index, KEY_VALUE_HEADS, request_groups),
            "req",
            split_axis=0,
            concat_axis=0,
            tiled=True,
        ),
        lax.all_to_all(
            grand_total.reshape(request_count, token_index, KEY_VALUE_HEADS, request_groups),
            "req",
            split_axis=0,
            concat_axis=0,
            tiled=True,
        ),
        lax.all_to_all(
            summed_output.reshape(
                request_count, token_index, KEY_VALUE_HEADS, request_groups, HEAD_SIZE
            ),
            "req",
            split_axis=0,
            concat_axis=0,
            tiled=True,
        ),
    )
    highest = jnp.max(peaks, axis=0)
    factor = jnp.exp(peaks - highest[None])
    carry = (highest, jnp.sum(factor * totals, axis=0), jnp.sum(factor[..., None] * sums, axis=0))
    segment = lax.all_gather(suffix_kv, "exp", axis=0, tiled=True)
    token_count = segment.shape[0]
    keypos = jnp.arange(token_count, dtype=jnp.int32)
    weights = (
        (keypos[None, :] <= positions[:, None]) & (keypos[None, :] >= first[:, None])
    ).astype(jnp.float32)
    key_rows = segment[:, :row_width].reshape(token_count, KEY_VALUE_HEADS, HEAD_SIZE)
    value_rows = segment[:, row_width:].reshape(token_count, KEY_VALUE_HEADS, HEAD_SIZE)
    running_maximum, grand_total, summed_output = fold_scores(
        carry, query_matrix, key_rows, value_rows, weights
    )
    attended = (
        (summed_output / grand_total[..., None])
        .reshape(token_index, QUERY_HEADS * HEAD_SIZE)
        .astype(jnp.bfloat16)
    )
    projected = jnp.dot(attended, w_out, preferred_element_type=jnp.float32)
    resid = lax.optimization_barrier((hidden.astype(jnp.float32) + projected).astype(jnp.bfloat16))
    resid_f = resid.astype(jnp.float32)
    normed = (resid_f * lax.rsqrt(jnp.mean(resid_f * resid_f, axis=1, keepdims=True) + EPS)).astype(
        jnp.bfloat16
    )
    n_experts = w_router.shape[1]
    logits = jnp.dot(normed, w_router, preferred_element_type=jnp.float32)
    expert_ids = jnp.arange(n_experts, dtype=jnp.int32)
    chosen = jnp.sum(
        jnp.where(routes[:, :, None] == expert_ids[None, None, :], logits[:, None, :], 0.0), axis=2
    )
    gates = jax.nn.softmax(chosen, axis=1)
    capacity = 16
    member = routes[:, :, None] == expert_ids[None, None, :]
    picks = jnp.any(member, axis=1).astype(jnp.float32)
    gate_of = jnp.sum(jnp.where(member, gates[:, :, None], 0.0), axis=1)
    earlier = (
        jnp.arange(token_index, dtype=jnp.int32)[:, None]
        > jnp.arange(token_index, dtype=jnp.int32)[None, :]
    ).astype(jnp.float32)
    rank = jnp.dot(earlier, picks, precision=lax.Precision.HIGHEST).astype(jnp.int32)
    place = jnp.arange(capacity, dtype=jnp.int32)
    select = (picks[None, :, :] > 0) & (rank[None, :, :] == place[:, None, None])
    select = jnp.transpose(select, (2, 0, 1))
    select2 = jnp.broadcast_to(
        select[:, None], (n_experts, 2, capacity, token_index)
    ).reshape(2 * n_experts * capacity, token_index)
    outgoing = jnp.dot(
        select2.astype(jnp.bfloat16), normed, preferred_element_type=jnp.float32
    ).astype(jnp.bfloat16)
    outgoing = outgoing.reshape(2 * n_experts, capacity, D)
    rows = lax.all_to_all(outgoing, ("req", "exp"), split_axis=0, concat_axis=0, tiled=True)
    array_shape = rows.shape
    flat_rows = rows.reshape(-1, D)
    gate_part = jnp.dot(flat_rows, w_gate[0], preferred_element_type=jnp.float32)
    up_part = jnp.dot(flat_rows, w_up[0], preferred_element_type=jnp.float32)
    inner = (jax.nn.silu(gate_part) * up_part).astype(jnp.bfloat16)
    returned = lax.all_to_all(
        jnp.dot(inner, w_down[0], preferred_element_type=jnp.float32)
        .astype(jnp.bfloat16)
        .reshape(array_shape),
        ("req", "exp"),
        split_axis=0,
        concat_axis=0,
        tiled=True,
    ).reshape(2 * n_experts * capacity, D)
    weight = jnp.where(
        jnp.transpose(select, (2, 0, 1))[:, :, None, :],
        gate_of[:, :, None, None],
        0.0,
    )
    weight = jnp.broadcast_to(
        weight, (token_index, n_experts, 2, capacity)
    ).reshape(token_index, 2 * n_experts * capacity)
    high = weight.astype(jnp.bfloat16)
    low = (weight - high.astype(jnp.float32)).astype(jnp.bfloat16)
    moe = jnp.dot(high, returned, preferred_element_type=jnp.float32) + jnp.dot(
        low, returned, preferred_element_type=jnp.float32
    )
    return (resid_f + moe).astype(jnp.bfloat16)


def solution(mesh):
    placed = (
        P(("req", "exp"), None),
        P(("req", "exp"), None),
        P(("req", "exp"), None),
        P("req", None),
        P("req", None, None),
        P("req", None, None),
        P(),
        P(),
        P(("req", "exp"), None),
        P(("req", "exp"), None, None),
        P(("req", "exp"), None, None),
        P(("req", "exp"), None, None),
    )
    return jax.shard_map(
        on_device, mesh=mesh, in_specs=placed, out_specs=P(("req", "exp"), None), check_vma=False
    )
```

```python
import functools
import math

import jax
import jax.numpy as jnp
from jax import lax
from jax.experimental import pallas as pl
from jax.experimental.pallas import tpu as pltpu
from jax.sharding import PartitionSpec as P

D = 2560
QUERY_HEADS = 10
KEY_VALUE_HEADS = 2
HEAD_SIZE = 128
TOP = 6
PAGE_TOKENS = 128


NEGATIVE_MASK = -1e30
EPS = 1e-06


KEY_BLOCK = 512


def attn_kernel(q_ref, w_ref, pool_ref, suf_ref, o_ref, qs, m_ref, l_ref, acc_ref, *, n_pool, n_blocks, groups, reps, hs):
    j = pl.program_id(0)
    t = q_ref.shape[0]

    @pl.when(j == 0)
    def _():
        for g in range(groups):
            qs[g] = jnp.concatenate(
                [q_ref[:, (g * reps + h) * hs:(g * reps + h + 1) * hs] for h in range(reps)], axis=0)
        m_ref[...] = jnp.full(m_ref.shape, NEGATIVE_MASK, jnp.float32)
        l_ref[...] = jnp.zeros(l_ref.shape, jnp.float32)
        acc_ref[...] = jnp.zeros(acc_ref.shape, jnp.float32)

    def step(kv_ref):
        w = w_ref[...].astype(jnp.float32)
        live = (w > 0)[None]
        for g in range(groups):
            k = kv_ref[:, g * hs:(g + 1) * hs]
            v = kv_ref[:, (groups + g) * hs:(groups + g + 1) * hs]
            s = lax.dot_general(qs[g], k, (((1,), (1,)), ((), ())),
                                preferred_element_type=jnp.float32) * (1.0 / math.sqrt(hs))
            s = s.reshape(reps, t, KEY_BLOCK)
            m_old = m_ref[g].reshape(reps, t, 1)
            m_new = jnp.maximum(m_old, jnp.max(jnp.where(live, s, NEGATIVE_MASK), axis=-1, keepdims=True))
            p = jnp.where(live, jnp.exp(s - m_new), 0.0) * w[None]
            alpha = jnp.exp(m_old - m_new)
            l_ref[g] = (alpha * l_ref[g].reshape(reps, t, 1) + jnp.sum(p, axis=-1, keepdims=True)).reshape(reps * t, 1)
            pv = jnp.dot(p.reshape(reps * t, KEY_BLOCK).astype(jnp.bfloat16), v, preferred_element_type=jnp.float32)
            acc_ref[g] = alpha.reshape(reps * t, 1) * acc_ref[g] + pv
            m_ref[g] = m_new.reshape(reps * t, 1)

    @pl.when(j < n_pool)
    def _():
        step(pool_ref)

    @pl.when(j >= n_pool)
    def _():
        step(suf_ref)

    @pl.when(j == n_blocks - 1)
    def _():
        for g in range(groups):
            for h in range(reps):
                rows = slice(h * t, (h + 1) * t)
                o_ref[:, (g * reps + h) * hs:(g * reps + h + 1) * hs] = (
                    acc_ref[g, rows, :] / l_ref[g, rows, :]).astype(o_ref.dtype)


def flash(queries, weights, pool_rows, suffix_rows, groups=2, hs=128):
    t, width = queries.shape
    reps = width // hs // groups
    n_pool = pool_rows.shape[0] // KEY_BLOCK
    n_suf = suffix_rows.shape[0] // KEY_BLOCK
    n_blocks = n_pool + n_suf
    kern = functools.partial(attn_kernel, n_pool=n_pool, n_blocks=n_blocks, groups=groups, reps=reps, hs=hs)
    return pl.pallas_call(
        kern,
        grid=(n_blocks,),
        in_specs=[
            pl.BlockSpec((t, width), lambda j: (0, 0)),
            pl.BlockSpec((t, KEY_BLOCK), lambda j: (0, j)),
            pl.BlockSpec((KEY_BLOCK, pool_rows.shape[1]), lambda j: (jnp.minimum(j, n_pool - 1), 0)),
            pl.BlockSpec((KEY_BLOCK, suffix_rows.shape[1]), lambda j: (jnp.maximum(j - n_pool, 0), 0)),
        ],
        out_specs=pl.BlockSpec((t, width), lambda j: (0, 0)),
        out_shape=jax.ShapeDtypeStruct((t, width), jnp.bfloat16),
        scratch_shapes=[
            pltpu.VMEM((groups, reps * t, hs), jnp.bfloat16),
            pltpu.VMEM((groups, reps * t, 1), jnp.float32),
            pltpu.VMEM((groups, reps * t, 1), jnp.float32),
            pltpu.VMEM((groups, reps * t, hs), jnp.float32),
        ],
    )(queries, weights, pool_rows, suffix_rows)


def on_device(
    hidden,
    queries,
    suffix_kv,
    lengths,
    page_table,
    page_pool,
    w_out,
    w_router,
    routes,
    w_gate,
    w_up,
    w_down,
):
    token_index = hidden.shape[0]
    row_width = KEY_VALUE_HEADS * HEAD_SIZE
    request_groups = QUERY_HEADS // KEY_VALUE_HEADS
    request_count = lax.axis_size("req")
    pool_per_shard = page_pool.shape[0]
    pool_all = pool_per_shard * request_count
    positions = lax.axis_index("exp") * token_index + jnp.arange(token_index, dtype=jnp.int32)
    lens = lengths[0]
    ends = jnp.cumsum(lens)
    starts = ends - lens
    req_of = jnp.sum((positions[:, None] >= ends[None, :]).astype(jnp.int32), axis=1)
    pick = req_of[:, None] == jnp.arange(lens.shape[0], dtype=jnp.int32)[None, :]
    first = jnp.sum(jnp.where(pick, starts[None, :], 0), axis=1)
    pool_rows = lax.all_gather(page_pool, "req", axis=0, tiled=True).reshape(
        pool_all * PAGE_TOKENS, 2 * row_width
    )
    segment = lax.all_gather(suffix_kv, "exp", axis=0, tiled=True)
    counts = jnp.sum(
        (page_table[0][:, :, None] == jnp.arange(pool_all, dtype=jnp.int32)[None, None, :]).astype(
            jnp.float32
        ),
        axis=1,
    )
    query_counts = jnp.dot(pick.astype(jnp.float32), counts, precision=lax.Precision.HIGHEST)
    keypos = jnp.arange(segment.shape[0], dtype=jnp.int32)
    suffix_weights = (keypos[None, :] <= positions[:, None]) & (keypos[None, :] >= first[:, None])
    weights = jnp.concatenate(
        [
            jnp.repeat(query_counts, PAGE_TOKENS, axis=1).astype(jnp.bfloat16),
            suffix_weights.astype(jnp.bfloat16),
        ],
        axis=1,
    )
    attended = flash(queries, weights, pool_rows, segment, groups=KEY_VALUE_HEADS, hs=HEAD_SIZE)
    projected = jnp.dot(attended, w_out, preferred_element_type=jnp.float32)
    resid = lax.optimization_barrier((hidden.astype(jnp.float32) + projected).astype(jnp.bfloat16))
    resid_f = resid.astype(jnp.float32)
    normed = (resid_f * lax.rsqrt(jnp.mean(resid_f * resid_f, axis=1, keepdims=True) + EPS)).astype(
        jnp.bfloat16
    )
    n_experts = w_router.shape[1]
    logits = jnp.dot(normed, w_router, preferred_element_type=jnp.float32)
    expert_ids = jnp.arange(n_experts, dtype=jnp.int32)
    chosen = jnp.sum(
        jnp.where(routes[:, :, None] == expert_ids[None, None, :], logits[:, None, :], 0.0), axis=2
    )
    gates = jax.nn.softmax(chosen, axis=1)
    capacity = 16
    member = routes[:, :, None] == expert_ids[None, None, :]
    picks = jnp.any(member, axis=1).astype(jnp.float32)
    gate_of = jnp.sum(jnp.where(member, gates[:, :, None], 0.0), axis=1)
    earlier = (
        jnp.arange(token_index, dtype=jnp.int32)[:, None]
        > jnp.arange(token_index, dtype=jnp.int32)[None, :]
    ).astype(jnp.float32)
    rank = jnp.dot(earlier, picks, precision=lax.Precision.HIGHEST).astype(jnp.int32)
    place = jnp.arange(capacity, dtype=jnp.int32)
    select = (picks[None, :, :] > 0) & (rank[None, :, :] == place[:, None, None])
    select = jnp.transpose(select, (2, 0, 1))
    select2 = jnp.broadcast_to(
        select[:, None], (n_experts, 2, capacity, token_index)
    ).reshape(2 * n_experts * capacity, token_index)
    outgoing = jnp.dot(
        select2.astype(jnp.bfloat16), normed, preferred_element_type=jnp.float32
    ).astype(jnp.bfloat16)
    outgoing = outgoing.reshape(2 * n_experts, capacity, D)
    rows = lax.all_to_all(outgoing, ("req", "exp"), split_axis=0, concat_axis=0, tiled=True)
    array_shape = rows.shape
    flat_rows = rows.reshape(-1, D)
    gate_part = jnp.dot(flat_rows, w_gate[0], preferred_element_type=jnp.float32)
    up_part = jnp.dot(flat_rows, w_up[0], preferred_element_type=jnp.float32)
    inner = (jax.nn.silu(gate_part) * up_part).astype(jnp.bfloat16)
    returned = lax.all_to_all(
        jnp.dot(inner, w_down[0], preferred_element_type=jnp.float32)
        .astype(jnp.bfloat16)
        .reshape(array_shape),
        ("req", "exp"),
        split_axis=0,
        concat_axis=0,
        tiled=True,
    ).reshape(2 * n_experts * capacity, D)
    weight = jnp.where(
        jnp.transpose(select, (2, 0, 1))[:, :, None, :],
        gate_of[:, :, None, None],
        0.0,
    )
    weight = jnp.broadcast_to(
        weight, (token_index, n_experts, 2, capacity)
    ).reshape(token_index, 2 * n_experts * capacity)
    high = weight.astype(jnp.bfloat16)
    low = (weight - high.astype(jnp.float32)).astype(jnp.bfloat16)
    moe = jnp.dot(high, returned, preferred_element_type=jnp.float32) + jnp.dot(
        low, returned, preferred_element_type=jnp.float32
    )
    return (resid_f + moe).astype(jnp.bfloat16)


def solution(mesh):
    placed = (
        P(("req", "exp"), None),
        P(("req", "exp"), None),
        P(("req", "exp"), None),
        P("req", None),
        P("req", None, None),
        P("req", None, None),
        P(),
        P(),
        P(("req", "exp"), None),
        P(("req", "exp"), None, None),
        P(("req", "exp"), None, None),
        P(("req", "exp"), None, None),
    )
    return jax.shard_map(
        on_device, mesh=mesh, in_specs=placed, out_specs=P(("req", "exp"), None), check_vma=False
    )
```

```python
import functools
import math

import jax
import jax.numpy as jnp
from jax import lax
from jax.experimental import pallas as pl
from jax.experimental.pallas import tpu as pltpu
from jax.sharding import PartitionSpec as P

D = 2560
QUERY_HEADS = 10
KEY_VALUE_HEADS = 2
HEAD_SIZE = 128
TOP = 6
PAGE_TOKENS = 128


NEGATIVE_MASK = -1e30
EPS = 1e-06


KEY_BLOCK = 512


def attn_kernel(flags_ref, q_ref, w_ref, kv_ref, m_in, l_in, acc_in, *refs, first_call, last_call, groups, reps, hs):
    if last_call:
        o_ref, qs, m_ref, l_ref, acc_ref = refs
    else:
        m_out, l_out, acc_out, qs, m_ref, l_ref, acc_ref = refs
    j = pl.program_id(0)
    t = q_ref.shape[0]
    key_block = kv_ref.shape[0]

    @pl.when(j == 0)
    def _():
        for g in range(groups):
            qs[g] = jnp.concatenate(
                [q_ref[:, (g * reps + h) * hs:(g * reps + h + 1) * hs] for h in range(reps)], axis=0)
        if first_call:
            m_ref[...] = jnp.full(m_ref.shape, NEGATIVE_MASK, jnp.float32)
            l_ref[...] = jnp.zeros(l_ref.shape, jnp.float32)
            acc_ref[...] = jnp.zeros(acc_ref.shape, jnp.float32)
        else:
            m_ref[...] = m_in[...]
            l_ref[...] = l_in[...]
            acc_ref[...] = acc_in[...]

    @pl.when(flags_ref[j] > 0)
    def _():
        w = w_ref[...].astype(jnp.float32)
        live = (w > 0)[None]
        for g in range(groups):
            k = kv_ref[:, g * hs:(g + 1) * hs]
            v = kv_ref[:, (groups + g) * hs:(groups + g + 1) * hs]
            s = lax.dot_general(qs[g], k, (((1,), (1,)), ((), ())),
                                preferred_element_type=jnp.float32) * (1.0 / math.sqrt(hs))
            s = jnp.where(live, s.reshape(reps, t, key_block), NEGATIVE_MASK)
            m_old = m_ref[g].reshape(reps, t, 1)
            m_new = jnp.maximum(m_old, jnp.max(s, axis=-1, keepdims=True))
            p = jnp.exp(s - m_new) * w[None]
            alpha = jnp.exp(m_old - m_new)
            l_ref[g] = (alpha * l_ref[g].reshape(reps, t, 1) + jnp.sum(p, axis=-1, keepdims=True)).reshape(reps * t, 1)
            pv = jnp.dot(p.reshape(reps * t, key_block).astype(jnp.bfloat16), v, preferred_element_type=jnp.float32)
            acc_ref[g] = alpha.reshape(reps * t, 1) * acc_ref[g] + pv
            m_ref[g] = m_new.reshape(reps * t, 1)

    @pl.when(j == pl.num_programs(0) - 1)
    def _():
        if last_call:
            for g in range(groups):
                for h in range(reps):
                    rows = slice(h * t, (h + 1) * t)
                    o_ref[:, (g * reps + h) * hs:(g * reps + h + 1) * hs] = (
                        acc_ref[g, rows, :] / l_ref[g, rows, :]).astype(o_ref.dtype)
        else:
            m_out[...] = m_ref[...]
            l_out[...] = l_ref[...]
            acc_out[...] = acc_ref[...]


def flash(queries, weights, kv_rows, carry, first_call, last_call, groups, hs):
    t, width = queries.shape
    reps = width // hs // groups
    n_blocks = kv_rows.shape[0] // KEY_BLOCK
    flags = (jnp.max(weights.reshape(t, n_blocks, KEY_BLOCK), axis=(0, 2)) > 0).astype(jnp.int32)
    kern = functools.partial(attn_kernel, first_call=first_call, last_call=last_call,
                             groups=groups, reps=reps, hs=hs)
    state = [
        jax.ShapeDtypeStruct((groups, reps * t, 1), jnp.float32),
        jax.ShapeDtypeStruct((groups, reps * t, 1), jnp.float32),
        jax.ShapeDtypeStruct((groups, reps * t, hs), jnp.float32),
    ]
    state_specs = [
        pl.BlockSpec((groups, reps * t, 1), lambda j, f: (0, 0, 0)),
        pl.BlockSpec((groups, reps * t, 1), lambda j, f: (0, 0, 0)),
        pl.BlockSpec((groups, reps * t, hs), lambda j, f: (0, 0, 0)),
    ]
    if last_call:
        out_shape = jax.ShapeDtypeStruct((t, width), jnp.bfloat16)
        out_specs = pl.BlockSpec((t, width), lambda j, f: (0, 0))
    else:
        out_shape, out_specs = state, state_specs
    grid_spec = pltpu.PrefetchScalarGridSpec(
        num_scalar_prefetch=1,
        grid=(n_blocks,),
        in_specs=[
            pl.BlockSpec((t, width), lambda j, f: (0, 0)),
            pl.BlockSpec((t, KEY_BLOCK), lambda j, f: (0, j)),
            pl.BlockSpec((KEY_BLOCK, kv_rows.shape[1]), lambda j, f: (j, 0)),
        ] + state_specs,
        out_specs=out_specs,
        scratch_shapes=[
            pltpu.VMEM((groups, reps * t, hs), jnp.bfloat16),
            pltpu.VMEM((groups, reps * t, 1), jnp.float32),
            pltpu.VMEM((groups, reps * t, 1), jnp.float32),
            pltpu.VMEM((groups, reps * t, hs), jnp.float32),
        ],
    )
    if carry is None:
        carry = tuple(jnp.zeros(s.shape, s.dtype) for s in state)
    return pl.pallas_call(kern, grid_spec=grid_spec, out_shape=out_shape)(
        flags, queries, weights, kv_rows, *carry)


def on_device(
    hidden,
    queries,
    suffix_kv,
    lengths,
    page_table,
    page_pool,
    w_out,
    w_router,
    routes,
    w_gate,
    w_up,
    w_down,
):
    token_index = hidden.shape[0]
    row_width = KEY_VALUE_HEADS * HEAD_SIZE
    request_groups = QUERY_HEADS // KEY_VALUE_HEADS
    request_count = lax.axis_size("req")
    pool_per_shard = page_pool.shape[0]
    pool_all = pool_per_shard * request_count
    positions = lax.axis_index("exp") * token_index + jnp.arange(token_index, dtype=jnp.int32)
    lens = lengths[0]
    ends = jnp.cumsum(lens)
    starts = ends - lens
    req_of = jnp.sum((positions[:, None] >= ends[None, :]).astype(jnp.int32), axis=1)
    pick = req_of[:, None] == jnp.arange(lens.shape[0], dtype=jnp.int32)[None, :]
    first = jnp.sum(jnp.where(pick, starts[None, :], 0), axis=1)
    pool_rows = lax.all_gather(page_pool, "req", axis=0, tiled=True).reshape(
        pool_all * PAGE_TOKENS, 2 * row_width
    )
    pool_rows, suffix_after = lax.optimization_barrier((pool_rows, suffix_kv))
    segment = lax.all_gather(suffix_after, "exp", axis=0, tiled=True)
    counts = jnp.sum(
        (page_table[0][:, :, None] == jnp.arange(pool_all, dtype=jnp.int32)[None, None, :]).astype(
            jnp.float32
        ),
        axis=1,
    )
    query_counts = jnp.dot(pick.astype(jnp.float32), counts, precision=lax.Precision.HIGHEST)
    keypos = jnp.arange(segment.shape[0], dtype=jnp.int32)
    suffix_weights = (keypos[None, :] <= positions[:, None]) & (keypos[None, :] >= first[:, None])
    pool_weights = jnp.repeat(query_counts, PAGE_TOKENS, axis=1).astype(jnp.bfloat16)
    carry = flash(queries, pool_weights, pool_rows, None, True, False, KEY_VALUE_HEADS, HEAD_SIZE)
    attended = flash(
        queries,
        suffix_weights.astype(jnp.bfloat16),
        segment,
        carry,
        False,
        True,
        KEY_VALUE_HEADS,
        HEAD_SIZE,
    )
    projected = jnp.dot(attended, w_out, preferred_element_type=jnp.float32)
    resid = lax.optimization_barrier((hidden.astype(jnp.float32) + projected).astype(jnp.bfloat16))
    resid_f = resid.astype(jnp.float32)
    normed = (resid_f * lax.rsqrt(jnp.mean(resid_f * resid_f, axis=1, keepdims=True) + EPS)).astype(
        jnp.bfloat16
    )
    n_experts = w_router.shape[1]
    logits = jnp.dot(normed, w_router, preferred_element_type=jnp.float32)
    expert_ids = jnp.arange(n_experts, dtype=jnp.int32)
    chosen = jnp.sum(
        jnp.where(routes[:, :, None] == expert_ids[None, None, :], logits[:, None, :], 0.0), axis=2
    )
    gates = jax.nn.softmax(chosen, axis=1)
    capacity = 16
    member = routes[:, :, None] == expert_ids[None, None, :]
    picks = jnp.any(member, axis=1).astype(jnp.float32)
    gate_of = jnp.sum(jnp.where(member, gates[:, :, None], 0.0), axis=1)
    earlier = (
        jnp.arange(token_index, dtype=jnp.int32)[:, None]
        > jnp.arange(token_index, dtype=jnp.int32)[None, :]
    ).astype(jnp.float32)
    rank = jnp.dot(earlier, picks, precision=lax.Precision.HIGHEST).astype(jnp.int32)
    place = jnp.arange(capacity, dtype=jnp.int32)
    select = (picks[None, :, :] > 0) & (rank[None, :, :] == place[:, None, None])
    select = jnp.transpose(select, (2, 0, 1))
    select2 = jnp.broadcast_to(
        select[:, None], (n_experts, 2, capacity, token_index)
    ).reshape(2 * n_experts * capacity, token_index)
    outgoing = jnp.dot(
        select2.astype(jnp.bfloat16), normed, preferred_element_type=jnp.float32
    ).astype(jnp.bfloat16)
    outgoing = outgoing.reshape(2 * n_experts, capacity, D)
    rows = lax.all_to_all(outgoing, ("req", "exp"), split_axis=0, concat_axis=0, tiled=True)
    array_shape = rows.shape
    flat_rows = rows.reshape(-1, D)
    gate_part = jnp.dot(flat_rows, w_gate[0], preferred_element_type=jnp.float32)
    up_part = jnp.dot(flat_rows, w_up[0], preferred_element_type=jnp.float32)
    inner = (jax.nn.silu(gate_part) * up_part).astype(jnp.bfloat16)
    returned = lax.all_to_all(
        jnp.dot(inner, w_down[0], preferred_element_type=jnp.float32)
        .astype(jnp.bfloat16)
        .reshape(array_shape),
        ("req", "exp"),
        split_axis=0,
        concat_axis=0,
        tiled=True,
    ).reshape(2 * n_experts * capacity, D)
    weight = jnp.where(
        jnp.transpose(select, (2, 0, 1))[:, :, None, :],
        gate_of[:, :, None, None],
        0.0,
    )
    weight = jnp.broadcast_to(
        weight, (token_index, n_experts, 2, capacity)
    ).reshape(token_index, 2 * n_experts * capacity)
    high = weight.astype(jnp.bfloat16)
    low = (weight - high.astype(jnp.float32)).astype(jnp.bfloat16)
    moe = jnp.dot(high, returned, preferred_element_type=jnp.float32) + jnp.dot(
        low, returned, preferred_element_type=jnp.float32
    )
    return (resid_f + moe).astype(jnp.bfloat16)


def solution(mesh):
    placed = (
        P(("req", "exp"), None),
        P(("req", "exp"), None),
        P(("req", "exp"), None),
        P("req", None),
        P("req", None, None),
        P("req", None, None),
        P(),
        P(),
        P(("req", "exp"), None),
        P(("req", "exp"), None, None),
        P(("req", "exp"), None, None),
        P(("req", "exp"), None, None),
    )
    return jax.shard_map(
        on_device, mesh=mesh, in_specs=placed, out_specs=P(("req", "exp"), None), check_vma=False
    )
```

```python
import functools
import math

import jax
import jax.numpy as jnp
from jax import lax
from jax.experimental import pallas as pl
from jax.experimental.pallas import tpu as pltpu
from jax.sharding import PartitionSpec as P

D = 2560
QUERY_HEADS = 10
KEY_VALUE_HEADS = 2
HEAD_SIZE = 128
TOP = 6
PAGE_TOKENS = 128


NEGATIVE_MASK = -1e30
EPS = 1e-06


KEY_BLOCK = 512


def attn_kernel(flags_ref, q_ref, w_ref, kv_ref, m_in, l_in, acc_in, *refs, first_call, last_call, groups, reps, hs):
    if last_call:
        o_ref, qs, m_ref, l_ref, acc_ref = refs
    else:
        m_out, l_out, acc_out, qs, m_ref, l_ref, acc_ref = refs
    j = pl.program_id(0)
    t = q_ref.shape[0]
    key_block = kv_ref.shape[0]

    @pl.when(j == 0)
    def _():
        for g in range(groups):
            qs[g] = jnp.concatenate(
                [q_ref[:, (g * reps + h) * hs:(g * reps + h + 1) * hs] for h in range(reps)], axis=0)
        if first_call:
            m_ref[...] = jnp.full(m_ref.shape, NEGATIVE_MASK, jnp.float32)
            l_ref[...] = jnp.zeros(l_ref.shape, jnp.float32)
            acc_ref[...] = jnp.zeros(acc_ref.shape, jnp.float32)
        else:
            m_ref[...] = m_in[...]
            l_ref[...] = l_in[...]
            acc_ref[...] = acc_in[...]

    @pl.when(flags_ref[j] > 0)
    def _():
        w = w_ref[...].astype(jnp.float32)
        live = (w > 0)[None]
        for g in range(groups):
            k = kv_ref[:, g * hs:(g + 1) * hs]
            v = kv_ref[:, (groups + g) * hs:(groups + g + 1) * hs]
            s = lax.dot_general(qs[g], k, (((1,), (1,)), ((), ())),
                                preferred_element_type=jnp.float32) * (1.0 / math.sqrt(hs))
            s = jnp.where(live, s.reshape(reps, t, key_block), NEGATIVE_MASK)
            m_old = m_ref[g].reshape(reps, t, 1)
            m_new = jnp.maximum(m_old, jnp.max(s, axis=-1, keepdims=True))
            p = jnp.exp(s - m_new) * w[None]
            alpha = jnp.exp(m_old - m_new)
            l_ref[g] = (alpha * l_ref[g].reshape(reps, t, 1) + jnp.sum(p, axis=-1, keepdims=True)).reshape(reps * t, 1)
            pv = jnp.dot(p.reshape(reps * t, key_block).astype(jnp.bfloat16), v, preferred_element_type=jnp.float32)
            acc_ref[g] = alpha.reshape(reps * t, 1) * acc_ref[g] + pv
            m_ref[g] = m_new.reshape(reps * t, 1)

    @pl.when(j == pl.num_programs(0) - 1)
    def _():
        if last_call:
            for g in range(groups):
                for h in range(reps):
                    rows = slice(h * t, (h + 1) * t)
                    o_ref[:, (g * reps + h) * hs:(g * reps + h + 1) * hs] = (
                        acc_ref[g, rows, :] / l_ref[g, rows, :]).astype(o_ref.dtype)
        else:
            m_out[...] = m_ref[...]
            l_out[...] = l_ref[...]
            acc_out[...] = acc_ref[...]


def flash(queries, weights, kv_rows, carry, first_call, last_call, groups, hs):
    t, width = queries.shape
    reps = width // hs // groups
    n_blocks = kv_rows.shape[0] // KEY_BLOCK
    flags = (jnp.max(weights.reshape(t, n_blocks, KEY_BLOCK), axis=(0, 2)) > 0).astype(jnp.int32)
    kern = functools.partial(attn_kernel, first_call=first_call, last_call=last_call,
                             groups=groups, reps=reps, hs=hs)
    state = [
        jax.ShapeDtypeStruct((groups, reps * t, 1), jnp.float32),
        jax.ShapeDtypeStruct((groups, reps * t, 1), jnp.float32),
        jax.ShapeDtypeStruct((groups, reps * t, hs), jnp.float32),
    ]
    state_specs = [
        pl.BlockSpec((groups, reps * t, 1), lambda j, f: (0, 0, 0)),
        pl.BlockSpec((groups, reps * t, 1), lambda j, f: (0, 0, 0)),
        pl.BlockSpec((groups, reps * t, hs), lambda j, f: (0, 0, 0)),
    ]
    if last_call:
        out_shape = jax.ShapeDtypeStruct((t, width), jnp.bfloat16)
        out_specs = pl.BlockSpec((t, width), lambda j, f: (0, 0))
    else:
        out_shape, out_specs = state, state_specs
    grid_spec = pltpu.PrefetchScalarGridSpec(
        num_scalar_prefetch=1,
        grid=(n_blocks,),
        in_specs=[
            pl.BlockSpec((t, width), lambda j, f: (0, 0)),
            pl.BlockSpec((t, KEY_BLOCK), lambda j, f: (0, j)),
            pl.BlockSpec((KEY_BLOCK, kv_rows.shape[1]), lambda j, f: (j, 0)),
        ] + state_specs,
        out_specs=out_specs,
        scratch_shapes=[
            pltpu.VMEM((groups, reps * t, hs), jnp.bfloat16),
            pltpu.VMEM((groups, reps * t, 1), jnp.float32),
            pltpu.VMEM((groups, reps * t, 1), jnp.float32),
            pltpu.VMEM((groups, reps * t, hs), jnp.float32),
        ],
    )
    if carry is None:
        carry = tuple(jnp.zeros(s.shape, s.dtype) for s in state)
    return pl.pallas_call(kern, grid_spec=grid_spec, out_shape=out_shape)(
        flags, queries, weights, kv_rows, *carry)


def on_device(
    hidden,
    queries,
    suffix_kv,
    lengths,
    page_table,
    page_pool,
    w_out,
    w_router,
    routes,
    w_gate,
    w_up,
    w_down,
):
    token_index = hidden.shape[0]
    row_width = KEY_VALUE_HEADS * HEAD_SIZE
    request_groups = QUERY_HEADS // KEY_VALUE_HEADS
    request_count = lax.axis_size("req")
    pool_per_shard = page_pool.shape[0]
    pool_all = pool_per_shard * request_count
    positions = lax.axis_index("exp") * token_index + jnp.arange(token_index, dtype=jnp.int32)
    lens = lengths[0]
    ends = jnp.cumsum(lens)
    starts = ends - lens
    req_of = jnp.sum((positions[:, None] >= ends[None, :]).astype(jnp.int32), axis=1)
    pick = req_of[:, None] == jnp.arange(lens.shape[0], dtype=jnp.int32)[None, :]
    first = jnp.sum(jnp.where(pick, starts[None, :], 0), axis=1)
    pool_rows = lax.all_gather(page_pool, "req", axis=0, tiled=True).reshape(
        pool_all * PAGE_TOKENS, 2 * row_width
    )
    pool_rows, suffix_after = lax.optimization_barrier((pool_rows, suffix_kv))
    segment = lax.all_gather(suffix_after, "exp", axis=0, tiled=True)
    counts = jnp.sum(
        (page_table[0][:, :, None] == jnp.arange(pool_all, dtype=jnp.int32)[None, None, :]).astype(
            jnp.float32
        ),
        axis=1,
    )
    query_counts = jnp.dot(pick.astype(jnp.float32), counts, precision=lax.Precision.HIGHEST)
    keypos = jnp.arange(segment.shape[0], dtype=jnp.int32)
    suffix_weights = (keypos[None, :] <= positions[:, None]) & (keypos[None, :] >= first[:, None])
    pool_weights = jnp.repeat(query_counts, PAGE_TOKENS, axis=1).astype(jnp.bfloat16)
    carry = flash(queries, pool_weights, pool_rows, None, True, False, KEY_VALUE_HEADS, HEAD_SIZE)
    attended = flash(
        queries,
        suffix_weights.astype(jnp.bfloat16),
        segment,
        carry,
        False,
        True,
        KEY_VALUE_HEADS,
        HEAD_SIZE,
    )
    projected = jnp.dot(attended, w_out, preferred_element_type=jnp.float32)
    resid = lax.optimization_barrier((hidden.astype(jnp.float32) + projected).astype(jnp.bfloat16))
    resid_f = resid.astype(jnp.float32)
    normed = (resid_f * lax.rsqrt(jnp.mean(resid_f * resid_f, axis=1, keepdims=True) + EPS)).astype(
        jnp.bfloat16
    )
    n_experts = w_router.shape[1]
    logits = jnp.dot(normed, w_router, preferred_element_type=jnp.float32)
    expert_ids = jnp.arange(n_experts, dtype=jnp.int32)
    chosen = jnp.sum(
        jnp.where(routes[:, :, None] == expert_ids[None, None, :], logits[:, None, :], 0.0), axis=2
    )
    gates = jax.nn.softmax(chosen, axis=1)
    capacity = 16
    member = routes[:, :, None] == expert_ids[None, None, :]
    picks = jnp.any(member, axis=1).astype(jnp.float32)
    gate_of = jnp.sum(jnp.where(member, gates[:, :, None], 0.0), axis=1)
    earlier = (
        jnp.arange(token_index, dtype=jnp.int32)[:, None]
        > jnp.arange(token_index, dtype=jnp.int32)[None, :]
    ).astype(jnp.float32)
    rank = jnp.dot(earlier, picks, precision=lax.Precision.HIGHEST).astype(jnp.int32)
    place = jnp.arange(capacity, dtype=jnp.int32)
    select = (picks[None, :, :] > 0) & (rank[None, :, :] == place[:, None, None])
    select = jnp.transpose(select, (2, 0, 1))
    select2 = jnp.broadcast_to(
        select[:, None], (n_experts, 2, capacity, token_index)
    ).reshape(2 * n_experts * capacity, token_index)
    weight = jnp.where(
        jnp.transpose(select, (2, 0, 1))[:, :, None, :],
        gate_of[:, :, None, None],
        0.0,
    )
    weight = jnp.broadcast_to(weight, (token_index, n_experts, 2, capacity))
    chunks = 2
    part = capacity // chunks
    select2 = select2.reshape(2 * n_experts, capacity, token_index)
    moe = resid_f
    for c in range(chunks):
        picked_rows = select2[:, c * part:(c + 1) * part].reshape(-1, token_index)
        outgoing = jnp.dot(
            picked_rows.astype(jnp.bfloat16), normed, preferred_element_type=jnp.float32
        ).astype(jnp.bfloat16)
        outgoing = outgoing.reshape(2 * n_experts, part, D)
        rows = lax.all_to_all(outgoing, ("req", "exp"), split_axis=0, concat_axis=0, tiled=True)
        flat_rows = rows.reshape(-1, D)
        gate_part = jnp.dot(flat_rows, w_gate[0], preferred_element_type=jnp.float32)
        up_part = jnp.dot(flat_rows, w_up[0], preferred_element_type=jnp.float32)
        inner = (jax.nn.silu(gate_part) * up_part).astype(jnp.bfloat16)
        returned = lax.all_to_all(
            jnp.dot(inner, w_down[0], preferred_element_type=jnp.float32)
            .astype(jnp.bfloat16)
            .reshape(rows.shape),
            ("req", "exp"),
            split_axis=0,
            concat_axis=0,
            tiled=True,
        ).reshape(-1, D)
        chunk_weight = weight[:, :, :, c * part:(c + 1) * part].reshape(token_index, -1)
        high = chunk_weight.astype(jnp.bfloat16)
        low = (chunk_weight - high.astype(jnp.float32)).astype(jnp.bfloat16)
        moe = (
            moe
            + jnp.dot(high, returned, preferred_element_type=jnp.float32)
            + jnp.dot(low, returned, preferred_element_type=jnp.float32)
        )
    return moe.astype(jnp.bfloat16)


def solution(mesh):
    placed = (
        P(("req", "exp"), None),
        P(("req", "exp"), None),
        P(("req", "exp"), None),
        P("req", None),
        P("req", None, None),
        P("req", None, None),
        P(),
        P(),
        P(("req", "exp"), None),
        P(("req", "exp"), None, None),
        P(("req", "exp"), None, None),
        P(("req", "exp"), None, None),
    )
    return jax.shard_map(
        on_device, mesh=mesh, in_specs=placed, out_specs=P(("req", "exp"), None), check_vma=False
    )
```

```python
import functools
import math

import jax
import jax.numpy as jnp
from jax import lax
from jax.experimental import pallas as pl
from jax.experimental.pallas import tpu as pltpu
from jax.sharding import PartitionSpec as P

D = 2560
QUERY_HEADS = 10
KEY_VALUE_HEADS = 2
HEAD_SIZE = 128
TOP = 6
PAGE_TOKENS = 128


NEGATIVE_MASK = -1e30
EPS = 1e-06


KEY_BLOCK = 512


def attn_kernel(flags_ref, q_ref, w_ref, kv_ref, m_in, l_in, acc_in, *refs, first_call, last_call, groups, reps, hs):
    if last_call:
        o_ref, qs, m_ref, l_ref, acc_ref = refs
    else:
        m_out, l_out, acc_out, qs, m_ref, l_ref, acc_ref = refs
    j = pl.program_id(0)
    t = q_ref.shape[0]
    key_block = kv_ref.shape[0]

    @pl.when(j == 0)
    def _():
        for g in range(groups):
            qs[g] = jnp.concatenate(
                [q_ref[:, (g * reps + h) * hs:(g * reps + h + 1) * hs] for h in range(reps)], axis=0)
        if first_call:
            m_ref[...] = jnp.full(m_ref.shape, NEGATIVE_MASK, jnp.float32)
            l_ref[...] = jnp.zeros(l_ref.shape, jnp.float32)
            acc_ref[...] = jnp.zeros(acc_ref.shape, jnp.float32)
        else:
            m_ref[...] = m_in[...]
            l_ref[...] = l_in[...]
            acc_ref[...] = acc_in[...]

    @pl.when(flags_ref[j] > 0)
    def _():
        w = w_ref[...].astype(jnp.float32)
        live = (w > 0)[None]
        for g in range(groups):
            k = kv_ref[:, g * hs:(g + 1) * hs]
            v = kv_ref[:, (groups + g) * hs:(groups + g + 1) * hs]
            s = lax.dot_general(qs[g], k, (((1,), (1,)), ((), ())),
                                preferred_element_type=jnp.float32) * (1.0 / math.sqrt(hs))
            s = jnp.where(live, s.reshape(reps, t, key_block), NEGATIVE_MASK)
            m_old = m_ref[g].reshape(reps, t, 1)
            m_new = jnp.maximum(m_old, jnp.max(s, axis=-1, keepdims=True))
            p = jnp.exp(s - m_new) * w[None]
            alpha = jnp.exp(m_old - m_new)
            l_ref[g] = (alpha * l_ref[g].reshape(reps, t, 1) + jnp.sum(p, axis=-1, keepdims=True)).reshape(reps * t, 1)
            pv = jnp.dot(p.reshape(reps * t, key_block).astype(jnp.bfloat16), v, preferred_element_type=jnp.float32)
            acc_ref[g] = alpha.reshape(reps * t, 1) * acc_ref[g] + pv
            m_ref[g] = m_new.reshape(reps * t, 1)

    @pl.when(j == pl.num_programs(0) - 1)
    def _():
        if last_call:
            for g in range(groups):
                for h in range(reps):
                    rows = slice(h * t, (h + 1) * t)
                    o_ref[:, (g * reps + h) * hs:(g * reps + h + 1) * hs] = (
                        acc_ref[g, rows, :] / l_ref[g, rows, :]).astype(o_ref.dtype)
        else:
            m_out[...] = m_ref[...]
            l_out[...] = l_ref[...]
            acc_out[...] = acc_ref[...]


def flash(queries, weights, kv_rows, carry, first_call, last_call, groups, hs):
    t, width = queries.shape
    reps = width // hs // groups
    n_blocks = kv_rows.shape[0] // KEY_BLOCK
    flags = (jnp.max(weights.reshape(t, n_blocks, KEY_BLOCK), axis=(0, 2)) > 0).astype(jnp.int32)
    kern = functools.partial(attn_kernel, first_call=first_call, last_call=last_call,
                             groups=groups, reps=reps, hs=hs)
    state = [
        jax.ShapeDtypeStruct((groups, reps * t, 1), jnp.float32),
        jax.ShapeDtypeStruct((groups, reps * t, 1), jnp.float32),
        jax.ShapeDtypeStruct((groups, reps * t, hs), jnp.float32),
    ]
    state_specs = [
        pl.BlockSpec((groups, reps * t, 1), lambda j, f: (0, 0, 0)),
        pl.BlockSpec((groups, reps * t, 1), lambda j, f: (0, 0, 0)),
        pl.BlockSpec((groups, reps * t, hs), lambda j, f: (0, 0, 0)),
    ]
    if last_call:
        out_shape = jax.ShapeDtypeStruct((t, width), jnp.bfloat16)
        out_specs = pl.BlockSpec((t, width), lambda j, f: (0, 0))
    else:
        out_shape, out_specs = state, state_specs
    grid_spec = pltpu.PrefetchScalarGridSpec(
        num_scalar_prefetch=1,
        grid=(n_blocks,),
        in_specs=[
            pl.BlockSpec((t, width), lambda j, f: (0, 0)),
            pl.BlockSpec((t, KEY_BLOCK), lambda j, f: (0, j)),
            pl.BlockSpec((KEY_BLOCK, kv_rows.shape[1]), lambda j, f: (j, 0)),
        ] + state_specs,
        out_specs=out_specs,
        scratch_shapes=[
            pltpu.VMEM((groups, reps * t, hs), jnp.bfloat16),
            pltpu.VMEM((groups, reps * t, 1), jnp.float32),
            pltpu.VMEM((groups, reps * t, 1), jnp.float32),
            pltpu.VMEM((groups, reps * t, hs), jnp.float32),
        ],
    )
    if carry is None:
        carry = tuple(jnp.zeros(s.shape, s.dtype) for s in state)
    return pl.pallas_call(kern, grid_spec=grid_spec, out_shape=out_shape)(
        flags, queries, weights, kv_rows, *carry)


def on_device(
    hidden,
    queries,
    suffix_kv,
    lengths,
    page_table,
    page_pool,
    w_out,
    w_router,
    routes,
    w_gate,
    w_up,
    w_down,
):
    token_index = hidden.shape[0]
    row_width = KEY_VALUE_HEADS * HEAD_SIZE
    request_groups = QUERY_HEADS // KEY_VALUE_HEADS
    request_count = lax.axis_size("req")
    pool_per_shard = page_pool.shape[0]
    pool_all = pool_per_shard * request_count
    positions = lax.axis_index("exp") * token_index + jnp.arange(token_index, dtype=jnp.int32)
    lens = lengths[0]
    ends = jnp.cumsum(lens)
    starts = ends - lens
    req_of = jnp.sum((positions[:, None] >= ends[None, :]).astype(jnp.int32), axis=1)
    pick = req_of[:, None] == jnp.arange(lens.shape[0], dtype=jnp.int32)[None, :]
    first = jnp.sum(jnp.where(pick, starts[None, :], 0), axis=1)
    split = (pool_per_shard + 1) // 2
    pool_first = lax.all_gather(page_pool[:split], "req", axis=0, tiled=True)
    pool_first, pool_later, suffix_after = lax.optimization_barrier(
        (pool_first, page_pool[split:], suffix_kv)
    )
    pool_second = lax.all_gather(pool_later, "req", axis=0, tiled=True)
    segment = lax.all_gather(suffix_after, "exp", axis=0, tiled=True)
    counts = jnp.sum(
        (page_table[0][:, :, None] == jnp.arange(pool_all, dtype=jnp.int32)[None, None, :]).astype(
            jnp.float32
        ),
        axis=1,
    )
    query_counts = jnp.dot(pick.astype(jnp.float32), counts, precision=lax.Precision.HIGHEST)
    keypos = jnp.arange(segment.shape[0], dtype=jnp.int32)
    suffix_weights = (keypos[None, :] <= positions[:, None]) & (keypos[None, :] >= first[:, None])
    shard_counts = query_counts.reshape(token_index, request_count, pool_per_shard)
    carry = None
    for pages, rows in (
        (shard_counts[:, :, :split], pool_first),
        (shard_counts[:, :, split:], pool_second),
    ):
        page_weights = jnp.repeat(
            pages.reshape(token_index, -1), PAGE_TOKENS, axis=1
        ).astype(jnp.bfloat16)
        carry = flash(
            queries,
            page_weights,
            rows.reshape(-1, 2 * row_width),
            carry,
            carry is None,
            False,
            KEY_VALUE_HEADS,
            HEAD_SIZE,
        )
    attended = flash(
        queries,
        suffix_weights.astype(jnp.bfloat16),
        segment,
        carry,
        False,
        True,
        KEY_VALUE_HEADS,
        HEAD_SIZE,
    )
    projected = jnp.dot(attended, w_out, preferred_element_type=jnp.float32)
    resid = lax.optimization_barrier((hidden.astype(jnp.float32) + projected).astype(jnp.bfloat16))
    resid_f = resid.astype(jnp.float32)
    normed = (resid_f * lax.rsqrt(jnp.mean(resid_f * resid_f, axis=1, keepdims=True) + EPS)).astype(
        jnp.bfloat16
    )
    n_experts = w_router.shape[1]
    logits = jnp.dot(normed, w_router, preferred_element_type=jnp.float32)
    expert_ids = jnp.arange(n_experts, dtype=jnp.int32)
    chosen = jnp.sum(
        jnp.where(routes[:, :, None] == expert_ids[None, None, :], logits[:, None, :], 0.0), axis=2
    )
    gates = jax.nn.softmax(chosen, axis=1)
    capacity = 16
    member = routes[:, :, None] == expert_ids[None, None, :]
    picks = jnp.any(member, axis=1).astype(jnp.float32)
    gate_of = jnp.sum(jnp.where(member, gates[:, :, None], 0.0), axis=1)
    earlier = (
        jnp.arange(token_index, dtype=jnp.int32)[:, None]
        > jnp.arange(token_index, dtype=jnp.int32)[None, :]
    ).astype(jnp.float32)
    rank = jnp.dot(earlier, picks, precision=lax.Precision.HIGHEST).astype(jnp.int32)
    place = jnp.arange(capacity, dtype=jnp.int32)
    select = (picks[None, :, :] > 0) & (rank[None, :, :] == place[:, None, None])
    select = jnp.transpose(select, (2, 0, 1))
    select2 = jnp.broadcast_to(
        select[:, None], (n_experts, 2, capacity, token_index)
    ).reshape(2 * n_experts * capacity, token_index)
    weight = jnp.where(
        jnp.transpose(select, (2, 0, 1))[:, :, None, :],
        gate_of[:, :, None, None],
        0.0,
    )
    weight = jnp.broadcast_to(weight, (token_index, n_experts, 2, capacity))
    chunks = 2
    part = capacity // chunks
    select2 = select2.reshape(2 * n_experts, capacity, token_index)
    moe = resid_f
    for c in range(chunks):
        picked_rows = select2[:, c * part:(c + 1) * part].reshape(-1, token_index)
        outgoing = jnp.dot(
            picked_rows.astype(jnp.bfloat16), normed, preferred_element_type=jnp.float32
        ).astype(jnp.bfloat16)
        outgoing = outgoing.reshape(2 * n_experts, part, D)
        rows = lax.all_to_all(outgoing, ("req", "exp"), split_axis=0, concat_axis=0, tiled=True)
        flat_rows = rows.reshape(-1, D)
        gate_part = jnp.dot(flat_rows, w_gate[0], preferred_element_type=jnp.float32)
        up_part = jnp.dot(flat_rows, w_up[0], preferred_element_type=jnp.float32)
        inner = (jax.nn.silu(gate_part) * up_part).astype(jnp.bfloat16)
        returned = lax.all_to_all(
            jnp.dot(inner, w_down[0], preferred_element_type=jnp.float32)
            .astype(jnp.bfloat16)
            .reshape(rows.shape),
            ("req", "exp"),
            split_axis=0,
            concat_axis=0,
            tiled=True,
        ).reshape(-1, D)
        chunk_weight = weight[:, :, :, c * part:(c + 1) * part].reshape(token_index, -1)
        high = chunk_weight.astype(jnp.bfloat16)
        low = (chunk_weight - high.astype(jnp.float32)).astype(jnp.bfloat16)
        moe = (
            moe
            + jnp.dot(high, returned, preferred_element_type=jnp.float32)
            + jnp.dot(low, returned, preferred_element_type=jnp.float32)
        )
    return moe.astype(jnp.bfloat16)


def solution(mesh):
    placed = (
        P(("req", "exp"), None),
        P(("req", "exp"), None),
        P(("req", "exp"), None),
        P("req", None),
        P("req", None, None),
        P("req", None, None),
        P(),
        P(),
        P(("req", "exp"), None),
        P(("req", "exp"), None, None),
        P(("req", "exp"), None, None),
        P(("req", "exp"), None, None),
    )
    return jax.shard_map(
        on_device, mesh=mesh, in_specs=placed, out_specs=P(("req", "exp"), None), check_vma=False
    )
```

```python
import functools
import math

import jax
import jax.numpy as jnp
from jax import lax
from jax.experimental import pallas as pl
from jax.experimental.pallas import tpu as pltpu
from jax.sharding import PartitionSpec as P

D = 2560
QUERY_HEADS = 10
KEY_VALUE_HEADS = 2
HEAD_SIZE = 128
TOP = 6
PAGE_TOKENS = 128


NEGATIVE_MASK = -1e30
EPS = 1e-06


KEY_BLOCK = 512
GROUP_REACH = 1024


def attn_kernel(flags_ref, q_ref, w_ref, kv_ref, m_in, l_in, acc_in, *refs, first_call, last_call, groups, reps, hs):
    if last_call:
        o_ref, qs, m_ref, l_ref, acc_ref = refs
    else:
        m_out, l_out, acc_out, qs, m_ref, l_ref, acc_ref = refs
    j = pl.program_id(0)
    t = q_ref.shape[0]
    key_block = kv_ref.shape[0]

    @pl.when(j == 0)
    def _():
        for g in range(groups):
            qs[g] = jnp.concatenate(
                [q_ref[:, (g * reps + h) * hs:(g * reps + h + 1) * hs] for h in range(reps)], axis=0)
        if first_call:
            m_ref[...] = jnp.full(m_ref.shape, NEGATIVE_MASK, jnp.float32)
            l_ref[...] = jnp.zeros(l_ref.shape, jnp.float32)
            acc_ref[...] = jnp.zeros(acc_ref.shape, jnp.float32)
        else:
            m_ref[...] = m_in[...]
            l_ref[...] = l_in[...]
            acc_ref[...] = acc_in[...]

    @pl.when(flags_ref[j] > 0)
    def _():
        w = w_ref[...].astype(jnp.float32)
        live = (w > 0)[None]
        for g in range(groups):
            k = kv_ref[:, g * hs:(g + 1) * hs]
            v = kv_ref[:, (groups + g) * hs:(groups + g + 1) * hs]
            s = lax.dot_general(qs[g], k, (((1,), (1,)), ((), ())),
                                preferred_element_type=jnp.float32) * (1.0 / math.sqrt(hs))
            s = jnp.where(live, s.reshape(reps, t, key_block), NEGATIVE_MASK)
            m_old = m_ref[g].reshape(reps, t, 1)
            m_new = jnp.maximum(m_old, jnp.max(s, axis=-1, keepdims=True))
            p = jnp.exp(s - m_new) * w[None]
            alpha = jnp.exp(m_old - m_new)
            l_ref[g] = (alpha * l_ref[g].reshape(reps, t, 1) + jnp.sum(p, axis=-1, keepdims=True)).reshape(reps * t, 1)
            pv = jnp.dot(p.reshape(reps * t, key_block).astype(jnp.bfloat16), v, preferred_element_type=jnp.float32)
            acc_ref[g] = alpha.reshape(reps * t, 1) * acc_ref[g] + pv
            m_ref[g] = m_new.reshape(reps * t, 1)

    @pl.when(j == pl.num_programs(0) - 1)
    def _():
        if last_call:
            for g in range(groups):
                for h in range(reps):
                    rows = slice(h * t, (h + 1) * t)
                    o_ref[:, (g * reps + h) * hs:(g * reps + h + 1) * hs] = (
                        acc_ref[g, rows, :] / l_ref[g, rows, :]).astype(o_ref.dtype)
        else:
            m_out[...] = m_ref[...]
            l_out[...] = l_ref[...]
            acc_out[...] = acc_ref[...]


def flash(queries, weights, kv_rows, carry, first_call, last_call, groups, hs, key_block=KEY_BLOCK):
    t, width = queries.shape
    reps = width // hs // groups
    n_blocks = kv_rows.shape[0] // key_block
    flags = (jnp.max(weights.reshape(t, n_blocks, key_block), axis=(0, 2)) > 0).astype(jnp.int32)
    kern = functools.partial(attn_kernel, first_call=first_call, last_call=last_call,
                             groups=groups, reps=reps, hs=hs)
    state = [
        jax.ShapeDtypeStruct((groups, reps * t, 1), jnp.float32),
        jax.ShapeDtypeStruct((groups, reps * t, 1), jnp.float32),
        jax.ShapeDtypeStruct((groups, reps * t, hs), jnp.float32),
    ]
    state_specs = [
        pl.BlockSpec((groups, reps * t, 1), lambda j, f: (0, 0, 0)),
        pl.BlockSpec((groups, reps * t, 1), lambda j, f: (0, 0, 0)),
        pl.BlockSpec((groups, reps * t, hs), lambda j, f: (0, 0, 0)),
    ]
    if last_call:
        out_shape = jax.ShapeDtypeStruct((t, width), jnp.bfloat16)
        out_specs = pl.BlockSpec((t, width), lambda j, f: (0, 0))
    else:
        out_shape, out_specs = state, state_specs
    grid_spec = pltpu.PrefetchScalarGridSpec(
        num_scalar_prefetch=1,
        grid=(n_blocks,),
        in_specs=[
            pl.BlockSpec((t, width), lambda j, f: (0, 0)),
            pl.BlockSpec((t, key_block), lambda j, f: (0, j)),
            pl.BlockSpec((key_block, kv_rows.shape[1]), lambda j, f: (j, 0)),
        ] + state_specs,
        out_specs=out_specs,
        scratch_shapes=[
            pltpu.VMEM((groups, reps * t, hs), jnp.bfloat16),
            pltpu.VMEM((groups, reps * t, 1), jnp.float32),
            pltpu.VMEM((groups, reps * t, 1), jnp.float32),
            pltpu.VMEM((groups, reps * t, hs), jnp.float32),
        ],
    )
    if carry is None:
        carry = tuple(jnp.zeros(s.shape, s.dtype) for s in state)
    return pl.pallas_call(kern, grid_spec=grid_spec, out_shape=out_shape)(
        flags, queries, weights, kv_rows, *carry)


def on_device(
    hidden,
    queries,
    suffix_kv,
    lengths,
    page_table,
    page_pool,
    w_out,
    w_router,
    routes,
    w_gate,
    w_up,
    w_down,
):
    token_index = hidden.shape[0]
    row_width = KEY_VALUE_HEADS * HEAD_SIZE
    request_groups = QUERY_HEADS // KEY_VALUE_HEADS
    request_count = lax.axis_size("req")
    pool_per_shard = page_pool.shape[0]
    pool_all = pool_per_shard * request_count
    positions = lax.axis_index("exp") * token_index + jnp.arange(token_index, dtype=jnp.int32)
    lens = lengths[0]
    ends = jnp.cumsum(lens)
    starts = ends - lens
    req_of = jnp.sum((positions[:, None] >= ends[None, :]).astype(jnp.int32), axis=1)
    pick = req_of[:, None] == jnp.arange(lens.shape[0], dtype=jnp.int32)[None, :]
    first = jnp.sum(jnp.where(pick, starts[None, :], 0), axis=1)
    split = (pool_per_shard + 1) // 2
    pool_first = lax.all_gather(page_pool[:split], "req", axis=0, tiled=True)
    pool_first, pool_later = lax.optimization_barrier((pool_first, page_pool[split:]))
    pool_second = lax.all_gather(pool_later, "req", axis=0, tiled=True)
    exp_count = lax.axis_size("exp")
    reach = min(exp_count - 1, (GROUP_REACH + token_index - 2) // token_index)
    segment = jnp.concatenate(
        [
            lax.ppermute(
                suffix_kv, "exp", [(s, (s + k) % exp_count) for s in range(exp_count)]
            )
            for k in range(reach, 0, -1)
        ]
        + [suffix_kv],
        axis=0,
    )
    source_block = (lax.axis_index("exp") - jnp.arange(reach, -1, -1, dtype=jnp.int32)) % exp_count
    counts = jnp.sum(
        (page_table[0][:, :, None] == jnp.arange(pool_all, dtype=jnp.int32)[None, None, :]).astype(
            jnp.float32
        ),
        axis=1,
    )
    query_counts = jnp.dot(pick.astype(jnp.float32), counts, precision=lax.Precision.HIGHEST)
    keypos = (
        source_block[:, None] * token_index + jnp.arange(token_index, dtype=jnp.int32)[None, :]
    ).reshape(-1)
    suffix_weights = (keypos[None, :] <= positions[:, None]) & (keypos[None, :] >= first[:, None])
    shard_counts = query_counts.reshape(token_index, request_count, pool_per_shard)
    carry = None
    for pages, rows in (
        (shard_counts[:, :, :split], pool_first),
        (shard_counts[:, :, split:], pool_second),
    ):
        page_weights = jnp.repeat(
            pages.reshape(token_index, -1), PAGE_TOKENS, axis=1
        ).astype(jnp.bfloat16)
        carry = flash(
            queries,
            page_weights,
            rows.reshape(-1, 2 * row_width),
            carry,
            carry is None,
            False,
            KEY_VALUE_HEADS,
            HEAD_SIZE,
        )
    attended = flash(
        queries,
        suffix_weights.astype(jnp.bfloat16),
        segment,
        carry,
        False,
        True,
        KEY_VALUE_HEADS,
        HEAD_SIZE,
        segment.shape[0] // 3,
    )
    projected = jnp.dot(attended, w_out, preferred_element_type=jnp.float32)
    resid = lax.optimization_barrier((hidden.astype(jnp.float32) + projected).astype(jnp.bfloat16))
    resid_f = resid.astype(jnp.float32)
    normed = (resid_f * lax.rsqrt(jnp.mean(resid_f * resid_f, axis=1, keepdims=True) + EPS)).astype(
        jnp.bfloat16
    )
    n_experts = w_router.shape[1]
    logits = jnp.dot(normed, w_router, preferred_element_type=jnp.float32)
    expert_ids = jnp.arange(n_experts, dtype=jnp.int32)
    chosen = jnp.sum(
        jnp.where(routes[:, :, None] == expert_ids[None, None, :], logits[:, None, :], 0.0), axis=2
    )
    gates = jax.nn.softmax(chosen, axis=1)
    capacity = 16
    member = routes[:, :, None] == expert_ids[None, None, :]
    picks = jnp.any(member, axis=1).astype(jnp.float32)
    gate_of = jnp.sum(jnp.where(member, gates[:, :, None], 0.0), axis=1)
    earlier = (
        jnp.arange(token_index, dtype=jnp.int32)[:, None]
        > jnp.arange(token_index, dtype=jnp.int32)[None, :]
    ).astype(jnp.float32)
    rank = jnp.dot(earlier, picks, precision=lax.Precision.HIGHEST).astype(jnp.int32)
    place = jnp.arange(capacity, dtype=jnp.int32)
    select = (picks[None, :, :] > 0) & (rank[None, :, :] == place[:, None, None])
    select = jnp.transpose(select, (2, 0, 1))
    select2 = jnp.broadcast_to(
        select[:, None], (n_experts, 2, capacity, token_index)
    ).reshape(2 * n_experts * capacity, token_index)
    weight = jnp.where(
        jnp.transpose(select, (2, 0, 1))[:, :, None, :],
        gate_of[:, :, None, None],
        0.0,
    )
    weight = jnp.broadcast_to(weight, (token_index, n_experts, 2, capacity))
    chunks = 2
    part = capacity // chunks
    select2 = select2.reshape(2 * n_experts, capacity, token_index)
    moe = resid_f
    for c in range(chunks):
        picked_rows = select2[:, c * part:(c + 1) * part].reshape(-1, token_index)
        outgoing = jnp.dot(
            picked_rows.astype(jnp.bfloat16), normed, preferred_element_type=jnp.float32
        ).astype(jnp.bfloat16)
        outgoing = outgoing.reshape(2 * n_experts, part, D)
        rows = lax.all_to_all(outgoing, ("req", "exp"), split_axis=0, concat_axis=0, tiled=True)
        flat_rows = rows.reshape(-1, D)
        gate_part = jnp.dot(flat_rows, w_gate[0], preferred_element_type=jnp.float32)
        up_part = jnp.dot(flat_rows, w_up[0], preferred_element_type=jnp.float32)
        inner = (jax.nn.silu(gate_part) * up_part).astype(jnp.bfloat16)
        returned = lax.all_to_all(
            jnp.dot(inner, w_down[0], preferred_element_type=jnp.float32)
            .astype(jnp.bfloat16)
            .reshape(rows.shape),
            ("req", "exp"),
            split_axis=0,
            concat_axis=0,
            tiled=True,
        ).reshape(-1, D)
        chunk_weight = weight[:, :, :, c * part:(c + 1) * part].reshape(token_index, -1)
        high = chunk_weight.astype(jnp.bfloat16)
        low = (chunk_weight - high.astype(jnp.float32)).astype(jnp.bfloat16)
        moe = (
            moe
            + jnp.dot(high, returned, preferred_element_type=jnp.float32)
            + jnp.dot(low, returned, preferred_element_type=jnp.float32)
        )
    return moe.astype(jnp.bfloat16)


def solution(mesh):
    placed = (
        P(("req", "exp"), None),
        P(("req", "exp"), None),
        P(("req", "exp"), None),
        P("req", None),
        P("req", None, None),
        P("req", None, None),
        P(),
        P(),
        P(("req", "exp"), None),
        P(("req", "exp"), None, None),
        P(("req", "exp"), None, None),
        P(("req", "exp"), None, None),
    )
    return jax.shard_map(
        on_device, mesh=mesh, in_specs=placed, out_specs=P(("req", "exp"), None), check_vma=False
    )
```

```python
import functools
import math

import jax
import jax.numpy as jnp
from jax import lax
from jax.experimental import pallas as pl
from jax.experimental.pallas import tpu as pltpu
from jax.sharding import PartitionSpec as P

D = 2560
QUERY_HEADS = 10
KEY_VALUE_HEADS = 2
HEAD_SIZE = 128
TOP = 6
PAGE_TOKENS = 128


NEGATIVE_MASK = -1e30
EPS = 1e-06


KEY_BLOCK = 512
LOG2_E = 1.4426950408889634


def attn_kernel(flags_ref, q_ref, w_ref, kv_ref, m_in, l_in, acc_in, *refs, first_call, last_call, groups, reps, hs):
    if last_call:
        o_ref, qs, m_ref, l_ref, acc_ref = refs
    else:
        m_out, l_out, acc_out, qs, m_ref, l_ref, acc_ref = refs
    j = pl.program_id(0)
    t = q_ref.shape[0]
    key_block = kv_ref.shape[0]

    @pl.when(j == 0)
    def _():
        for g in range(groups):
            qs[g] = jnp.concatenate(
                [q_ref[:, (g * reps + h) * hs:(g * reps + h + 1) * hs] for h in range(reps)], axis=0)
        if first_call:
            m_ref[...] = jnp.full(m_ref.shape, NEGATIVE_MASK, jnp.float32)
            l_ref[...] = jnp.zeros(l_ref.shape, jnp.float32)
            acc_ref[...] = jnp.zeros(acc_ref.shape, jnp.float32)
        else:
            m_ref[...] = m_in[...]
            l_ref[...] = l_in[...]
            acc_ref[...] = acc_in[...]

    @pl.when(flags_ref[j] > 0)
    def _():
        bias = w_ref[...][None]
        for g in range(groups):
            k = kv_ref[:, g * hs:(g + 1) * hs]
            v = kv_ref[:, (groups + g) * hs:(groups + g + 1) * hs]
            s = lax.dot_general(qs[g], k, (((1,), (1,)), ((), ())),
                                preferred_element_type=jnp.float32) * (LOG2_E / math.sqrt(hs))
            s = s.reshape(reps, t, key_block) + bias
            m_old = m_ref[g].reshape(reps, t, 1)
            m_new = jnp.maximum(m_old, jnp.max(s, axis=-1, keepdims=True))
            p = jnp.exp2(s - m_new)
            alpha = jnp.exp2(m_old - m_new)
            l_ref[g] = (alpha * l_ref[g].reshape(reps, t, 1) + jnp.sum(p, axis=-1, keepdims=True)).reshape(reps * t, 1)
            pv = jnp.dot(p.reshape(reps * t, key_block).astype(jnp.bfloat16), v, preferred_element_type=jnp.float32)
            acc_ref[g] = alpha.reshape(reps * t, 1) * acc_ref[g] + pv
            m_ref[g] = m_new.reshape(reps * t, 1)

    @pl.when(j == pl.num_programs(0) - 1)
    def _():
        if last_call:
            for g in range(groups):
                for h in range(reps):
                    rows = slice(h * t, (h + 1) * t)
                    o_ref[:, (g * reps + h) * hs:(g * reps + h + 1) * hs] = (
                        acc_ref[g, rows, :] / l_ref[g, rows, :]).astype(o_ref.dtype)
        else:
            m_out[...] = m_ref[...]
            l_out[...] = l_ref[...]
            acc_out[...] = acc_ref[...]


def flash(queries, weights, kv_rows, carry, first_call, last_call, groups, hs):
    t, width = queries.shape
    reps = width // hs // groups
    n_blocks = kv_rows.shape[0] // KEY_BLOCK
    flags = (
        jnp.max(weights.reshape(t, n_blocks, KEY_BLOCK), axis=(0, 2)) > 0.5 * NEGATIVE_MASK
    ).astype(jnp.int32)
    kern = functools.partial(attn_kernel, first_call=first_call, last_call=last_call,
                             groups=groups, reps=reps, hs=hs)
    state = [
        jax.ShapeDtypeStruct((groups, reps * t, 1), jnp.float32),
        jax.ShapeDtypeStruct((groups, reps * t, 1), jnp.float32),
        jax.ShapeDtypeStruct((groups, reps * t, hs), jnp.float32),
    ]
    state_specs = [
        pl.BlockSpec((groups, reps * t, 1), lambda j, f: (0, 0, 0)),
        pl.BlockSpec((groups, reps * t, 1), lambda j, f: (0, 0, 0)),
        pl.BlockSpec((groups, reps * t, hs), lambda j, f: (0, 0, 0)),
    ]
    if last_call:
        out_shape = jax.ShapeDtypeStruct((t, width), jnp.bfloat16)
        out_specs = pl.BlockSpec((t, width), lambda j, f: (0, 0))
    else:
        out_shape, out_specs = state, state_specs
    grid_spec = pltpu.PrefetchScalarGridSpec(
        num_scalar_prefetch=1,
        grid=(n_blocks,),
        in_specs=[
            pl.BlockSpec((t, width), lambda j, f: (0, 0)),
            pl.BlockSpec((t, KEY_BLOCK), lambda j, f: (0, j)),
            pl.BlockSpec((KEY_BLOCK, kv_rows.shape[1]), lambda j, f: (j, 0)),
        ] + state_specs,
        out_specs=out_specs,
        scratch_shapes=[
            pltpu.VMEM((groups, reps * t, hs), jnp.bfloat16),
            pltpu.VMEM((groups, reps * t, 1), jnp.float32),
            pltpu.VMEM((groups, reps * t, 1), jnp.float32),
            pltpu.VMEM((groups, reps * t, hs), jnp.float32),
        ],
    )
    if carry is None:
        carry = tuple(jnp.zeros(s.shape, s.dtype) for s in state)
    return pl.pallas_call(kern, grid_spec=grid_spec, out_shape=out_shape)(
        flags, queries, weights, kv_rows, *carry)


def on_device(
    hidden,
    queries,
    suffix_kv,
    lengths,
    page_table,
    page_pool,
    w_out,
    w_router,
    routes,
    w_gate,
    w_up,
    w_down,
):
    token_index = hidden.shape[0]
    row_width = KEY_VALUE_HEADS * HEAD_SIZE
    request_groups = QUERY_HEADS // KEY_VALUE_HEADS
    request_count = lax.axis_size("req")
    pool_per_shard = page_pool.shape[0]
    pool_all = pool_per_shard * request_count
    positions = lax.axis_index("exp") * token_index + jnp.arange(token_index, dtype=jnp.int32)
    lens = lengths[0]
    ends = jnp.cumsum(lens)
    starts = ends - lens
    req_of = jnp.sum((positions[:, None] >= ends[None, :]).astype(jnp.int32), axis=1)
    pick = req_of[:, None] == jnp.arange(lens.shape[0], dtype=jnp.int32)[None, :]
    first = jnp.sum(jnp.where(pick, starts[None, :], 0), axis=1)
    pool_rows = lax.all_gather(page_pool, "req", axis=0, tiled=True).reshape(
        pool_all * PAGE_TOKENS, 2 * row_width
    )
    pool_rows, suffix_after = lax.optimization_barrier((pool_rows, suffix_kv))
    segment = lax.all_gather(suffix_after, "exp", axis=0, tiled=True)
    counts = jnp.sum(
        (page_table[0][:, :, None] == jnp.arange(pool_all, dtype=jnp.int32)[None, None, :]).astype(
            jnp.float32
        ),
        axis=1,
    )
    query_counts = jnp.dot(pick.astype(jnp.float32), counts, precision=lax.Precision.HIGHEST)
    keypos = jnp.arange(segment.shape[0], dtype=jnp.int32)
    suffix_weights = (keypos[None, :] <= positions[:, None]) & (keypos[None, :] >= first[:, None])
    pool_bias = jnp.where(
        query_counts > 0, jnp.log2(jnp.maximum(query_counts, 1.0)), NEGATIVE_MASK
    )
    pool_weights = jnp.repeat(pool_bias, PAGE_TOKENS, axis=1)
    carry = flash(queries, pool_weights, pool_rows, None, True, False, KEY_VALUE_HEADS, HEAD_SIZE)
    attended = flash(
        queries,
        jnp.where(suffix_weights, 0.0, NEGATIVE_MASK).astype(jnp.float32),
        segment,
        carry,
        False,
        True,
        KEY_VALUE_HEADS,
        HEAD_SIZE,
    )
    projected = jnp.dot(attended, w_out, preferred_element_type=jnp.float32)
    resid = lax.optimization_barrier((hidden.astype(jnp.float32) + projected).astype(jnp.bfloat16))
    resid_f = resid.astype(jnp.float32)
    normed = (resid_f * lax.rsqrt(jnp.mean(resid_f * resid_f, axis=1, keepdims=True) + EPS)).astype(
        jnp.bfloat16
    )
    n_experts = w_router.shape[1]
    logits = jnp.dot(normed, w_router, preferred_element_type=jnp.float32)
    expert_ids = jnp.arange(n_experts, dtype=jnp.int32)
    chosen = jnp.sum(
        jnp.where(routes[:, :, None] == expert_ids[None, None, :], logits[:, None, :], 0.0), axis=2
    )
    gates = jax.nn.softmax(chosen, axis=1)
    capacity = 16
    member = routes[:, :, None] == expert_ids[None, None, :]
    picks = jnp.any(member, axis=1).astype(jnp.float32)
    gate_of = jnp.sum(jnp.where(member, gates[:, :, None], 0.0), axis=1)
    earlier = (
        jnp.arange(token_index, dtype=jnp.int32)[:, None]
        > jnp.arange(token_index, dtype=jnp.int32)[None, :]
    ).astype(jnp.float32)
    rank = jnp.dot(earlier, picks, precision=lax.Precision.HIGHEST).astype(jnp.int32)
    place = jnp.arange(capacity, dtype=jnp.int32)
    select = (picks[None, :, :] > 0) & (rank[None, :, :] == place[:, None, None])
    select = jnp.transpose(select, (2, 0, 1))
    select2 = jnp.broadcast_to(
        select[:, None], (n_experts, 2, capacity, token_index)
    ).reshape(2 * n_experts * capacity, token_index)
    weight = jnp.where(
        jnp.transpose(select, (2, 0, 1))[:, :, None, :],
        gate_of[:, :, None, None],
        0.0,
    )
    weight = jnp.broadcast_to(weight, (token_index, n_experts, 2, capacity))
    chunks = 2
    part = capacity // chunks
    select2 = select2.reshape(2 * n_experts, capacity, token_index)
    moe = resid_f
    for c in range(chunks):
        picked_rows = select2[:, c * part:(c + 1) * part].reshape(-1, token_index)
        outgoing = jnp.dot(
            picked_rows.astype(jnp.bfloat16), normed, preferred_element_type=jnp.float32
        ).astype(jnp.bfloat16)
        outgoing = outgoing.reshape(2 * n_experts, part, D)
        rows = lax.all_to_all(outgoing, ("req", "exp"), split_axis=0, concat_axis=0, tiled=True)
        flat_rows = rows.reshape(-1, D)
        gate_part = jnp.dot(flat_rows, w_gate[0], preferred_element_type=jnp.float32)
        up_part = jnp.dot(flat_rows, w_up[0], preferred_element_type=jnp.float32)
        inner = (jax.nn.silu(gate_part) * up_part).astype(jnp.bfloat16)
        returned = lax.all_to_all(
            jnp.dot(inner, w_down[0], preferred_element_type=jnp.float32)
            .astype(jnp.bfloat16)
            .reshape(rows.shape),
            ("req", "exp"),
            split_axis=0,
            concat_axis=0,
            tiled=True,
        ).reshape(-1, D)
        chunk_weight = weight[:, :, :, c * part:(c + 1) * part].reshape(token_index, -1)
        high = chunk_weight.astype(jnp.bfloat16)
        low = (chunk_weight - high.astype(jnp.float32)).astype(jnp.bfloat16)
        moe = (
            moe
            + jnp.dot(high, returned, preferred_element_type=jnp.float32)
            + jnp.dot(low, returned, preferred_element_type=jnp.float32)
        )
    return moe.astype(jnp.bfloat16)


def solution(mesh):
    placed = (
        P(("req", "exp"), None),
        P(("req", "exp"), None),
        P(("req", "exp"), None),
        P("req", None),
        P("req", None, None),
        P("req", None, None),
        P(),
        P(),
        P(("req", "exp"), None),
        P(("req", "exp"), None, None),
        P(("req", "exp"), None, None),
        P(("req", "exp"), None, None),
    )
    return jax.shard_map(
        on_device, mesh=mesh, in_specs=placed, out_specs=P(("req", "exp"), None), check_vma=False
    )
```

```python
import functools
import math

import jax
import jax.numpy as jnp
from jax import lax
from jax.experimental import pallas as pl
from jax.experimental.pallas import tpu as pltpu
from jax.sharding import PartitionSpec as P

D = 2560
QUERY_HEADS = 10
KEY_VALUE_HEADS = 2
HEAD_SIZE = 128
TOP = 6
PAGE_TOKENS = 128


NEGATIVE_MASK = -1e30
EPS = 1e-06


KEY_BLOCK = 512
LOG2_E = 1.4426950408889634
SOFTMAX_ROWS = 32


def attn_kernel(flags_ref, q_ref, w_ref, kv_ref, m_in, l_in, acc_in, *refs, first_call, last_call, groups, reps, hs):
    if last_call:
        o_ref, qs, m_ref, l_ref, acc_ref, s_scr, p_scr, a_scr = refs
    else:
        m_out, l_out, acc_out, qs, m_ref, l_ref, acc_ref, s_scr, p_scr, a_scr = refs
    j = pl.program_id(0)
    t = q_ref.shape[0]
    key_block = kv_ref.shape[0]

    @pl.when(j == 0)
    def _():
        for g in range(groups):
            qs[g] = jnp.concatenate(
                [q_ref[:, (g * reps + h) * hs:(g * reps + h + 1) * hs] for h in range(reps)], axis=0)
        if first_call:
            m_ref[...] = jnp.full(m_ref.shape, NEGATIVE_MASK, jnp.float32)
            l_ref[...] = jnp.zeros(l_ref.shape, jnp.float32)
            acc_ref[...] = jnp.zeros(acc_ref.shape, jnp.float32)
        else:
            m_ref[...] = m_in[...]
            l_ref[...] = l_in[...]
            acc_ref[...] = acc_in[...]

    @pl.when(flags_ref[j] > 0)
    def _():
        chunk = SOFTMAX_ROWS
        for g in range(groups):
            k = kv_ref[:, g * hs:(g + 1) * hs]
            v = kv_ref[:, (groups + g) * hs:(groups + g + 1) * hs]
            s_scr[...] = lax.dot_general(qs[g], k, (((1,), (1,)), ((), ())),
                                         preferred_element_type=jnp.float32)

            def body(i, c):
                r = pl.multiple_of(i * chunk, chunk)
                b = pl.multiple_of((i * chunk) % t, chunk)
                s = s_scr[pl.ds(r, chunk), :] * (LOG2_E / math.sqrt(hs)) + w_ref[pl.ds(b, chunk), :]
                m_old = m_ref[g, pl.ds(r, chunk), :]
                m_new = jnp.maximum(m_old, jnp.max(s, axis=-1, keepdims=True))
                p = jnp.exp2(s - m_new)
                alpha = jnp.exp2(m_old - m_new)
                l_ref[g, pl.ds(r, chunk), :] = alpha * l_ref[g, pl.ds(r, chunk), :] + jnp.sum(
                    p, axis=-1, keepdims=True)
                m_ref[g, pl.ds(r, chunk), :] = m_new
                a_scr[pl.ds(r, chunk), :] = alpha
                p_scr[pl.ds(r, chunk), :] = p.astype(jnp.bfloat16)
                return c

            lax.fori_loop(0, reps * t // chunk, body, 0, unroll=2)
            pv = jnp.dot(p_scr[...], v, preferred_element_type=jnp.float32)
            acc_ref[g] = a_scr[...] * acc_ref[g] + pv

    @pl.when(j == pl.num_programs(0) - 1)
    def _():
        if last_call:
            for g in range(groups):
                for h in range(reps):
                    rows = slice(h * t, (h + 1) * t)
                    o_ref[:, (g * reps + h) * hs:(g * reps + h + 1) * hs] = (
                        acc_ref[g, rows, :] / l_ref[g, rows, :]).astype(o_ref.dtype)
        else:
            m_out[...] = m_ref[...]
            l_out[...] = l_ref[...]
            acc_out[...] = acc_ref[...]


def flash(queries, weights, kv_rows, carry, first_call, last_call, groups, hs):
    t, width = queries.shape
    reps = width // hs // groups
    n_blocks = kv_rows.shape[0] // KEY_BLOCK
    flags = (
        jnp.max(weights.reshape(t, n_blocks, KEY_BLOCK), axis=(0, 2)) > 0.5 * NEGATIVE_MASK
    ).astype(jnp.int32)
    kern = functools.partial(attn_kernel, first_call=first_call, last_call=last_call,
                             groups=groups, reps=reps, hs=hs)
    state = [
        jax.ShapeDtypeStruct((groups, reps * t, 1), jnp.float32),
        jax.ShapeDtypeStruct((groups, reps * t, 1), jnp.float32),
        jax.ShapeDtypeStruct((groups, reps * t, hs), jnp.float32),
    ]
    state_specs = [
        pl.BlockSpec((groups, reps * t, 1), lambda j, f: (0, 0, 0)),
        pl.BlockSpec((groups, reps * t, 1), lambda j, f: (0, 0, 0)),
        pl.BlockSpec((groups, reps * t, hs), lambda j, f: (0, 0, 0)),
    ]
    if last_call:
        out_shape = jax.ShapeDtypeStruct((t, width), jnp.bfloat16)
        out_specs = pl.BlockSpec((t, width), lambda j, f: (0, 0))
    else:
        out_shape, out_specs = state, state_specs
    grid_spec = pltpu.PrefetchScalarGridSpec(
        num_scalar_prefetch=1,
        grid=(n_blocks,),
        in_specs=[
            pl.BlockSpec((t, width), lambda j, f: (0, 0)),
            pl.BlockSpec((t, KEY_BLOCK), lambda j, f: (0, j)),
            pl.BlockSpec((KEY_BLOCK, kv_rows.shape[1]), lambda j, f: (j, 0)),
        ] + state_specs,
        out_specs=out_specs,
        scratch_shapes=[
            pltpu.VMEM((groups, reps * t, hs), jnp.bfloat16),
            pltpu.VMEM((groups, reps * t, 1), jnp.float32),
            pltpu.VMEM((groups, reps * t, 1), jnp.float32),
            pltpu.VMEM((groups, reps * t, hs), jnp.float32),
            pltpu.VMEM((reps * t, KEY_BLOCK), jnp.float32),
            pltpu.VMEM((reps * t, KEY_BLOCK), jnp.bfloat16),
            pltpu.VMEM((reps * t, 1), jnp.float32),
        ],
    )
    if carry is None:
        carry = tuple(jnp.zeros(s.shape, s.dtype) for s in state)
    return pl.pallas_call(kern, grid_spec=grid_spec, out_shape=out_shape)(
        flags, queries, weights, kv_rows, *carry)


def on_device(
    hidden,
    queries,
    suffix_kv,
    lengths,
    page_table,
    page_pool,
    w_out,
    w_router,
    routes,
    w_gate,
    w_up,
    w_down,
):
    token_index = hidden.shape[0]
    row_width = KEY_VALUE_HEADS * HEAD_SIZE
    request_groups = QUERY_HEADS // KEY_VALUE_HEADS
    request_count = lax.axis_size("req")
    pool_per_shard = page_pool.shape[0]
    pool_all = pool_per_shard * request_count
    positions = lax.axis_index("exp") * token_index + jnp.arange(token_index, dtype=jnp.int32)
    lens = lengths[0]
    ends = jnp.cumsum(lens)
    starts = ends - lens
    req_of = jnp.sum((positions[:, None] >= ends[None, :]).astype(jnp.int32), axis=1)
    pick = req_of[:, None] == jnp.arange(lens.shape[0], dtype=jnp.int32)[None, :]
    first = jnp.sum(jnp.where(pick, starts[None, :], 0), axis=1)
    pool_rows = lax.all_gather(page_pool, "req", axis=0, tiled=True).reshape(
        pool_all * PAGE_TOKENS, 2 * row_width
    )
    pool_rows, suffix_after = lax.optimization_barrier((pool_rows, suffix_kv))
    segment = lax.all_gather(suffix_after, "exp", axis=0, tiled=True)
    counts = jnp.sum(
        (page_table[0][:, :, None] == jnp.arange(pool_all, dtype=jnp.int32)[None, None, :]).astype(
            jnp.float32
        ),
        axis=1,
    )
    query_counts = jnp.dot(pick.astype(jnp.float32), counts, precision=lax.Precision.HIGHEST)
    keypos = jnp.arange(segment.shape[0], dtype=jnp.int32)
    suffix_weights = (keypos[None, :] <= positions[:, None]) & (keypos[None, :] >= first[:, None])
    pool_bias = jnp.where(
        query_counts > 0, jnp.log2(jnp.maximum(query_counts, 1.0)), NEGATIVE_MASK
    )
    pool_weights = jnp.repeat(pool_bias, PAGE_TOKENS, axis=1)
    carry = flash(queries, pool_weights, pool_rows, None, True, False, KEY_VALUE_HEADS, HEAD_SIZE)
    attended = flash(
        queries,
        jnp.where(suffix_weights, 0.0, NEGATIVE_MASK).astype(jnp.float32),
        segment,
        carry,
        False,
        True,
        KEY_VALUE_HEADS,
        HEAD_SIZE,
    )
    projected = jnp.dot(attended, w_out, preferred_element_type=jnp.float32)
    resid = lax.optimization_barrier((hidden.astype(jnp.float32) + projected).astype(jnp.bfloat16))
    resid_f = resid.astype(jnp.float32)
    normed = (resid_f * lax.rsqrt(jnp.mean(resid_f * resid_f, axis=1, keepdims=True) + EPS)).astype(
        jnp.bfloat16
    )
    n_experts = w_router.shape[1]
    logits = jnp.dot(normed, w_router, preferred_element_type=jnp.float32)
    expert_ids = jnp.arange(n_experts, dtype=jnp.int32)
    chosen = jnp.sum(
        jnp.where(routes[:, :, None] == expert_ids[None, None, :], logits[:, None, :], 0.0), axis=2
    )
    gates = jax.nn.softmax(chosen, axis=1)
    capacity = 16
    member = routes[:, :, None] == expert_ids[None, None, :]
    picks = jnp.any(member, axis=1).astype(jnp.float32)
    gate_of = jnp.sum(jnp.where(member, gates[:, :, None], 0.0), axis=1)
    earlier = (
        jnp.arange(token_index, dtype=jnp.int32)[:, None]
        > jnp.arange(token_index, dtype=jnp.int32)[None, :]
    ).astype(jnp.float32)
    rank = jnp.dot(earlier, picks, precision=lax.Precision.HIGHEST).astype(jnp.int32)
    place = jnp.arange(capacity, dtype=jnp.int32)
    select = (picks[None, :, :] > 0) & (rank[None, :, :] == place[:, None, None])
    select = jnp.transpose(select, (2, 0, 1))
    select2 = jnp.broadcast_to(
        select[:, None], (n_experts, 2, capacity, token_index)
    ).reshape(2 * n_experts * capacity, token_index)
    weight = jnp.where(
        jnp.transpose(select, (2, 0, 1))[:, :, None, :],
        gate_of[:, :, None, None],
        0.0,
    )
    weight = jnp.broadcast_to(weight, (token_index, n_experts, 2, capacity))
    chunks = 2
    part = capacity // chunks
    select2 = select2.reshape(2 * n_experts, capacity, token_index)
    moe = resid_f
    for c in range(chunks):
        picked_rows = select2[:, c * part:(c + 1) * part].reshape(-1, token_index)
        outgoing = jnp.dot(
            picked_rows.astype(jnp.bfloat16), normed, preferred_element_type=jnp.float32
        ).astype(jnp.bfloat16)
        outgoing = outgoing.reshape(2 * n_experts, part, D)
        rows = lax.all_to_all(outgoing, ("req", "exp"), split_axis=0, concat_axis=0, tiled=True)
        flat_rows = rows.reshape(-1, D)
        gate_part = jnp.dot(flat_rows, w_gate[0], preferred_element_type=jnp.float32)
        up_part = jnp.dot(flat_rows, w_up[0], preferred_element_type=jnp.float32)
        inner = (jax.nn.silu(gate_part) * up_part).astype(jnp.bfloat16)
        returned = lax.all_to_all(
            jnp.dot(inner, w_down[0], preferred_element_type=jnp.float32)
            .astype(jnp.bfloat16)
            .reshape(rows.shape),
            ("req", "exp"),
            split_axis=0,
            concat_axis=0,
            tiled=True,
        ).reshape(-1, D)
        chunk_weight = weight[:, :, :, c * part:(c + 1) * part].reshape(token_index, -1)
        high = chunk_weight.astype(jnp.bfloat16)
        low = (chunk_weight - high.astype(jnp.float32)).astype(jnp.bfloat16)
        moe = (
            moe
            + jnp.dot(high, returned, preferred_element_type=jnp.float32)
            + jnp.dot(low, returned, preferred_element_type=jnp.float32)
        )
    return moe.astype(jnp.bfloat16)


def solution(mesh):
    placed = (
        P(("req", "exp"), None),
        P(("req", "exp"), None),
        P(("req", "exp"), None),
        P("req", None),
        P("req", None, None),
        P("req", None, None),
        P(),
        P(),
        P(("req", "exp"), None),
        P(("req", "exp"), None, None),
        P(("req", "exp"), None, None),
        P(("req", "exp"), None, None),
    )
    return jax.shard_map(
        on_device, mesh=mesh, in_specs=placed, out_specs=P(("req", "exp"), None), check_vma=False
    )
```

```python
import functools
import math

import jax
import jax.numpy as jnp
from jax import lax
from jax.experimental import pallas as pl
from jax.experimental.pallas import tpu as pltpu
from jax.sharding import PartitionSpec as P

D = 2560
QUERY_HEADS = 10
KEY_VALUE_HEADS = 2
HEAD_SIZE = 128
TOP = 6
PAGE_TOKENS = 128


NEGATIVE_MASK = -1e30
EPS = 1e-06


KEY_BLOCK = 512
LOG2_E = 1.4426950408889634


def attn_kernel(flags_ref, order_ref, q_ref, *refs, parts, first_call, last_call, groups, reps, hs):
    w_refs = refs[:parts]
    kv_refs = refs[parts:2 * parts]
    m_in, l_in, acc_in = refs[2 * parts:2 * parts + 3]
    refs = refs[2 * parts + 3:]
    if last_call:
        o_ref, qs, m_ref, l_ref, acc_ref = refs
    else:
        m_out, l_out, acc_out, qs, m_ref, l_ref, acc_ref = refs
    j = pl.program_id(0)
    t = q_ref.shape[0]
    key_block = sum(kv.shape[0] for kv in kv_refs)

    @pl.when(j == 0)
    def _():
        for g in range(groups):
            qs[g] = jnp.concatenate(
                [q_ref[:, (g * reps + h) * hs:(g * reps + h + 1) * hs] for h in range(reps)], axis=0)
        if first_call:
            m_ref[...] = jnp.full(m_ref.shape, NEGATIVE_MASK, jnp.float32)
            l_ref[...] = jnp.zeros(l_ref.shape, jnp.float32)
            acc_ref[...] = jnp.zeros(acc_ref.shape, jnp.float32)
        else:
            m_ref[...] = m_in[...]
            l_ref[...] = l_in[...]
            acc_ref[...] = acc_in[...]

    def joined(pieces, axis):
        return pieces[0] if len(pieces) == 1 else jnp.concatenate(pieces, axis=axis)

    @pl.when(flags_ref[j] > 0)
    def _():
        bias = joined([w[...] for w in w_refs], 1)[None]
        for g in range(groups):
            k = joined([kv[:, g * hs:(g + 1) * hs] for kv in kv_refs], 0)
            v = joined([kv[:, (groups + g) * hs:(groups + g + 1) * hs] for kv in kv_refs], 0)
            s = lax.dot_general(qs[g], k, (((1,), (1,)), ((), ())),
                                preferred_element_type=jnp.float32) * (LOG2_E / math.sqrt(hs))
            s = s.reshape(reps, t, key_block) + bias
            m_old = m_ref[g].reshape(reps, t, 1)
            m_new = jnp.maximum(m_old, jnp.max(s, axis=-1, keepdims=True))
            p = jnp.exp2(s - m_new)
            alpha = jnp.exp2(m_old - m_new)
            l_ref[g] = (alpha * l_ref[g].reshape(reps, t, 1) + jnp.sum(p, axis=-1, keepdims=True)).reshape(reps * t, 1)
            pv = jnp.dot(p.reshape(reps * t, key_block).astype(jnp.bfloat16), v, preferred_element_type=jnp.float32)
            acc_ref[g] = alpha.reshape(reps * t, 1) * acc_ref[g] + pv
            m_ref[g] = m_new.reshape(reps * t, 1)

    @pl.when(j == pl.num_programs(0) - 1)
    def _():
        if last_call:
            for g in range(groups):
                for h in range(reps):
                    rows = slice(h * t, (h + 1) * t)
                    o_ref[:, (g * reps + h) * hs:(g * reps + h + 1) * hs] = (
                        acc_ref[g, rows, :] / l_ref[g, rows, :]).astype(o_ref.dtype)
        else:
            m_out[...] = m_ref[...]
            l_out[...] = l_ref[...]
            acc_out[...] = acc_ref[...]


def flash(queries, bias, kv_rows, carry, first_call, last_call, groups, hs, order=None, parts=1):
    t, width = queries.shape
    reps = width // hs // groups
    if order is None:
        block = KEY_BLOCK
        n_blocks = kv_rows.shape[0] // block
        flags = (
            jnp.max(bias.reshape(t, n_blocks, block), axis=(0, 2)) > 0.5 * NEGATIVE_MASK
        ).astype(jnp.int32)
        order = jnp.zeros((1,), jnp.int32)
        w_specs = [pl.BlockSpec((t, block), lambda j, f, o: (0, j))]
        kv_specs = [pl.BlockSpec((block, kv_rows.shape[1]), lambda j, f, o: (j, 0))]
    else:
        order, live_count = order
        block = kv_rows.shape[0] // order.shape[0]
        n_blocks = order.shape[0] // parts
        flags = (jnp.arange(n_blocks, dtype=jnp.int32) * parts < live_count).astype(jnp.int32)
        w_specs = [
            pl.BlockSpec((t, block), lambda j, f, o, i=i: (0, o[parts * j + i])) for i in range(parts)
        ]
        kv_specs = [
            pl.BlockSpec((block, kv_rows.shape[1]), lambda j, f, o, i=i: (o[parts * j + i], 0))
            for i in range(parts)
        ]
    kern = functools.partial(attn_kernel, parts=len(w_specs), first_call=first_call,
                             last_call=last_call, groups=groups, reps=reps, hs=hs)
    state = [
        jax.ShapeDtypeStruct((groups, reps * t, 1), jnp.float32),
        jax.ShapeDtypeStruct((groups, reps * t, 1), jnp.float32),
        jax.ShapeDtypeStruct((groups, reps * t, hs), jnp.float32),
    ]
    state_specs = [
        pl.BlockSpec((groups, reps * t, 1), lambda j, f, o: (0, 0, 0)),
        pl.BlockSpec((groups, reps * t, 1), lambda j, f, o: (0, 0, 0)),
        pl.BlockSpec((groups, reps * t, hs), lambda j, f, o: (0, 0, 0)),
    ]
    if last_call:
        out_shape = jax.ShapeDtypeStruct((t, width), jnp.bfloat16)
        out_specs = pl.BlockSpec((t, width), lambda j, f, o: (0, 0))
    else:
        out_shape, out_specs = state, state_specs
    grid_spec = pltpu.PrefetchScalarGridSpec(
        num_scalar_prefetch=2,
        grid=(n_blocks,),
        in_specs=[pl.BlockSpec((t, width), lambda j, f, o: (0, 0))] + w_specs + kv_specs + state_specs,
        out_specs=out_specs,
        scratch_shapes=[
            pltpu.VMEM((groups, reps * t, hs), jnp.bfloat16),
            pltpu.VMEM((groups, reps * t, 1), jnp.float32),
            pltpu.VMEM((groups, reps * t, 1), jnp.float32),
            pltpu.VMEM((groups, reps * t, hs), jnp.float32),
        ],
    )
    if carry is None:
        carry = tuple(jnp.zeros(s.shape, s.dtype) for s in state)
    operands = [queries] + [bias] * len(w_specs) + [kv_rows] * len(kv_specs) + list(carry)
    return pl.pallas_call(kern, grid_spec=grid_spec, out_shape=out_shape)(flags, order, *operands)


def on_device(
    hidden,
    queries,
    suffix_kv,
    lengths,
    page_table,
    page_pool,
    w_out,
    w_router,
    routes,
    w_gate,
    w_up,
    w_down,
):
    token_index = hidden.shape[0]
    row_width = KEY_VALUE_HEADS * HEAD_SIZE
    request_groups = QUERY_HEADS // KEY_VALUE_HEADS
    request_count = lax.axis_size("req")
    pool_per_shard = page_pool.shape[0]
    pool_all = pool_per_shard * request_count
    positions = lax.axis_index("exp") * token_index + jnp.arange(token_index, dtype=jnp.int32)
    lens = lengths[0]
    ends = jnp.cumsum(lens)
    starts = ends - lens
    req_of = jnp.sum((positions[:, None] >= ends[None, :]).astype(jnp.int32), axis=1)
    pick = req_of[:, None] == jnp.arange(lens.shape[0], dtype=jnp.int32)[None, :]
    first = jnp.sum(jnp.where(pick, starts[None, :], 0), axis=1)
    pool_rows = lax.all_gather(page_pool, "req", axis=0, tiled=True).reshape(
        pool_all * PAGE_TOKENS, 2 * row_width
    )
    pool_rows, suffix_after = lax.optimization_barrier((pool_rows, suffix_kv))
    segment = lax.all_gather(suffix_after, "exp", axis=0, tiled=True)
    counts = jnp.sum(
        (page_table[0][:, :, None] == jnp.arange(pool_all, dtype=jnp.int32)[None, None, :]).astype(
            jnp.float32
        ),
        axis=1,
    )
    query_counts = jnp.dot(pick.astype(jnp.float32), counts, precision=lax.Precision.HIGHEST)
    keypos = jnp.arange(segment.shape[0], dtype=jnp.int32)
    suffix_weights = (keypos[None, :] <= positions[:, None]) & (keypos[None, :] >= first[:, None])
    pool_bias = jnp.where(
        query_counts > 0, jnp.log2(jnp.maximum(query_counts, 1.0)), NEGATIVE_MASK
    )
    pool_weights = jnp.repeat(pool_bias, PAGE_TOKENS, axis=1)
    live = jnp.max(query_counts, axis=0) > 0
    live_int = live.astype(jnp.int32)
    live_count = jnp.sum(live_int)
    destination = jnp.where(
        live, jnp.cumsum(live_int) - 1, live_count + jnp.cumsum(1 - live_int) - 1
    )
    slots = jnp.arange(pool_all, dtype=jnp.int32)
    order = jnp.sum(
        jnp.where(destination[None, :] == slots[:, None], slots[None, :], 0), axis=1
    ).astype(jnp.int32)
    carry = flash(
        queries,
        pool_weights,
        pool_rows,
        None,
        True,
        False,
        KEY_VALUE_HEADS,
        HEAD_SIZE,
        (order, live_count),
        KEY_BLOCK // PAGE_TOKENS,
    )
    attended = flash(
        queries,
        jnp.where(suffix_weights, 0.0, NEGATIVE_MASK).astype(jnp.float32),
        segment,
        carry,
        False,
        True,
        KEY_VALUE_HEADS,
        HEAD_SIZE,
    )
    projected = jnp.dot(attended, w_out, preferred_element_type=jnp.float32)
    resid = lax.optimization_barrier((hidden.astype(jnp.float32) + projected).astype(jnp.bfloat16))
    resid_f = resid.astype(jnp.float32)
    normed = (resid_f * lax.rsqrt(jnp.mean(resid_f * resid_f, axis=1, keepdims=True) + EPS)).astype(
        jnp.bfloat16
    )
    n_experts = w_router.shape[1]
    logits = jnp.dot(normed, w_router, preferred_element_type=jnp.float32)
    expert_ids = jnp.arange(n_experts, dtype=jnp.int32)
    chosen = jnp.sum(
        jnp.where(routes[:, :, None] == expert_ids[None, None, :], logits[:, None, :], 0.0), axis=2
    )
    gates = jax.nn.softmax(chosen, axis=1)
    capacity = 16
    member = routes[:, :, None] == expert_ids[None, None, :]
    picks = jnp.any(member, axis=1).astype(jnp.float32)
    gate_of = jnp.sum(jnp.where(member, gates[:, :, None], 0.0), axis=1)
    earlier = (
        jnp.arange(token_index, dtype=jnp.int32)[:, None]
        > jnp.arange(token_index, dtype=jnp.int32)[None, :]
    ).astype(jnp.float32)
    rank = jnp.dot(earlier, picks, precision=lax.Precision.HIGHEST).astype(jnp.int32)
    place = jnp.arange(capacity, dtype=jnp.int32)
    select = (picks[None, :, :] > 0) & (rank[None, :, :] == place[:, None, None])
    select = jnp.transpose(select, (2, 0, 1))
    select2 = jnp.broadcast_to(
        select[:, None], (n_experts, 2, capacity, token_index)
    ).reshape(2 * n_experts * capacity, token_index)
    weight = jnp.where(
        jnp.transpose(select, (2, 0, 1))[:, :, None, :],
        gate_of[:, :, None, None],
        0.0,
    )
    weight = jnp.broadcast_to(weight, (token_index, n_experts, 2, capacity))
    chunks = 2
    part = capacity // chunks
    select2 = select2.reshape(2 * n_experts, capacity, token_index)
    moe = resid_f
    for c in range(chunks):
        picked_rows = select2[:, c * part:(c + 1) * part].reshape(-1, token_index)
        outgoing = jnp.dot(
            picked_rows.astype(jnp.bfloat16), normed, preferred_element_type=jnp.float32
        ).astype(jnp.bfloat16)
        outgoing = outgoing.reshape(2 * n_experts, part, D)
        rows = lax.all_to_all(outgoing, ("req", "exp"), split_axis=0, concat_axis=0, tiled=True)
        flat_rows = rows.reshape(-1, D)
        gate_part = jnp.dot(flat_rows, w_gate[0], preferred_element_type=jnp.float32)
        up_part = jnp.dot(flat_rows, w_up[0], preferred_element_type=jnp.float32)
        inner = (jax.nn.silu(gate_part) * up_part).astype(jnp.bfloat16)
        returned = lax.all_to_all(
            jnp.dot(inner, w_down[0], preferred_element_type=jnp.float32)
            .astype(jnp.bfloat16)
            .reshape(rows.shape),
            ("req", "exp"),
            split_axis=0,
            concat_axis=0,
            tiled=True,
        ).reshape(-1, D)
        chunk_weight = weight[:, :, :, c * part:(c + 1) * part].reshape(token_index, -1)
        high = chunk_weight.astype(jnp.bfloat16)
        low = (chunk_weight - high.astype(jnp.float32)).astype(jnp.bfloat16)
        moe = (
            moe
            + jnp.dot(high, returned, preferred_element_type=jnp.float32)
            + jnp.dot(low, returned, preferred_element_type=jnp.float32)
        )
    return moe.astype(jnp.bfloat16)


def solution(mesh):
    placed = (
        P(("req", "exp"), None),
        P(("req", "exp"), None),
        P(("req", "exp"), None),
        P("req", None),
        P("req", None, None),
        P("req", None, None),
        P(),
        P(),
        P(("req", "exp"), None),
        P(("req", "exp"), None, None),
        P(("req", "exp"), None, None),
        P(("req", "exp"), None, None),
    )
    return jax.shard_map(
        on_device, mesh=mesh, in_specs=placed, out_specs=P(("req", "exp"), None), check_vma=False
    )
```

```python
import functools
import math

import jax
import jax.numpy as jnp
from jax import lax
from jax.experimental import pallas as pl
from jax.experimental.pallas import tpu as pltpu
from jax.sharding import PartitionSpec as P

D = 2560
QUERY_HEADS = 10
KEY_VALUE_HEADS = 2
HEAD_SIZE = 128
TOP = 6
PAGE_TOKENS = 128


NEGATIVE_MASK = -1e30
EPS = 1e-06


KEY_BLOCK = 512
LOG2_E = 1.4426950408889634


def attn_kernel(flags_ref, order_ref, q_ref, *refs, parts, first_call, last_call, groups, reps, hs):
    w_refs = refs[:parts]
    kv_refs = refs[parts:2 * parts]
    carried = 0 if first_call else 3
    if not first_call:
        m_in, l_in, acc_in = refs[2 * parts:2 * parts + 3]
    refs = refs[2 * parts + carried:]
    if last_call:
        o_ref, qs, m_ref, l_ref, acc_ref = refs
    else:
        m_out, l_out, acc_out, qs, m_ref, l_ref, acc_ref = refs
    j = pl.program_id(0)
    t = q_ref.shape[0]
    key_block = sum(kv.shape[0] for kv in kv_refs)

    @pl.when(j == 0)
    def _():
        for g in range(groups):
            qs[g] = jnp.concatenate(
                [q_ref[:, (g * reps + h) * hs:(g * reps + h + 1) * hs] for h in range(reps)], axis=0)
        if first_call:
            m_ref[...] = jnp.full(m_ref.shape, NEGATIVE_MASK, jnp.float32)
            l_ref[...] = jnp.zeros(l_ref.shape, jnp.float32)
            acc_ref[...] = jnp.zeros(acc_ref.shape, jnp.float32)
        else:
            m_ref[...] = m_in[...]
            l_ref[...] = l_in[...]
            acc_ref[...] = acc_in[...]

    def joined(pieces, axis):
        return pieces[0] if len(pieces) == 1 else jnp.concatenate(pieces, axis=axis)

    @pl.when(flags_ref[j] > 0)
    def _():
        bias = joined([w[...] for w in w_refs], 1)[None]
        for g in range(groups):
            k = joined([kv[:, g * hs:(g + 1) * hs] for kv in kv_refs], 0)
            v = joined([kv[:, (groups + g) * hs:(groups + g + 1) * hs] for kv in kv_refs], 0)
            s = lax.dot_general(qs[g], k, (((1,), (1,)), ((), ())),
                                preferred_element_type=jnp.float32) * (LOG2_E / math.sqrt(hs))
            s = s.reshape(reps, t, key_block) + bias
            m_old = m_ref[g].reshape(reps, t, 1)
            m_new = jnp.maximum(m_old, jnp.max(s, axis=-1, keepdims=True))
            p = jnp.exp2(s - m_new)
            alpha = jnp.exp2(m_old - m_new)
            l_ref[g] = (alpha * l_ref[g].reshape(reps, t, 1) + jnp.sum(p, axis=-1, keepdims=True)).reshape(reps * t, 1)
            pv = jnp.dot(p.reshape(reps * t, key_block).astype(jnp.bfloat16), v, preferred_element_type=jnp.float32)
            acc_ref[g] = alpha.reshape(reps * t, 1) * acc_ref[g] + pv
            m_ref[g] = m_new.reshape(reps * t, 1)

    @pl.when(j == pl.num_programs(0) - 1)
    def _():
        if last_call:
            for g in range(groups):
                for h in range(reps):
                    rows = slice(h * t, (h + 1) * t)
                    o_ref[:, (g * reps + h) * hs:(g * reps + h + 1) * hs] = (
                        acc_ref[g, rows, :] / l_ref[g, rows, :]).astype(o_ref.dtype)
        else:
            m_out[...] = m_ref[...]
            l_out[...] = l_ref[...]
            acc_out[...] = acc_ref[...]


def flash(queries, bias, kv_rows, carry, first_call, last_call, groups, hs, order=None, parts=1):
    t, width = queries.shape
    reps = width // hs // groups
    if order is None:
        block = KEY_BLOCK
        n_blocks = kv_rows.shape[0] // block
        flags = (
            jnp.max(bias.reshape(t, n_blocks, block), axis=(0, 2)) > 0.5 * NEGATIVE_MASK
        ).astype(jnp.int32)
        order = jnp.zeros((1,), jnp.int32)
        w_specs = [pl.BlockSpec((t, block), lambda j, f, o: (0, j))]
        kv_specs = [pl.BlockSpec((block, kv_rows.shape[1]), lambda j, f, o: (j, 0))]
    else:
        order, live_count = order
        block = kv_rows.shape[0] // order.shape[0]
        n_blocks = order.shape[0] // parts
        flags = (jnp.arange(n_blocks, dtype=jnp.int32) * parts < live_count).astype(jnp.int32)
        w_specs = [
            pl.BlockSpec((t, block), lambda j, f, o, i=i: (0, o[parts * j + i])) for i in range(parts)
        ]
        kv_specs = [
            pl.BlockSpec((block, kv_rows.shape[1]), lambda j, f, o, i=i: (o[parts * j + i], 0))
            for i in range(parts)
        ]
    kern = functools.partial(attn_kernel, parts=len(w_specs), first_call=first_call,
                             last_call=last_call, groups=groups, reps=reps, hs=hs)
    state = [
        jax.ShapeDtypeStruct((groups, reps * t, 1), jnp.float32),
        jax.ShapeDtypeStruct((groups, reps * t, 1), jnp.float32),
        jax.ShapeDtypeStruct((groups, reps * t, hs), jnp.float32),
    ]
    state_specs = [
        pl.BlockSpec((groups, reps * t, 1), lambda j, f, o: (0, 0, 0)),
        pl.BlockSpec((groups, reps * t, 1), lambda j, f, o: (0, 0, 0)),
        pl.BlockSpec((groups, reps * t, hs), lambda j, f, o: (0, 0, 0)),
    ]
    if last_call:
        out_shape = jax.ShapeDtypeStruct((t, width), jnp.bfloat16)
        out_specs = pl.BlockSpec((t, width), lambda j, f, o: (0, 0))
    else:
        out_shape, out_specs = state, state_specs
    grid_spec = pltpu.PrefetchScalarGridSpec(
        num_scalar_prefetch=2,
        grid=(n_blocks,),
        in_specs=[pl.BlockSpec((t, width), lambda j, f, o: (0, 0))]
        + w_specs
        + kv_specs
        + ([] if first_call else state_specs),
        out_specs=out_specs,
        scratch_shapes=[
            pltpu.VMEM((groups, reps * t, hs), jnp.bfloat16),
            pltpu.VMEM((groups, reps * t, 1), jnp.float32),
            pltpu.VMEM((groups, reps * t, 1), jnp.float32),
            pltpu.VMEM((groups, reps * t, hs), jnp.float32),
        ],
    )
    operands = [queries] + [bias] * len(w_specs) + [kv_rows] * len(kv_specs)
    if not first_call:
        operands += list(carry)
    return pl.pallas_call(kern, grid_spec=grid_spec, out_shape=out_shape)(flags, order, *operands)


def on_device(
    hidden,
    queries,
    suffix_kv,
    lengths,
    page_table,
    page_pool,
    w_out,
    w_router,
    routes,
    w_gate,
    w_up,
    w_down,
):
    token_index = hidden.shape[0]
    row_width = KEY_VALUE_HEADS * HEAD_SIZE
    request_groups = QUERY_HEADS // KEY_VALUE_HEADS
    request_count = lax.axis_size("req")
    pool_per_shard = page_pool.shape[0]
    pool_all = pool_per_shard * request_count
    positions = lax.axis_index("exp") * token_index + jnp.arange(token_index, dtype=jnp.int32)
    lens = lengths[0]
    ends = jnp.cumsum(lens)
    starts = ends - lens
    req_of = jnp.sum((positions[:, None] >= ends[None, :]).astype(jnp.int32), axis=1)
    pick = req_of[:, None] == jnp.arange(lens.shape[0], dtype=jnp.int32)[None, :]
    first = jnp.sum(jnp.where(pick, starts[None, :], 0), axis=1)
    pool_rows = lax.all_gather(page_pool, "req", axis=0, tiled=True).reshape(
        pool_all * PAGE_TOKENS, 2 * row_width
    )
    pool_rows, suffix_after = lax.optimization_barrier((pool_rows, suffix_kv))
    segment = lax.all_gather(suffix_after, "exp", axis=0, tiled=True)
    counts = jnp.sum(
        (page_table[0][:, :, None] == jnp.arange(pool_all, dtype=jnp.int32)[None, None, :]).astype(
            jnp.float32
        ),
        axis=1,
    )
    query_counts = jnp.dot(pick.astype(jnp.float32), counts, precision=lax.Precision.HIGHEST)
    keypos = jnp.arange(segment.shape[0], dtype=jnp.int32)
    suffix_weights = (keypos[None, :] <= positions[:, None]) & (keypos[None, :] >= first[:, None])
    spread = (
        jnp.arange(pool_all, dtype=jnp.int32)[:, None]
        == jnp.arange(pool_all * PAGE_TOKENS, dtype=jnp.int32)[None, :] // PAGE_TOKENS
    ).astype(jnp.bfloat16)
    key_counts = jnp.dot(
        query_counts.astype(jnp.bfloat16), spread, preferred_element_type=jnp.float32
    )
    pool_weights = jnp.where(
        key_counts > 0, jnp.log2(jnp.maximum(key_counts, 1.0)), NEGATIVE_MASK
    )
    live = jnp.max(query_counts, axis=0) > 0
    live_int = live.astype(jnp.int32)
    live_count = jnp.sum(live_int)
    destination = jnp.where(
        live, jnp.cumsum(live_int) - 1, live_count + jnp.cumsum(1 - live_int) - 1
    )
    slots = jnp.arange(pool_all, dtype=jnp.int32)
    order = jnp.sum(
        jnp.where(destination[None, :] == slots[:, None], slots[None, :], 0), axis=1
    ).astype(jnp.int32)
    carry = flash(
        queries,
        pool_weights,
        pool_rows,
        None,
        True,
        False,
        KEY_VALUE_HEADS,
        HEAD_SIZE,
        (order, live_count),
        KEY_BLOCK // PAGE_TOKENS,
    )
    attended = flash(
        queries,
        jnp.where(suffix_weights, 0.0, NEGATIVE_MASK).astype(jnp.float32),
        segment,
        carry,
        False,
        True,
        KEY_VALUE_HEADS,
        HEAD_SIZE,
    )
    projected = jnp.dot(attended, w_out, preferred_element_type=jnp.float32)
    resid = lax.optimization_barrier((hidden.astype(jnp.float32) + projected).astype(jnp.bfloat16))
    resid_f = resid.astype(jnp.float32)
    normed = (resid_f * lax.rsqrt(jnp.mean(resid_f * resid_f, axis=1, keepdims=True) + EPS)).astype(
        jnp.bfloat16
    )
    n_experts = w_router.shape[1]
    logits = jnp.dot(normed, w_router, preferred_element_type=jnp.float32)
    expert_ids = jnp.arange(n_experts, dtype=jnp.int32)
    chosen = jnp.sum(
        jnp.where(routes[:, :, None] == expert_ids[None, None, :], logits[:, None, :], 0.0), axis=2
    )
    gates = jax.nn.softmax(chosen, axis=1)
    capacity = 16
    member = routes[:, :, None] == expert_ids[None, None, :]
    picks = jnp.any(member, axis=1).astype(jnp.float32)
    gate_of = jnp.sum(jnp.where(member, gates[:, :, None], 0.0), axis=1)
    earlier = (
        jnp.arange(token_index, dtype=jnp.int32)[:, None]
        > jnp.arange(token_index, dtype=jnp.int32)[None, :]
    ).astype(jnp.float32)
    rank = jnp.dot(earlier, picks, precision=lax.Precision.HIGHEST).astype(jnp.int32)
    place = jnp.arange(capacity, dtype=jnp.int32)
    select = (picks[None, :, :] > 0) & (rank[None, :, :] == place[:, None, None])
    select = jnp.transpose(select, (2, 0, 1))
    select2 = jnp.broadcast_to(
        select[:, None], (n_experts, 2, capacity, token_index)
    ).reshape(2 * n_experts * capacity, token_index)
    weight = jnp.where(
        jnp.transpose(select, (2, 0, 1))[:, :, None, :],
        gate_of[:, :, None, None],
        0.0,
    )
    weight = jnp.broadcast_to(weight, (token_index, n_experts, 2, capacity))
    chunks = 2
    part = capacity // chunks
    select2 = select2.reshape(2 * n_experts, capacity, token_index)
    moe = resid_f
    for c in range(chunks):
        picked_rows = select2[:, c * part:(c + 1) * part].reshape(-1, token_index)
        outgoing = jnp.dot(
            picked_rows.astype(jnp.bfloat16), normed, preferred_element_type=jnp.float32
        ).astype(jnp.bfloat16)
        outgoing = outgoing.reshape(2 * n_experts, part, D)
        rows = lax.all_to_all(outgoing, ("req", "exp"), split_axis=0, concat_axis=0, tiled=True)
        flat_rows = rows.reshape(-1, D)
        gate_part = jnp.dot(flat_rows, w_gate[0], preferred_element_type=jnp.float32)
        up_part = jnp.dot(flat_rows, w_up[0], preferred_element_type=jnp.float32)
        inner = (jax.nn.silu(gate_part) * up_part).astype(jnp.bfloat16)
        returned = lax.all_to_all(
            jnp.dot(inner, w_down[0], preferred_element_type=jnp.float32)
            .astype(jnp.bfloat16)
            .reshape(rows.shape),
            ("req", "exp"),
            split_axis=0,
            concat_axis=0,
            tiled=True,
        ).reshape(-1, D)
        chunk_weight = weight[:, :, :, c * part:(c + 1) * part].reshape(token_index, -1)
        high = chunk_weight.astype(jnp.bfloat16)
        low = (chunk_weight - high.astype(jnp.float32)).astype(jnp.bfloat16)
        moe = (
            moe
            + jnp.dot(high, returned, preferred_element_type=jnp.float32)
            + jnp.dot(low, returned, preferred_element_type=jnp.float32)
        )
    return moe.astype(jnp.bfloat16)


def solution(mesh):
    placed = (
        P(("req", "exp"), None),
        P(("req", "exp"), None),
        P(("req", "exp"), None),
        P("req", None),
        P("req", None, None),
        P("req", None, None),
        P(),
        P(),
        P(("req", "exp"), None),
        P(("req", "exp"), None, None),
        P(("req", "exp"), None, None),
        P(("req", "exp"), None, None),
    )
    return jax.shard_map(
        on_device, mesh=mesh, in_specs=placed, out_specs=P(("req", "exp"), None), check_vma=False
    )
```

```python
import functools
import math

import jax
import jax.numpy as jnp
from jax import lax
from jax.experimental import pallas as pl
from jax.experimental.pallas import tpu as pltpu
from jax.sharding import PartitionSpec as P

D = 2560
QUERY_HEADS = 10
KEY_VALUE_HEADS = 2
HEAD_SIZE = 128
TOP = 6
PAGE_TOKENS = 128


NEGATIVE_MASK = -1e30
EPS = 1e-06


KEY_BLOCK = 512
LOG2_E = 1.4426950408889634


def attn_kernel(flags_ref, order_ref, q_ref, *refs, parts, first_call, last_call, groups, reps, hs):
    w_refs = refs[:parts]
    kv_refs = refs[parts:2 * parts]
    carried = 0 if first_call else 3
    if not first_call:
        m_in, l_in, acc_in = refs[2 * parts:2 * parts + 3]
    refs = refs[2 * parts + carried:]
    if last_call:
        o_ref, qs, m_ref, l_ref, acc_ref = refs
    else:
        m_out, l_out, acc_out, qs, m_ref, l_ref, acc_ref = refs
    j = pl.program_id(0)
    t = q_ref.shape[0]
    key_block = sum(kv.shape[0] for kv in kv_refs)

    @pl.when(j == 0)
    def _():
        for g in range(groups):
            qs[g] = jnp.concatenate(
                [q_ref[:, (g * reps + h) * hs:(g * reps + h + 1) * hs] for h in range(reps)], axis=0)
        if first_call:
            m_ref[...] = jnp.full(m_ref.shape, NEGATIVE_MASK, jnp.float32)
            l_ref[...] = jnp.zeros(l_ref.shape, jnp.float32)
            acc_ref[...] = jnp.zeros(acc_ref.shape, jnp.float32)
        else:
            m_ref[...] = m_in[...]
            l_ref[...] = l_in[...]
            acc_ref[...] = acc_in[...]

    def joined(pieces, axis):
        return pieces[0] if len(pieces) == 1 else jnp.concatenate(pieces, axis=axis)

    @pl.when(flags_ref[j] > 0)
    def _():
        bias = joined([w[...] for w in w_refs], 1)[None]
        for g in range(groups):
            k = joined([kv[:, g * hs:(g + 1) * hs] for kv in kv_refs], 0)
            v = joined([kv[:, (groups + g) * hs:(groups + g + 1) * hs] for kv in kv_refs], 0)
            s = lax.dot_general(qs[g], k, (((1,), (1,)), ((), ())),
                                preferred_element_type=jnp.float32) * (LOG2_E / math.sqrt(hs))
            s = s.reshape(reps, t, key_block) + bias
            m_old = m_ref[g].reshape(reps, t, 1)
            m_new = jnp.maximum(m_old, jnp.max(s, axis=-1, keepdims=True))
            p = jnp.exp2(s - m_new)
            alpha = jnp.exp2(m_old - m_new)
            l_ref[g] = (alpha * l_ref[g].reshape(reps, t, 1) + jnp.sum(p, axis=-1, keepdims=True)).reshape(reps * t, 1)
            pv = jnp.dot(p.reshape(reps * t, key_block).astype(jnp.bfloat16), v, preferred_element_type=jnp.float32)
            acc_ref[g] = alpha.reshape(reps * t, 1) * acc_ref[g] + pv
            m_ref[g] = m_new.reshape(reps * t, 1)

    @pl.when(j == pl.num_programs(0) - 1)
    def _():
        if last_call:
            for g in range(groups):
                for h in range(reps):
                    rows = slice(h * t, (h + 1) * t)
                    o_ref[:, (g * reps + h) * hs:(g * reps + h + 1) * hs] = (
                        acc_ref[g, rows, :] / l_ref[g, rows, :]).astype(o_ref.dtype)
        else:
            m_out[...] = m_ref[...]
            l_out[...] = l_ref[...]
            acc_out[...] = acc_ref[...]


def flash(queries, bias, kv_rows, carry, first_call, last_call, groups, hs, order=None, parts=1):
    t, width = queries.shape
    reps = width // hs // groups
    if order is None:
        block = KEY_BLOCK
        n_blocks = kv_rows.shape[0] // block
        flags = (
            jnp.max(bias.reshape(t, n_blocks, block), axis=(0, 2)) > 0.5 * NEGATIVE_MASK
        ).astype(jnp.int32)
        order = jnp.zeros((1,), jnp.int32)
        w_specs = [pl.BlockSpec((t, block), lambda j, f, o: (0, j))]
        kv_specs = [pl.BlockSpec((block, kv_rows.shape[1]), lambda j, f, o: (j, 0))]
    else:
        order, live_count = order
        block = kv_rows.shape[0] // order.shape[0]
        n_blocks = order.shape[0] // parts
        flags = (jnp.arange(n_blocks, dtype=jnp.int32) * parts < live_count).astype(jnp.int32)
        w_specs = [
            pl.BlockSpec((t, block), lambda j, f, o, i=i: (0, o[parts * j + i])) for i in range(parts)
        ]
        kv_specs = [
            pl.BlockSpec((block, kv_rows.shape[1]), lambda j, f, o, i=i: (o[parts * j + i], 0))
            for i in range(parts)
        ]
    kern = functools.partial(attn_kernel, parts=len(w_specs), first_call=first_call,
                             last_call=last_call, groups=groups, reps=reps, hs=hs)
    state = [
        jax.ShapeDtypeStruct((groups, reps * t, 1), jnp.float32),
        jax.ShapeDtypeStruct((groups, reps * t, 1), jnp.float32),
        jax.ShapeDtypeStruct((groups, reps * t, hs), jnp.float32),
    ]
    state_specs = [
        pl.BlockSpec((groups, reps * t, 1), lambda j, f, o: (0, 0, 0)),
        pl.BlockSpec((groups, reps * t, 1), lambda j, f, o: (0, 0, 0)),
        pl.BlockSpec((groups, reps * t, hs), lambda j, f, o: (0, 0, 0)),
    ]
    if last_call:
        out_shape = jax.ShapeDtypeStruct((t, width), jnp.bfloat16)
        out_specs = pl.BlockSpec((t, width), lambda j, f, o: (0, 0))
    else:
        out_shape, out_specs = state, state_specs
    grid_spec = pltpu.PrefetchScalarGridSpec(
        num_scalar_prefetch=2,
        grid=(n_blocks,),
        in_specs=[pl.BlockSpec((t, width), lambda j, f, o: (0, 0))]
        + w_specs
        + kv_specs
        + ([] if first_call else state_specs),
        out_specs=out_specs,
        scratch_shapes=[
            pltpu.VMEM((groups, reps * t, hs), jnp.bfloat16),
            pltpu.VMEM((groups, reps * t, 1), jnp.float32),
            pltpu.VMEM((groups, reps * t, 1), jnp.float32),
            pltpu.VMEM((groups, reps * t, hs), jnp.float32),
        ],
    )
    operands = [queries] + [bias] * len(w_specs) + [kv_rows] * len(kv_specs)
    if not first_call:
        operands += list(carry)
    return pl.pallas_call(kern, grid_spec=grid_spec, out_shape=out_shape)(flags, order, *operands)


def on_device(
    hidden,
    queries,
    suffix_kv,
    lengths,
    page_table,
    page_pool,
    w_out,
    w_router,
    routes,
    w_gate,
    w_up,
    w_down,
):
    token_index = hidden.shape[0]
    row_width = KEY_VALUE_HEADS * HEAD_SIZE
    request_groups = QUERY_HEADS // KEY_VALUE_HEADS
    request_count = lax.axis_size("req")
    pool_per_shard = page_pool.shape[0]
    pool_all = pool_per_shard * request_count
    positions = lax.axis_index("exp") * token_index + jnp.arange(token_index, dtype=jnp.int32)
    lens = lengths[0]
    ends = jnp.cumsum(lens)
    starts = ends - lens
    req_of = jnp.sum((positions[:, None] >= ends[None, :]).astype(jnp.int32), axis=1)
    pick = req_of[:, None] == jnp.arange(lens.shape[0], dtype=jnp.int32)[None, :]
    first = jnp.sum(jnp.where(pick, starts[None, :], 0), axis=1)
    split = (pool_per_shard + 1) // 2
    pool_first = lax.all_gather(page_pool[:split], "req", axis=0, tiled=True)
    pool_first, pool_later, suffix_after = lax.optimization_barrier(
        (pool_first, page_pool[split:], suffix_kv)
    )
    pool_second = lax.all_gather(pool_later, "req", axis=0, tiled=True)
    segment = lax.all_gather(suffix_after, "exp", axis=0, tiled=True)
    counts = jnp.sum(
        (page_table[0][:, :, None] == jnp.arange(pool_all, dtype=jnp.int32)[None, None, :]).astype(
            jnp.float32
        ),
        axis=1,
    )
    query_counts = jnp.dot(pick.astype(jnp.float32), counts, precision=lax.Precision.HIGHEST)
    keypos = jnp.arange(segment.shape[0], dtype=jnp.int32)
    suffix_weights = (keypos[None, :] <= positions[:, None]) & (keypos[None, :] >= first[:, None])
    shard_counts = query_counts.reshape(token_index, request_count, pool_per_shard)
    carry = None
    for part_counts, rows in (
        (shard_counts[:, :, :split], pool_first),
        (shard_counts[:, :, split:], pool_second),
    ):
        part_counts = part_counts.reshape(token_index, -1)
        pages = part_counts.shape[1]
        spread = (
            jnp.arange(pages, dtype=jnp.int32)[:, None]
            == jnp.arange(pages * PAGE_TOKENS, dtype=jnp.int32)[None, :] // PAGE_TOKENS
        ).astype(jnp.bfloat16)
        key_counts = jnp.dot(
            part_counts.astype(jnp.bfloat16), spread, preferred_element_type=jnp.float32
        )
        part_bias = jnp.where(
            key_counts > 0, jnp.log2(jnp.maximum(key_counts, 1.0)), NEGATIVE_MASK
        )
        live = jnp.max(part_counts, axis=0) > 0
        live_int = live.astype(jnp.int32)
        live_count = jnp.sum(live_int)
        destination = jnp.where(
            live, jnp.cumsum(live_int) - 1, live_count + jnp.cumsum(1 - live_int) - 1
        )
        slots = jnp.arange(pages, dtype=jnp.int32)
        order = jnp.sum(
            jnp.where(destination[None, :] == slots[:, None], slots[None, :], 0), axis=1
        ).astype(jnp.int32)
        carry = flash(
            queries,
            part_bias,
            rows.reshape(-1, 2 * row_width),
            carry,
            carry is None,
            False,
            KEY_VALUE_HEADS,
            HEAD_SIZE,
            (order, live_count),
            KEY_BLOCK // PAGE_TOKENS,
        )
    attended = flash(
        queries,
        jnp.where(suffix_weights, 0.0, NEGATIVE_MASK).astype(jnp.float32),
        segment,
        carry,
        False,
        True,
        KEY_VALUE_HEADS,
        HEAD_SIZE,
    )
    projected = jnp.dot(attended, w_out, preferred_element_type=jnp.float32)
    resid = lax.optimization_barrier((hidden.astype(jnp.float32) + projected).astype(jnp.bfloat16))
    resid_f = resid.astype(jnp.float32)
    normed = (resid_f * lax.rsqrt(jnp.mean(resid_f * resid_f, axis=1, keepdims=True) + EPS)).astype(
        jnp.bfloat16
    )
    n_experts = w_router.shape[1]
    logits = jnp.dot(normed, w_router, preferred_element_type=jnp.float32)
    expert_ids = jnp.arange(n_experts, dtype=jnp.int32)
    chosen = jnp.sum(
        jnp.where(routes[:, :, None] == expert_ids[None, None, :], logits[:, None, :], 0.0), axis=2
    )
    gates = jax.nn.softmax(chosen, axis=1)
    capacity = 16
    member = routes[:, :, None] == expert_ids[None, None, :]
    picks = jnp.any(member, axis=1).astype(jnp.float32)
    gate_of = jnp.sum(jnp.where(member, gates[:, :, None], 0.0), axis=1)
    earlier = (
        jnp.arange(token_index, dtype=jnp.int32)[:, None]
        > jnp.arange(token_index, dtype=jnp.int32)[None, :]
    ).astype(jnp.float32)
    rank = jnp.dot(earlier, picks, precision=lax.Precision.HIGHEST).astype(jnp.int32)
    place = jnp.arange(capacity, dtype=jnp.int32)
    select = (picks[None, :, :] > 0) & (rank[None, :, :] == place[:, None, None])
    select = jnp.transpose(select, (2, 0, 1))
    select2 = jnp.broadcast_to(
        select[:, None], (n_experts, 2, capacity, token_index)
    ).reshape(2 * n_experts * capacity, token_index)
    weight = jnp.where(
        jnp.transpose(select, (2, 0, 1))[:, :, None, :],
        gate_of[:, :, None, None],
        0.0,
    )
    weight = jnp.broadcast_to(weight, (token_index, n_experts, 2, capacity))
    chunks = 2
    part = capacity // chunks
    select2 = select2.reshape(2 * n_experts, capacity, token_index)
    moe = resid_f
    for c in range(chunks):
        picked_rows = select2[:, c * part:(c + 1) * part].reshape(-1, token_index)
        outgoing = jnp.dot(
            picked_rows.astype(jnp.bfloat16), normed, preferred_element_type=jnp.float32
        ).astype(jnp.bfloat16)
        outgoing = outgoing.reshape(2 * n_experts, part, D)
        rows = lax.all_to_all(outgoing, ("req", "exp"), split_axis=0, concat_axis=0, tiled=True)
        flat_rows = rows.reshape(-1, D)
        gate_part = jnp.dot(flat_rows, w_gate[0], preferred_element_type=jnp.float32)
        up_part = jnp.dot(flat_rows, w_up[0], preferred_element_type=jnp.float32)
        inner = (jax.nn.silu(gate_part) * up_part).astype(jnp.bfloat16)
        returned = lax.all_to_all(
            jnp.dot(inner, w_down[0], preferred_element_type=jnp.float32)
            .astype(jnp.bfloat16)
            .reshape(rows.shape),
            ("req", "exp"),
            split_axis=0,
            concat_axis=0,
            tiled=True,
        ).reshape(-1, D)
        chunk_weight = weight[:, :, :, c * part:(c + 1) * part].reshape(token_index, -1)
        high = chunk_weight.astype(jnp.bfloat16)
        low = (chunk_weight - high.astype(jnp.float32)).astype(jnp.bfloat16)
        moe = (
            moe
            + jnp.dot(high, returned, preferred_element_type=jnp.float32)
            + jnp.dot(low, returned, preferred_element_type=jnp.float32)
        )
    return moe.astype(jnp.bfloat16)


def solution(mesh):
    placed = (
        P(("req", "exp"), None),
        P(("req", "exp"), None),
        P(("req", "exp"), None),
        P("req", None),
        P("req", None, None),
        P("req", None, None),
        P(),
        P(),
        P(("req", "exp"), None),
        P(("req", "exp"), None, None),
        P(("req", "exp"), None, None),
        P(("req", "exp"), None, None),
    )
    return jax.shard_map(
        on_device, mesh=mesh, in_specs=placed, out_specs=P(("req", "exp"), None), check_vma=False
    )
```

```python
import functools
import math

import jax
import jax.numpy as jnp
from jax import lax
from jax.experimental import pallas as pl
from jax.experimental.pallas import tpu as pltpu
from jax.sharding import PartitionSpec as P

D = 2560
QUERY_HEADS = 10
KEY_VALUE_HEADS = 2
HEAD_SIZE = 128
TOP = 6
PAGE_TOKENS = 128


NEGATIVE_MASK = -1e30
EPS = 1e-06


KEY_BLOCK = 512
LOG2_E = 1.4426950408889634


def attn_kernel(flags_ref, order_ref, q_ref, *refs, parts, first_call, last_call, groups, reps, hs):
    w_refs = refs[:parts]
    kv_refs = refs[parts:2 * parts]
    carried = 0 if first_call else 3
    if not first_call:
        m_in, l_in, acc_in = refs[2 * parts:2 * parts + 3]
    refs = refs[2 * parts + carried:]
    if last_call:
        o_ref, qs, m_ref, l_ref, acc_ref = refs
    else:
        m_out, l_out, acc_out, qs, m_ref, l_ref, acc_ref = refs
    j = pl.program_id(0)
    t = q_ref.shape[0]
    key_block = sum(kv.shape[0] for kv in kv_refs)

    @pl.when(j == 0)
    def _():
        for g in range(groups):
            qs[g] = jnp.concatenate(
                [q_ref[:, (g * reps + h) * hs:(g * reps + h + 1) * hs] for h in range(reps)], axis=0)
        if first_call:
            m_ref[...] = jnp.full(m_ref.shape, NEGATIVE_MASK, jnp.float32)
            l_ref[...] = jnp.zeros(l_ref.shape, jnp.float32)
            acc_ref[...] = jnp.zeros(acc_ref.shape, jnp.float32)
        else:
            m_ref[...] = m_in[...]
            l_ref[...] = l_in[...]
            acc_ref[...] = acc_in[...]

    def joined(pieces, axis):
        return pieces[0] if len(pieces) == 1 else jnp.concatenate(pieces, axis=axis)

    @pl.when(flags_ref[j] > 0)
    def _():
        bias = joined([w[...] for w in w_refs], 1)[None]
        for g in range(groups):
            k = joined([kv[:, g * hs:(g + 1) * hs] for kv in kv_refs], 0)
            v = joined([kv[:, (groups + g) * hs:(groups + g + 1) * hs] for kv in kv_refs], 0)
            s = lax.dot_general(qs[g], k, (((1,), (1,)), ((), ())),
                                preferred_element_type=jnp.float32) * (LOG2_E / math.sqrt(hs))
            s = s.reshape(reps, t, key_block) + bias
            m_old = m_ref[g].reshape(reps, t, 1)
            m_new = jnp.maximum(m_old, jnp.max(s, axis=-1, keepdims=True))
            p = jnp.exp2(s - m_new)
            alpha = jnp.exp2(m_old - m_new)
            l_ref[g] = (alpha * l_ref[g].reshape(reps, t, 1) + jnp.sum(p, axis=-1, keepdims=True)).reshape(reps * t, 1)
            pv = jnp.dot(p.reshape(reps * t, key_block).astype(jnp.bfloat16), v, preferred_element_type=jnp.float32)
            acc_ref[g] = alpha.reshape(reps * t, 1) * acc_ref[g] + pv
            m_ref[g] = m_new.reshape(reps * t, 1)

    @pl.when(j == pl.num_programs(0) - 1)
    def _():
        if last_call:
            for g in range(groups):
                for h in range(reps):
                    rows = slice(h * t, (h + 1) * t)
                    o_ref[:, (g * reps + h) * hs:(g * reps + h + 1) * hs] = (
                        acc_ref[g, rows, :] / l_ref[g, rows, :]).astype(o_ref.dtype)
        else:
            m_out[...] = m_ref[...]
            l_out[...] = l_ref[...]
            acc_out[...] = acc_ref[...]


def flash(queries, bias, kv_rows, carry, first_call, last_call, groups, hs, order=None, parts=1):
    t, width = queries.shape
    reps = width // hs // groups
    if order is None:
        block = KEY_BLOCK
        n_blocks = kv_rows.shape[0] // block
        flags = (
            jnp.max(bias.reshape(t, n_blocks, block), axis=(0, 2)) > 0.5 * NEGATIVE_MASK
        ).astype(jnp.int32)
        order = jnp.zeros((1,), jnp.int32)
        w_specs = [pl.BlockSpec((t, block), lambda j, f, o: (0, j))]
        kv_specs = [pl.BlockSpec((block, kv_rows.shape[1]), lambda j, f, o: (j, 0))]
    else:
        order, live_count = order
        block = kv_rows.shape[0] // order.shape[0]
        n_blocks = order.shape[0] // parts
        flags = (jnp.arange(n_blocks, dtype=jnp.int32) * parts < live_count).astype(jnp.int32)
        w_specs = [
            pl.BlockSpec((t, block), lambda j, f, o, i=i: (0, o[parts * j + i])) for i in range(parts)
        ]
        kv_specs = [
            pl.BlockSpec((block, kv_rows.shape[1]), lambda j, f, o, i=i: (o[parts * j + i], 0))
            for i in range(parts)
        ]
    kern = functools.partial(attn_kernel, parts=len(w_specs), first_call=first_call,
                             last_call=last_call, groups=groups, reps=reps, hs=hs)
    state = [
        jax.ShapeDtypeStruct((groups, reps * t, 1), jnp.float32),
        jax.ShapeDtypeStruct((groups, reps * t, 1), jnp.float32),
        jax.ShapeDtypeStruct((groups, reps * t, hs), jnp.float32),
    ]
    state_specs = [
        pl.BlockSpec((groups, reps * t, 1), lambda j, f, o: (0, 0, 0)),
        pl.BlockSpec((groups, reps * t, 1), lambda j, f, o: (0, 0, 0)),
        pl.BlockSpec((groups, reps * t, hs), lambda j, f, o: (0, 0, 0)),
    ]
    if last_call:
        out_shape = jax.ShapeDtypeStruct((t, width), jnp.bfloat16)
        out_specs = pl.BlockSpec((t, width), lambda j, f, o: (0, 0))
    else:
        out_shape, out_specs = state, state_specs
    grid_spec = pltpu.PrefetchScalarGridSpec(
        num_scalar_prefetch=2,
        grid=(n_blocks,),
        in_specs=[pl.BlockSpec((t, width), lambda j, f, o: (0, 0))]
        + w_specs
        + kv_specs
        + ([] if first_call else state_specs),
        out_specs=out_specs,
        scratch_shapes=[
            pltpu.VMEM((groups, reps * t, hs), jnp.bfloat16),
            pltpu.VMEM((groups, reps * t, 1), jnp.float32),
            pltpu.VMEM((groups, reps * t, 1), jnp.float32),
            pltpu.VMEM((groups, reps * t, hs), jnp.float32),
        ],
    )
    operands = [queries] + [bias] * len(w_specs) + [kv_rows] * len(kv_specs)
    if not first_call:
        operands += list(carry)
    return pl.pallas_call(kern, grid_spec=grid_spec, out_shape=out_shape)(flags, order, *operands)


def on_device(
    hidden,
    queries,
    suffix_kv,
    lengths,
    page_table,
    page_pool,
    w_out,
    w_router,
    routes,
    w_gate,
    w_up,
    w_down,
):
    token_index = hidden.shape[0]
    row_width = KEY_VALUE_HEADS * HEAD_SIZE
    request_groups = QUERY_HEADS // KEY_VALUE_HEADS
    request_count = lax.axis_size("req")
    pool_per_shard = page_pool.shape[0]
    pool_all = pool_per_shard * request_count
    positions = lax.axis_index("exp") * token_index + jnp.arange(token_index, dtype=jnp.int32)
    lens = lengths[0]
    ends = jnp.cumsum(lens)
    starts = ends - lens
    req_of = jnp.sum((positions[:, None] >= ends[None, :]).astype(jnp.int32), axis=1)
    pick = req_of[:, None] == jnp.arange(lens.shape[0], dtype=jnp.int32)[None, :]
    first = jnp.sum(jnp.where(pick, starts[None, :], 0), axis=1)
    pool_rows = lax.all_gather(page_pool, "req", axis=0, tiled=True).reshape(
        pool_all * PAGE_TOKENS, 2 * row_width
    )
    counts = jnp.sum(
        (page_table[0][:, :, None] == jnp.arange(pool_all, dtype=jnp.int32)[None, None, :]).astype(
            jnp.float32
        ),
        axis=1,
    )
    query_counts = jnp.dot(pick.astype(jnp.float32), counts, precision=lax.Precision.HIGHEST)
    keypos = jnp.arange(lax.axis_size("exp") * token_index, dtype=jnp.int32)
    suffix_weights = (keypos[None, :] <= positions[:, None]) & (keypos[None, :] >= first[:, None])
    spread = (
        jnp.arange(pool_all, dtype=jnp.int32)[:, None]
        == jnp.arange(pool_all * PAGE_TOKENS, dtype=jnp.int32)[None, :] // PAGE_TOKENS
    ).astype(jnp.bfloat16)
    key_counts = jnp.dot(
        query_counts.astype(jnp.bfloat16), spread, preferred_element_type=jnp.float32
    )
    pool_weights = jnp.where(
        key_counts > 0, jnp.log2(jnp.maximum(key_counts, 1.0)), NEGATIVE_MASK
    )
    live = jnp.max(query_counts, axis=0) > 0
    live_int = live.astype(jnp.int32)
    live_count = jnp.sum(live_int)
    destination = jnp.where(
        live, jnp.cumsum(live_int) - 1, live_count + jnp.cumsum(1 - live_int) - 1
    )
    slots = jnp.arange(pool_all, dtype=jnp.int32)
    order = jnp.sum(
        jnp.where(destination[None, :] == slots[:, None], slots[None, :], 0), axis=1
    ).astype(jnp.int32)
    suffix_after, pool_weights, order, live_count = lax.optimization_barrier(
        (suffix_kv, pool_weights, order, live_count)
    )
    segment = lax.all_gather(suffix_after, "exp", axis=0, tiled=True)
    carry = flash(
        queries,
        pool_weights,
        pool_rows,
        None,
        True,
        False,
        KEY_VALUE_HEADS,
        HEAD_SIZE,
        (order, live_count),
        KEY_BLOCK // PAGE_TOKENS,
    )
    attended = flash(
        queries,
        jnp.where(suffix_weights, 0.0, NEGATIVE_MASK).astype(jnp.float32),
        segment,
        carry,
        False,
        True,
        KEY_VALUE_HEADS,
        HEAD_SIZE,
    )
    projected = jnp.dot(attended, w_out, preferred_element_type=jnp.float32)
    resid = lax.optimization_barrier((hidden.astype(jnp.float32) + projected).astype(jnp.bfloat16))
    resid_f = resid.astype(jnp.float32)
    normed = (resid_f * lax.rsqrt(jnp.mean(resid_f * resid_f, axis=1, keepdims=True) + EPS)).astype(
        jnp.bfloat16
    )
    n_experts = w_router.shape[1]
    logits = jnp.dot(normed, w_router, preferred_element_type=jnp.float32)
    expert_ids = jnp.arange(n_experts, dtype=jnp.int32)
    chosen = jnp.sum(
        jnp.where(routes[:, :, None] == expert_ids[None, None, :], logits[:, None, :], 0.0), axis=2
    )
    gates = jax.nn.softmax(chosen, axis=1)
    capacity = 16
    member = routes[:, :, None] == expert_ids[None, None, :]
    picks = jnp.any(member, axis=1).astype(jnp.float32)
    gate_of = jnp.sum(jnp.where(member, gates[:, :, None], 0.0), axis=1)
    earlier = (
        jnp.arange(token_index, dtype=jnp.int32)[:, None]
        > jnp.arange(token_index, dtype=jnp.int32)[None, :]
    ).astype(jnp.float32)
    rank = jnp.dot(earlier, picks, precision=lax.Precision.HIGHEST).astype(jnp.int32)
    place = jnp.arange(capacity, dtype=jnp.int32)
    select = (picks[None, :, :] > 0) & (rank[None, :, :] == place[:, None, None])
    select = jnp.transpose(select, (2, 0, 1))
    select2 = jnp.broadcast_to(
        select[:, None], (n_experts, 2, capacity, token_index)
    ).reshape(2 * n_experts * capacity, token_index)
    weight = jnp.where(
        jnp.transpose(select, (2, 0, 1))[:, :, None, :],
        gate_of[:, :, None, None],
        0.0,
    )
    weight = jnp.broadcast_to(weight, (token_index, n_experts, 2, capacity))
    chunks = 2
    part = capacity // chunks
    select2 = select2.reshape(2 * n_experts, capacity, token_index)
    moe = resid_f
    for c in range(chunks):
        picked_rows = select2[:, c * part:(c + 1) * part].reshape(-1, token_index)
        outgoing = jnp.dot(
            picked_rows.astype(jnp.bfloat16), normed, preferred_element_type=jnp.float32
        ).astype(jnp.bfloat16)
        outgoing = outgoing.reshape(2 * n_experts, part, D)
        rows = lax.all_to_all(outgoing, ("req", "exp"), split_axis=0, concat_axis=0, tiled=True)
        flat_rows = rows.reshape(-1, D)
        gate_part = jnp.dot(flat_rows, w_gate[0], preferred_element_type=jnp.float32)
        up_part = jnp.dot(flat_rows, w_up[0], preferred_element_type=jnp.float32)
        inner = (jax.nn.silu(gate_part) * up_part).astype(jnp.bfloat16)
        returned = lax.all_to_all(
            jnp.dot(inner, w_down[0], preferred_element_type=jnp.float32)
            .astype(jnp.bfloat16)
            .reshape(rows.shape),
            ("req", "exp"),
            split_axis=0,
            concat_axis=0,
            tiled=True,
        ).reshape(-1, D)
        chunk_weight = weight[:, :, :, c * part:(c + 1) * part].reshape(token_index, -1)
        high = chunk_weight.astype(jnp.bfloat16)
        low = (chunk_weight - high.astype(jnp.float32)).astype(jnp.bfloat16)
        moe = (
            moe
            + jnp.dot(high, returned, preferred_element_type=jnp.float32)
            + jnp.dot(low, returned, preferred_element_type=jnp.float32)
        )
    return moe.astype(jnp.bfloat16)


def solution(mesh):
    placed = (
        P(("req", "exp"), None),
        P(("req", "exp"), None),
        P(("req", "exp"), None),
        P("req", None),
        P("req", None, None),
        P("req", None, None),
        P(),
        P(),
        P(("req", "exp"), None),
        P(("req", "exp"), None, None),
        P(("req", "exp"), None, None),
        P(("req", "exp"), None, None),
    )
    return jax.shard_map(
        on_device, mesh=mesh, in_specs=placed, out_specs=P(("req", "exp"), None), check_vma=False
    )
```

```python
import functools
import math

import jax
import jax.numpy as jnp
from jax import lax
from jax.experimental import pallas as pl
from jax.experimental.pallas import tpu as pltpu
from jax.sharding import PartitionSpec as P

D = 2560
QUERY_HEADS = 10
KEY_VALUE_HEADS = 2
HEAD_SIZE = 128
TOP = 6
PAGE_TOKENS = 128


NEGATIVE_MASK = -1e30
EPS = 1e-06


KEY_BLOCK = 512
LOG2_E = 1.4426950408889634


def attn_kernel(flags_ref, order_ref, q_ref, *refs, parts, first_call, last_call, groups, reps, hs):
    w_refs = refs[:parts]
    kv_refs = refs[parts:2 * parts]
    carried = 0 if first_call else 3
    if not first_call:
        m_in, l_in, acc_in = refs[2 * parts:2 * parts + 3]
    refs = refs[2 * parts + carried:]
    if last_call:
        o_ref, qs, m_ref, l_ref, acc_ref = refs
    else:
        m_out, l_out, acc_out, qs, m_ref, l_ref, acc_ref = refs
    j = pl.program_id(0)
    t = q_ref.shape[0]
    key_block = sum(kv.shape[0] for kv in kv_refs)

    @pl.when(j == 0)
    def _():
        for g in range(groups):
            qs[g] = jnp.concatenate(
                [q_ref[:, (g * reps + h) * hs:(g * reps + h + 1) * hs] for h in range(reps)], axis=0)
        if first_call:
            m_ref[...] = jnp.full(m_ref.shape, NEGATIVE_MASK, jnp.float32)
            l_ref[...] = jnp.zeros(l_ref.shape, jnp.float32)
            acc_ref[...] = jnp.zeros(acc_ref.shape, jnp.float32)
        else:
            m_ref[...] = m_in[...]
            l_ref[...] = l_in[...]
            acc_ref[...] = acc_in[...]

    def joined(pieces, axis):
        return pieces[0] if len(pieces) == 1 else jnp.concatenate(pieces, axis=axis)

    @pl.when(flags_ref[j] > 0)
    def _():
        bias = joined([w[...] for w in w_refs], 1)[None]
        for g in range(groups):
            k = joined([kv[:, g * hs:(g + 1) * hs] for kv in kv_refs], 0)
            v = joined([kv[:, (groups + g) * hs:(groups + g + 1) * hs] for kv in kv_refs], 0)
            s = lax.dot_general(qs[g], k, (((1,), (1,)), ((), ())),
                                preferred_element_type=jnp.float32) * (LOG2_E / math.sqrt(hs))
            s = s.reshape(reps, t, key_block) + bias
            m_old = m_ref[g].reshape(reps, t, 1)
            m_new = jnp.maximum(m_old, jnp.max(s, axis=-1, keepdims=True))
            p = jnp.exp2(s - m_new)
            alpha = jnp.exp2(m_old - m_new)
            l_ref[g] = (alpha * l_ref[g].reshape(reps, t, 1) + jnp.sum(p, axis=-1, keepdims=True)).reshape(reps * t, 1)
            pv = jnp.dot(p.reshape(reps * t, key_block).astype(jnp.bfloat16), v, preferred_element_type=jnp.float32)
            acc_ref[g] = alpha.reshape(reps * t, 1) * acc_ref[g] + pv
            m_ref[g] = m_new.reshape(reps * t, 1)

    @pl.when(j == pl.num_programs(0) - 1)
    def _():
        if last_call:
            for g in range(groups):
                for h in range(reps):
                    rows = slice(h * t, (h + 1) * t)
                    o_ref[:, (g * reps + h) * hs:(g * reps + h + 1) * hs] = (
                        acc_ref[g, rows, :] / l_ref[g, rows, :]).astype(o_ref.dtype)
        else:
            m_out[...] = m_ref[...]
            l_out[...] = l_ref[...]
            acc_out[...] = acc_ref[...]


def flash(queries, bias, kv_rows, carry, first_call, last_call, groups, hs, order=None, parts=1):
    t, width = queries.shape
    reps = width // hs // groups
    if order is None:
        block = KEY_BLOCK
        n_blocks = kv_rows.shape[0] // block
        flags = (
            jnp.max(bias.reshape(t, n_blocks, block), axis=(0, 2)) > 0.5 * NEGATIVE_MASK
        ).astype(jnp.int32)
        order = jnp.zeros((1,), jnp.int32)
        w_specs = [pl.BlockSpec((t, block), lambda j, f, o: (0, j))]
        kv_specs = [pl.BlockSpec((block, kv_rows.shape[1]), lambda j, f, o: (j, 0))]
    else:
        order, live_count = order
        block = kv_rows.shape[0] // order.shape[0]
        n_blocks = order.shape[0] // parts
        flags = (jnp.arange(n_blocks, dtype=jnp.int32) * parts < live_count).astype(jnp.int32)
        w_specs = [
            pl.BlockSpec((t, block), lambda j, f, o, i=i: (0, o[parts * j + i])) for i in range(parts)
        ]
        kv_specs = [
            pl.BlockSpec((block, kv_rows.shape[1]), lambda j, f, o, i=i: (o[parts * j + i], 0))
            for i in range(parts)
        ]
    kern = functools.partial(attn_kernel, parts=len(w_specs), first_call=first_call,
                             last_call=last_call, groups=groups, reps=reps, hs=hs)
    state = [
        jax.ShapeDtypeStruct((groups, reps * t, 1), jnp.float32),
        jax.ShapeDtypeStruct((groups, reps * t, 1), jnp.float32),
        jax.ShapeDtypeStruct((groups, reps * t, hs), jnp.float32),
    ]
    state_specs = [
        pl.BlockSpec((groups, reps * t, 1), lambda j, f, o: (0, 0, 0)),
        pl.BlockSpec((groups, reps * t, 1), lambda j, f, o: (0, 0, 0)),
        pl.BlockSpec((groups, reps * t, hs), lambda j, f, o: (0, 0, 0)),
    ]
    if last_call:
        out_shape = jax.ShapeDtypeStruct((t, width), jnp.bfloat16)
        out_specs = pl.BlockSpec((t, width), lambda j, f, o: (0, 0))
    else:
        out_shape, out_specs = state, state_specs
    grid_spec = pltpu.PrefetchScalarGridSpec(
        num_scalar_prefetch=2,
        grid=(n_blocks,),
        in_specs=[pl.BlockSpec((t, width), lambda j, f, o: (0, 0))]
        + w_specs
        + kv_specs
        + ([] if first_call else state_specs),
        out_specs=out_specs,
        scratch_shapes=[
            pltpu.VMEM((groups, reps * t, hs), jnp.bfloat16),
            pltpu.VMEM((groups, reps * t, 1), jnp.float32),
            pltpu.VMEM((groups, reps * t, 1), jnp.float32),
            pltpu.VMEM((groups, reps * t, hs), jnp.float32),
        ],
    )
    operands = [queries] + [bias] * len(w_specs) + [kv_rows] * len(kv_specs)
    if not first_call:
        operands += list(carry)
    return pl.pallas_call(kern, grid_spec=grid_spec, out_shape=out_shape)(flags, order, *operands)


def on_device(
    hidden,
    queries,
    suffix_kv,
    lengths,
    page_table,
    page_pool,
    w_out,
    w_router,
    routes,
    w_gate,
    w_up,
    w_down,
):
    token_index = hidden.shape[0]
    row_width = KEY_VALUE_HEADS * HEAD_SIZE
    request_groups = QUERY_HEADS // KEY_VALUE_HEADS
    request_count = lax.axis_size("req")
    pool_per_shard = page_pool.shape[0]
    pool_all = pool_per_shard * request_count
    positions = lax.axis_index("exp") * token_index + jnp.arange(token_index, dtype=jnp.int32)
    lens = lengths[0]
    ends = jnp.cumsum(lens)
    starts = ends - lens
    req_of = jnp.sum((positions[:, None] >= ends[None, :]).astype(jnp.int32), axis=1)
    pick = req_of[:, None] == jnp.arange(lens.shape[0], dtype=jnp.int32)[None, :]
    first = jnp.sum(jnp.where(pick, starts[None, :], 0), axis=1)
    pool_rows = lax.all_gather(page_pool, "req", axis=0, tiled=True).reshape(
        pool_all * PAGE_TOKENS, 2 * row_width
    )
    counts = jnp.sum(
        (page_table[0][:, :, None] == jnp.arange(pool_all, dtype=jnp.int32)[None, None, :]).astype(
            jnp.float32
        ),
        axis=1,
    )
    query_counts = jnp.dot(pick.astype(jnp.float32), counts, precision=lax.Precision.HIGHEST)
    keypos = jnp.arange(lax.axis_size("exp") * token_index, dtype=jnp.int32)
    suffix_weights = (keypos[None, :] <= positions[:, None]) & (keypos[None, :] >= first[:, None])
    spread = (
        jnp.arange(pool_all, dtype=jnp.int32)[:, None]
        == jnp.arange(pool_all * PAGE_TOKENS, dtype=jnp.int32)[None, :] // PAGE_TOKENS
    ).astype(jnp.bfloat16)
    key_counts = jnp.dot(
        query_counts.astype(jnp.bfloat16), spread, preferred_element_type=jnp.float32
    )
    pool_weights = jnp.where(
        key_counts > 0, jnp.log2(jnp.maximum(key_counts, 1.0)), NEGATIVE_MASK
    )
    live = jnp.max(query_counts, axis=0) > 0
    live_int = live.astype(jnp.int32)
    live_count = jnp.sum(live_int)
    destination = jnp.where(
        live, jnp.cumsum(live_int) - 1, live_count + jnp.cumsum(1 - live_int) - 1
    )
    slots = jnp.arange(pool_all, dtype=jnp.int32)
    order = jnp.sum(
        jnp.where(destination[None, :] == slots[:, None], slots[None, :], 0), axis=1
    ).astype(jnp.int32)
    suffix_after, pool_weights, order, live_count = lax.optimization_barrier(
        (suffix_kv, pool_weights, order, live_count)
    )
    segment = lax.all_gather(suffix_after, "exp", axis=0, tiled=True)
    carry = flash(
        queries,
        pool_weights,
        pool_rows,
        None,
        True,
        False,
        KEY_VALUE_HEADS,
        HEAD_SIZE,
        (order, live_count),
        KEY_BLOCK // PAGE_TOKENS,
    )
    attended = flash(
        queries,
        jnp.where(suffix_weights, 0.0, NEGATIVE_MASK).astype(jnp.float32),
        segment,
        carry,
        False,
        True,
        KEY_VALUE_HEADS,
        HEAD_SIZE,
    )
    projected = jnp.dot(attended, w_out, preferred_element_type=jnp.float32)
    resid = lax.optimization_barrier((hidden.astype(jnp.float32) + projected).astype(jnp.bfloat16))
    resid_f = resid.astype(jnp.float32)
    normed = (resid_f * lax.rsqrt(jnp.mean(resid_f * resid_f, axis=1, keepdims=True) + EPS)).astype(
        jnp.bfloat16
    )
    n_experts = w_router.shape[1]
    logits = jnp.dot(normed, w_router, preferred_element_type=jnp.float32)
    expert_ids = jnp.arange(n_experts, dtype=jnp.int32)
    chosen = jnp.sum(
        jnp.where(routes[:, :, None] == expert_ids[None, None, :], logits[:, None, :], 0.0), axis=2
    )
    gates = jax.nn.softmax(chosen, axis=1)
    capacity = 16
    member = routes[:, :, None] == expert_ids[None, None, :]
    picks = jnp.any(member, axis=1).astype(jnp.float32)
    gate_of = jnp.sum(jnp.where(member, gates[:, :, None], 0.0), axis=1)
    earlier = (
        jnp.arange(token_index, dtype=jnp.int32)[:, None]
        > jnp.arange(token_index, dtype=jnp.int32)[None, :]
    ).astype(jnp.float32)
    rank = jnp.dot(earlier, picks, precision=lax.Precision.HIGHEST).astype(jnp.int32)
    place = jnp.arange(capacity, dtype=jnp.int32)
    select = (picks[None, :, :] > 0) & (rank[None, :, :] == place[:, None, None])
    select = jnp.transpose(select, (2, 0, 1))
    select2 = jnp.broadcast_to(
        select[:, None], (n_experts, 2, capacity, token_index)
    ).reshape(2 * n_experts * capacity, token_index)
    weight = jnp.where(
        jnp.transpose(select, (2, 0, 1))[:, :, None, :],
        gate_of[:, :, None, None],
        0.0,
    )
    weight = jnp.broadcast_to(weight, (token_index, n_experts, 2, capacity))
    chunks = 2
    part = capacity // chunks
    select2 = select2.reshape(2 * n_experts, capacity, token_index)
    moe = resid_f
    for c in range(chunks):
        picked_rows = select2[:, c * part:(c + 1) * part].reshape(-1, token_index)
        outgoing = jnp.dot(
            picked_rows.astype(jnp.bfloat16), normed, preferred_element_type=jnp.float32
        ).astype(jnp.bfloat16)
        outgoing = outgoing.reshape(2 * n_experts, part, D)
        rows = lax.all_to_all(outgoing, ("req", "exp"), split_axis=0, concat_axis=0, tiled=True)
        flat_rows = rows.reshape(-1, D)
        gate_part = jnp.dot(flat_rows, w_gate[0], preferred_element_type=jnp.float32)
        up_part = jnp.dot(flat_rows, w_up[0], preferred_element_type=jnp.float32)
        inner = (jax.nn.silu(gate_part) * up_part).astype(jnp.bfloat16)
        returned = lax.all_to_all(
            jnp.dot(inner, w_down[0], preferred_element_type=jnp.float32)
            .astype(jnp.bfloat16)
            .reshape(rows.shape),
            ("req", "exp"),
            split_axis=0,
            concat_axis=0,
            tiled=True,
        ).reshape(-1, D)
        chunk_weight = weight[:, :, :, c * part:(c + 1) * part].reshape(token_index, -1)
        high = chunk_weight.astype(jnp.bfloat16)
        low = (chunk_weight - high.astype(jnp.float32)).astype(jnp.bfloat16)
        both = jnp.dot(
            jnp.concatenate([high, low], axis=0), returned, preferred_element_type=jnp.float32
        )
        moe = moe + both[:token_index] + both[token_index:]
    return moe.astype(jnp.bfloat16)


def solution(mesh):
    placed = (
        P(("req", "exp"), None),
        P(("req", "exp"), None),
        P(("req", "exp"), None),
        P("req", None),
        P("req", None, None),
        P("req", None, None),
        P(),
        P(),
        P(("req", "exp"), None),
        P(("req", "exp"), None, None),
        P(("req", "exp"), None, None),
        P(("req", "exp"), None, None),
    )
    return jax.shard_map(
        on_device, mesh=mesh, in_specs=placed, out_specs=P(("req", "exp"), None), check_vma=False
    )
```

```python
import functools
import math

import jax
import jax.numpy as jnp
from jax import lax
from jax.experimental import pallas as pl
from jax.experimental.pallas import tpu as pltpu
from jax.sharding import PartitionSpec as P

D = 2560
QUERY_HEADS = 10
KEY_VALUE_HEADS = 2
HEAD_SIZE = 128
TOP = 6
PAGE_TOKENS = 128


NEGATIVE_MASK = -1e30
EPS = 1e-06


KEY_BLOCK = 512
LOG2_E = 1.4426950408889634


def attn_kernel(flags_ref, order_ref, q_ref, *refs, parts, first_call, last_call, groups, reps, hs):
    w_refs = refs[:parts]
    kv_refs = refs[parts:2 * parts]
    carried = 0 if first_call else 3
    if not first_call:
        m_in, l_in, acc_in = refs[2 * parts:2 * parts + 3]
    refs = refs[2 * parts + carried:]
    if last_call:
        o_ref, qs, m_ref, l_ref, acc_ref = refs
    else:
        m_out, l_out, acc_out, qs, m_ref, l_ref, acc_ref = refs
    j = pl.program_id(0)
    t = q_ref.shape[0]
    key_block = sum(kv.shape[0] for kv in kv_refs)

    @pl.when(j == 0)
    def _():
        for g in range(groups):
            qs[g] = jnp.concatenate(
                [q_ref[:, (g * reps + h) * hs:(g * reps + h + 1) * hs] for h in range(reps)], axis=0)
        if first_call:
            m_ref[...] = jnp.full(m_ref.shape, NEGATIVE_MASK, jnp.float32)
            l_ref[...] = jnp.zeros(l_ref.shape, jnp.float32)
            acc_ref[...] = jnp.zeros(acc_ref.shape, jnp.float32)
        else:
            m_ref[...] = m_in[...]
            l_ref[...] = l_in[...]
            acc_ref[...] = acc_in[...]

    def joined(pieces, axis):
        return pieces[0] if len(pieces) == 1 else jnp.concatenate(pieces, axis=axis)

    @pl.when(flags_ref[j] > 0)
    def _():
        bias = joined([w[...] for w in w_refs], 1)[None]
        for g in range(groups):
            k = joined([kv[:, g * hs:(g + 1) * hs] for kv in kv_refs], 0)
            v = joined([kv[:, (groups + g) * hs:(groups + g + 1) * hs] for kv in kv_refs], 0)
            s = lax.dot_general(qs[g], k, (((1,), (1,)), ((), ())),
                                preferred_element_type=jnp.float32) * (LOG2_E / math.sqrt(hs))
            s = s.reshape(reps, t, key_block) + bias
            m_old = m_ref[g].reshape(reps, t, 1)
            m_new = jnp.maximum(m_old, jnp.max(s, axis=-1, keepdims=True))
            p = jnp.exp2(s - m_new)
            alpha = jnp.exp2(m_old - m_new)
            l_ref[g] = (alpha * l_ref[g].reshape(reps, t, 1) + jnp.sum(p, axis=-1, keepdims=True)).reshape(reps * t, 1)
            pv = jnp.dot(p.reshape(reps * t, key_block).astype(jnp.bfloat16), v, preferred_element_type=jnp.float32)
            acc_ref[g] = alpha.reshape(reps * t, 1) * acc_ref[g] + pv
            m_ref[g] = m_new.reshape(reps * t, 1)

    @pl.when(j == pl.num_programs(0) - 1)
    def _():
        if last_call:
            for g in range(groups):
                for h in range(reps):
                    rows = slice(h * t, (h + 1) * t)
                    o_ref[:, (g * reps + h) * hs:(g * reps + h + 1) * hs] = (
                        acc_ref[g, rows, :] / l_ref[g, rows, :]).astype(o_ref.dtype)
        else:
            m_out[...] = m_ref[...]
            l_out[...] = l_ref[...]
            acc_out[...] = acc_ref[...]


def flash(queries, bias, kv_rows, carry, first_call, last_call, groups, hs, order=None, parts=1):
    t, width = queries.shape
    reps = width // hs // groups
    if order is None:
        block = KEY_BLOCK
        n_blocks = kv_rows.shape[0] // block
        flags = (
            jnp.max(bias.reshape(t, n_blocks, block), axis=(0, 2)) > 0.5 * NEGATIVE_MASK
        ).astype(jnp.int32)
        order = jnp.zeros((1,), jnp.int32)
        w_specs = [pl.BlockSpec((t, block), lambda j, f, o: (0, j))]
        kv_specs = [pl.BlockSpec((block, kv_rows.shape[1]), lambda j, f, o: (j, 0))]
    else:
        order, live_count = order
        block = kv_rows.shape[0] // order.shape[0]
        n_blocks = order.shape[0] // parts
        flags = (jnp.arange(n_blocks, dtype=jnp.int32) * parts < live_count).astype(jnp.int32)
        w_specs = [
            pl.BlockSpec((t, block), lambda j, f, o, i=i: (0, o[parts * j + i])) for i in range(parts)
        ]
        kv_specs = [
            pl.BlockSpec((block, kv_rows.shape[1]), lambda j, f, o, i=i: (o[parts * j + i], 0))
            for i in range(parts)
        ]
    kern = functools.partial(attn_kernel, parts=len(w_specs), first_call=first_call,
                             last_call=last_call, groups=groups, reps=reps, hs=hs)
    state = [
        jax.ShapeDtypeStruct((groups, reps * t, 1), jnp.float32),
        jax.ShapeDtypeStruct((groups, reps * t, 1), jnp.float32),
        jax.ShapeDtypeStruct((groups, reps * t, hs), jnp.float32),
    ]
    state_specs = [
        pl.BlockSpec((groups, reps * t, 1), lambda j, f, o: (0, 0, 0)),
        pl.BlockSpec((groups, reps * t, 1), lambda j, f, o: (0, 0, 0)),
        pl.BlockSpec((groups, reps * t, hs), lambda j, f, o: (0, 0, 0)),
    ]
    if last_call:
        out_shape = jax.ShapeDtypeStruct((t, width), jnp.bfloat16)
        out_specs = pl.BlockSpec((t, width), lambda j, f, o: (0, 0))
    else:
        out_shape, out_specs = state, state_specs
    grid_spec = pltpu.PrefetchScalarGridSpec(
        num_scalar_prefetch=2,
        grid=(n_blocks,),
        in_specs=[pl.BlockSpec((t, width), lambda j, f, o: (0, 0))]
        + w_specs
        + kv_specs
        + ([] if first_call else state_specs),
        out_specs=out_specs,
        scratch_shapes=[
            pltpu.VMEM((groups, reps * t, hs), jnp.bfloat16),
            pltpu.VMEM((groups, reps * t, 1), jnp.float32),
            pltpu.VMEM((groups, reps * t, 1), jnp.float32),
            pltpu.VMEM((groups, reps * t, hs), jnp.float32),
        ],
    )
    operands = [queries] + [bias] * len(w_specs) + [kv_rows] * len(kv_specs)
    if not first_call:
        operands += list(carry)
    return pl.pallas_call(kern, grid_spec=grid_spec, out_shape=out_shape)(flags, order, *operands)


def on_device(
    hidden,
    queries,
    suffix_kv,
    lengths,
    page_table,
    page_pool,
    w_out,
    w_router,
    routes,
    w_gate,
    w_up,
    w_down,
):
    token_index = hidden.shape[0]
    row_width = KEY_VALUE_HEADS * HEAD_SIZE
    request_groups = QUERY_HEADS // KEY_VALUE_HEADS
    request_count = lax.axis_size("req")
    pool_per_shard = page_pool.shape[0]
    pool_all = pool_per_shard * request_count
    positions = lax.axis_index("exp") * token_index + jnp.arange(token_index, dtype=jnp.int32)
    lens = lengths[0]
    ends = jnp.cumsum(lens)
    starts = ends - lens
    req_of = jnp.sum((positions[:, None] >= ends[None, :]).astype(jnp.int32), axis=1)
    pick = req_of[:, None] == jnp.arange(lens.shape[0], dtype=jnp.int32)[None, :]
    first = jnp.sum(jnp.where(pick, starts[None, :], 0), axis=1)
    pool_rows = lax.all_gather(page_pool, "req", axis=0, tiled=True).reshape(
        pool_all * PAGE_TOKENS, 2 * row_width
    )
    counts = jnp.sum(
        (page_table[0][:, :, None] == jnp.arange(pool_all, dtype=jnp.int32)[None, None, :]).astype(
            jnp.float32
        ),
        axis=1,
    )
    query_counts = jnp.dot(pick.astype(jnp.float32), counts, precision=lax.Precision.HIGHEST)
    keypos = jnp.arange(lax.axis_size("exp") * token_index, dtype=jnp.int32)
    suffix_weights = (keypos[None, :] <= positions[:, None]) & (keypos[None, :] >= first[:, None])
    spread = (
        jnp.arange(pool_all, dtype=jnp.int32)[:, None]
        == jnp.arange(pool_all * PAGE_TOKENS, dtype=jnp.int32)[None, :] // PAGE_TOKENS
    ).astype(jnp.bfloat16)
    key_counts = jnp.dot(
        query_counts.astype(jnp.bfloat16), spread, preferred_element_type=jnp.float32
    )
    pool_weights = jnp.where(
        key_counts > 0, jnp.log2(jnp.maximum(key_counts, 1.0)), NEGATIVE_MASK
    )
    live = jnp.max(query_counts, axis=0) > 0
    live_int = live.astype(jnp.int32)
    live_count = jnp.sum(live_int)
    destination = jnp.where(
        live, jnp.cumsum(live_int) - 1, live_count + jnp.cumsum(1 - live_int) - 1
    )
    slots = jnp.arange(pool_all, dtype=jnp.int32)
    order = jnp.sum(
        jnp.where(destination[None, :] == slots[:, None], slots[None, :], 0), axis=1
    ).astype(jnp.int32)
    suffix_after, pool_weights, order, live_count = lax.optimization_barrier(
        (suffix_kv, pool_weights, order, live_count)
    )
    segment = lax.all_gather(suffix_after, "exp", axis=0, tiled=True)
    carry = flash(
        queries,
        pool_weights,
        pool_rows,
        None,
        True,
        False,
        KEY_VALUE_HEADS,
        HEAD_SIZE,
        (order, live_count),
        2 * KEY_BLOCK // PAGE_TOKENS,
    )
    attended = flash(
        queries,
        jnp.where(suffix_weights, 0.0, NEGATIVE_MASK).astype(jnp.float32),
        segment,
        carry,
        False,
        True,
        KEY_VALUE_HEADS,
        HEAD_SIZE,
    )
    projected = jnp.dot(attended, w_out, preferred_element_type=jnp.float32)
    resid = lax.optimization_barrier((hidden.astype(jnp.float32) + projected).astype(jnp.bfloat16))
    resid_f = resid.astype(jnp.float32)
    normed = (resid_f * lax.rsqrt(jnp.mean(resid_f * resid_f, axis=1, keepdims=True) + EPS)).astype(
        jnp.bfloat16
    )
    n_experts = w_router.shape[1]
    logits = jnp.dot(normed, w_router, preferred_element_type=jnp.float32)
    expert_ids = jnp.arange(n_experts, dtype=jnp.int32)
    chosen = jnp.sum(
        jnp.where(routes[:, :, None] == expert_ids[None, None, :], logits[:, None, :], 0.0), axis=2
    )
    gates = jax.nn.softmax(chosen, axis=1)
    capacity = 16
    member = routes[:, :, None] == expert_ids[None, None, :]
    picks = jnp.any(member, axis=1).astype(jnp.float32)
    gate_of = jnp.sum(jnp.where(member, gates[:, :, None], 0.0), axis=1)
    earlier = (
        jnp.arange(token_index, dtype=jnp.int32)[:, None]
        > jnp.arange(token_index, dtype=jnp.int32)[None, :]
    ).astype(jnp.float32)
    rank = jnp.dot(earlier, picks, precision=lax.Precision.HIGHEST).astype(jnp.int32)
    place = jnp.arange(capacity, dtype=jnp.int32)
    select = (picks[None, :, :] > 0) & (rank[None, :, :] == place[:, None, None])
    select = jnp.transpose(select, (2, 0, 1))
    select2 = jnp.broadcast_to(
        select[:, None], (n_experts, 2, capacity, token_index)
    ).reshape(2 * n_experts * capacity, token_index)
    weight = jnp.where(
        jnp.transpose(select, (2, 0, 1))[:, :, None, :],
        gate_of[:, :, None, None],
        0.0,
    )
    weight = jnp.broadcast_to(weight, (token_index, n_experts, 2, capacity))
    chunks = 2
    part = capacity // chunks
    select2 = select2.reshape(2 * n_experts, capacity, token_index)
    moe = resid_f
    for c in range(chunks):
        picked_rows = select2[:, c * part:(c + 1) * part].reshape(-1, token_index)
        outgoing = jnp.dot(
            picked_rows.astype(jnp.bfloat16), normed, preferred_element_type=jnp.float32
        ).astype(jnp.bfloat16)
        outgoing = outgoing.reshape(2 * n_experts, part, D)
        rows = lax.all_to_all(outgoing, ("req", "exp"), split_axis=0, concat_axis=0, tiled=True)
        flat_rows = rows.reshape(-1, D)
        gate_part = jnp.dot(flat_rows, w_gate[0], preferred_element_type=jnp.float32)
        up_part = jnp.dot(flat_rows, w_up[0], preferred_element_type=jnp.float32)
        inner = (jax.nn.silu(gate_part) * up_part).astype(jnp.bfloat16)
        returned = lax.all_to_all(
            jnp.dot(inner, w_down[0], preferred_element_type=jnp.float32)
            .astype(jnp.bfloat16)
            .reshape(rows.shape),
            ("req", "exp"),
            split_axis=0,
            concat_axis=0,
            tiled=True,
        ).reshape(-1, D)
        chunk_weight = weight[:, :, :, c * part:(c + 1) * part].reshape(token_index, -1)
        high = chunk_weight.astype(jnp.bfloat16)
        low = (chunk_weight - high.astype(jnp.float32)).astype(jnp.bfloat16)
        both = jnp.dot(
            jnp.concatenate([high, low], axis=0), returned, preferred_element_type=jnp.float32
        )
        moe = moe + both[:token_index] + both[token_index:]
    return moe.astype(jnp.bfloat16)


def solution(mesh):
    placed = (
        P(("req", "exp"), None),
        P(("req", "exp"), None),
        P(("req", "exp"), None),
        P("req", None),
        P("req", None, None),
        P("req", None, None),
        P(),
        P(),
        P(("req", "exp"), None),
        P(("req", "exp"), None, None),
        P(("req", "exp"), None, None),
        P(("req", "exp"), None, None),
    )
    return jax.shard_map(
        on_device, mesh=mesh, in_specs=placed, out_specs=P(("req", "exp"), None), check_vma=False
    )
```

```python
import functools
import math

import jax
import jax.numpy as jnp
from jax import lax
from jax.experimental import pallas as pl
from jax.experimental.pallas import tpu as pltpu
from jax.sharding import PartitionSpec as P

D = 2560
QUERY_HEADS = 10
KEY_VALUE_HEADS = 2
HEAD_SIZE = 128
TOP = 6
PAGE_TOKENS = 128


NEGATIVE_MASK = -1e30
EPS = 1e-06


KEY_BLOCK = 512
LOG2_E = 1.4426950408889634


def attn_kernel(flags_ref, order_ref, q_ref, *refs, parts, first_call, last_call, groups, reps, hs):
    w_refs = refs[:parts]
    kv_refs = refs[parts:2 * parts]
    carried = 0 if first_call else 3
    if not first_call:
        m_in, l_in, acc_in = refs[2 * parts:2 * parts + 3]
    refs = refs[2 * parts + carried:]
    if last_call:
        o_ref, qs, m_ref, l_ref, acc_ref = refs
    else:
        m_out, l_out, acc_out, qs, m_ref, l_ref, acc_ref = refs
    j = pl.program_id(0)
    t = q_ref.shape[0]
    key_block = sum(kv.shape[0] for kv in kv_refs)

    @pl.when(j == 0)
    def _():
        for g in range(groups):
            qs[g] = jnp.concatenate(
                [q_ref[:, (g * reps + h) * hs:(g * reps + h + 1) * hs] for h in range(reps)], axis=0)
        if first_call:
            m_ref[...] = jnp.full(m_ref.shape, NEGATIVE_MASK, jnp.float32)
            l_ref[...] = jnp.zeros(l_ref.shape, jnp.float32)
            acc_ref[...] = jnp.zeros(acc_ref.shape, jnp.float32)
        else:
            m_ref[...] = m_in[...]
            l_ref[...] = l_in[...]
            acc_ref[...] = acc_in[...]

    def joined(pieces, axis):
        return pieces[0] if len(pieces) == 1 else jnp.concatenate(pieces, axis=axis)

    @pl.when(flags_ref[j] > 0)
    def _():
        bias = joined([w[...] for w in w_refs], 1)[None]
        for g in range(groups):
            k = joined([kv[:, g * hs:(g + 1) * hs] for kv in kv_refs], 0)
            v = joined([kv[:, (groups + g) * hs:(groups + g + 1) * hs] for kv in kv_refs], 0)
            s = lax.dot_general(qs[g], k, (((1,), (1,)), ((), ())),
                                preferred_element_type=jnp.float32) * (LOG2_E / math.sqrt(hs))
            s = s.reshape(reps, t, key_block) + bias
            m_old = m_ref[g].reshape(reps, t, 1)
            m_new = jnp.maximum(m_old, jnp.max(s, axis=-1, keepdims=True))
            p = jnp.exp2(s - m_new)
            alpha = jnp.exp2(m_old - m_new)
            l_ref[g] = (alpha * l_ref[g].reshape(reps, t, 1) + jnp.sum(p, axis=-1, keepdims=True)).reshape(reps * t, 1)
            pv = jnp.dot(p.reshape(reps * t, key_block).astype(jnp.bfloat16), v, preferred_element_type=jnp.float32)
            acc_ref[g] = alpha.reshape(reps * t, 1) * acc_ref[g] + pv
            m_ref[g] = m_new.reshape(reps * t, 1)

    @pl.when(j == pl.num_programs(0) - 1)
    def _():
        if last_call:
            for g in range(groups):
                for h in range(reps):
                    rows = slice(h * t, (h + 1) * t)
                    o_ref[:, (g * reps + h) * hs:(g * reps + h + 1) * hs] = (
                        acc_ref[g, rows, :] / l_ref[g, rows, :]).astype(o_ref.dtype)
        else:
            m_out[...] = m_ref[...]
            l_out[...] = l_ref[...]
            acc_out[...] = acc_ref[...]


def flash(queries, bias, kv_rows, carry, first_call, last_call, groups, hs, order=None, parts=1):
    t, width = queries.shape
    reps = width // hs // groups
    if order is None:
        block = KEY_BLOCK // 2
        n_blocks = kv_rows.shape[0] // block
        flags = (
            jnp.max(bias.reshape(t, n_blocks, block), axis=(0, 2)) > 0.5 * NEGATIVE_MASK
        ).astype(jnp.int32)
        order = jnp.zeros((1,), jnp.int32)
        w_specs = [pl.BlockSpec((t, block), lambda j, f, o: (0, j))]
        kv_specs = [pl.BlockSpec((block, kv_rows.shape[1]), lambda j, f, o: (j, 0))]
    else:
        order, live_count = order
        block = kv_rows.shape[0] // order.shape[0]
        n_blocks = order.shape[0] // parts
        flags = (jnp.arange(n_blocks, dtype=jnp.int32) * parts < live_count).astype(jnp.int32)
        w_specs = [
            pl.BlockSpec((t, block), lambda j, f, o, i=i: (0, o[parts * j + i])) for i in range(parts)
        ]
        kv_specs = [
            pl.BlockSpec((block, kv_rows.shape[1]), lambda j, f, o, i=i: (o[parts * j + i], 0))
            for i in range(parts)
        ]
    kern = functools.partial(attn_kernel, parts=len(w_specs), first_call=first_call,
                             last_call=last_call, groups=groups, reps=reps, hs=hs)
    state = [
        jax.ShapeDtypeStruct((groups, reps * t, 1), jnp.float32),
        jax.ShapeDtypeStruct((groups, reps * t, 1), jnp.float32),
        jax.ShapeDtypeStruct((groups, reps * t, hs), jnp.float32),
    ]
    state_specs = [
        pl.BlockSpec((groups, reps * t, 1), lambda j, f, o: (0, 0, 0)),
        pl.BlockSpec((groups, reps * t, 1), lambda j, f, o: (0, 0, 0)),
        pl.BlockSpec((groups, reps * t, hs), lambda j, f, o: (0, 0, 0)),
    ]
    if last_call:
        out_shape = jax.ShapeDtypeStruct((t, width), jnp.bfloat16)
        out_specs = pl.BlockSpec((t, width), lambda j, f, o: (0, 0))
    else:
        out_shape, out_specs = state, state_specs
    grid_spec = pltpu.PrefetchScalarGridSpec(
        num_scalar_prefetch=2,
        grid=(n_blocks,),
        in_specs=[pl.BlockSpec((t, width), lambda j, f, o: (0, 0))]
        + w_specs
        + kv_specs
        + ([] if first_call else state_specs),
        out_specs=out_specs,
        scratch_shapes=[
            pltpu.VMEM((groups, reps * t, hs), jnp.bfloat16),
            pltpu.VMEM((groups, reps * t, 1), jnp.float32),
            pltpu.VMEM((groups, reps * t, 1), jnp.float32),
            pltpu.VMEM((groups, reps * t, hs), jnp.float32),
        ],
    )
    operands = [queries] + [bias] * len(w_specs) + [kv_rows] * len(kv_specs)
    if not first_call:
        operands += list(carry)
    return pl.pallas_call(kern, grid_spec=grid_spec, out_shape=out_shape)(flags, order, *operands)


def on_device(
    hidden,
    queries,
    suffix_kv,
    lengths,
    page_table,
    page_pool,
    w_out,
    w_router,
    routes,
    w_gate,
    w_up,
    w_down,
):
    token_index = hidden.shape[0]
    row_width = KEY_VALUE_HEADS * HEAD_SIZE
    request_groups = QUERY_HEADS // KEY_VALUE_HEADS
    request_count = lax.axis_size("req")
    pool_per_shard = page_pool.shape[0]
    pool_all = pool_per_shard * request_count
    positions = lax.axis_index("exp") * token_index + jnp.arange(token_index, dtype=jnp.int32)
    lens = lengths[0]
    ends = jnp.cumsum(lens)
    starts = ends - lens
    req_of = jnp.sum((positions[:, None] >= ends[None, :]).astype(jnp.int32), axis=1)
    pick = req_of[:, None] == jnp.arange(lens.shape[0], dtype=jnp.int32)[None, :]
    first = jnp.sum(jnp.where(pick, starts[None, :], 0), axis=1)
    pool_rows = lax.all_gather(page_pool, "req", axis=0, tiled=True).reshape(
        pool_all * PAGE_TOKENS, 2 * row_width
    )
    counts = jnp.sum(
        (page_table[0][:, :, None] == jnp.arange(pool_all, dtype=jnp.int32)[None, None, :]).astype(
            jnp.float32
        ),
        axis=1,
    )
    query_counts = jnp.dot(pick.astype(jnp.float32), counts, precision=lax.Precision.HIGHEST)
    keypos = jnp.arange(lax.axis_size("exp") * token_index, dtype=jnp.int32)
    suffix_weights = (keypos[None, :] <= positions[:, None]) & (keypos[None, :] >= first[:, None])
    spread = (
        jnp.arange(pool_all, dtype=jnp.int32)[:, None]
        == jnp.arange(pool_all * PAGE_TOKENS, dtype=jnp.int32)[None, :] // PAGE_TOKENS
    ).astype(jnp.bfloat16)
    key_counts = jnp.dot(
        query_counts.astype(jnp.bfloat16), spread, preferred_element_type=jnp.float32
    )
    pool_weights = jnp.where(
        key_counts > 0, jnp.log2(jnp.maximum(key_counts, 1.0)), NEGATIVE_MASK
    )
    live = jnp.max(query_counts, axis=0) > 0
    live_int = live.astype(jnp.int32)
    live_count = jnp.sum(live_int)
    destination = jnp.where(
        live, jnp.cumsum(live_int) - 1, live_count + jnp.cumsum(1 - live_int) - 1
    )
    slots = jnp.arange(pool_all, dtype=jnp.int32)
    order = jnp.sum(
        jnp.where(destination[None, :] == slots[:, None], slots[None, :], 0), axis=1
    ).astype(jnp.int32)
    suffix_after, pool_weights, order, live_count = lax.optimization_barrier(
        (suffix_kv, pool_weights, order, live_count)
    )
    segment = lax.all_gather(suffix_after, "exp", axis=0, tiled=True)
    carry = flash(
        queries,
        pool_weights,
        pool_rows,
        None,
        True,
        False,
        KEY_VALUE_HEADS,
        HEAD_SIZE,
        (order, live_count),
        KEY_BLOCK // PAGE_TOKENS,
    )
    attended = flash(
        queries,
        jnp.where(suffix_weights, 0.0, NEGATIVE_MASK).astype(jnp.float32),
        segment,
        carry,
        False,
        True,
        KEY_VALUE_HEADS,
        HEAD_SIZE,
    )
    projected = jnp.dot(attended, w_out, preferred_element_type=jnp.float32)
    resid = lax.optimization_barrier((hidden.astype(jnp.float32) + projected).astype(jnp.bfloat16))
    resid_f = resid.astype(jnp.float32)
    normed = (resid_f * lax.rsqrt(jnp.mean(resid_f * resid_f, axis=1, keepdims=True) + EPS)).astype(
        jnp.bfloat16
    )
    n_experts = w_router.shape[1]
    logits = jnp.dot(normed, w_router, preferred_element_type=jnp.float32)
    expert_ids = jnp.arange(n_experts, dtype=jnp.int32)
    chosen = jnp.sum(
        jnp.where(routes[:, :, None] == expert_ids[None, None, :], logits[:, None, :], 0.0), axis=2
    )
    gates = jax.nn.softmax(chosen, axis=1)
    capacity = 16
    member = routes[:, :, None] == expert_ids[None, None, :]
    picks = jnp.any(member, axis=1).astype(jnp.float32)
    gate_of = jnp.sum(jnp.where(member, gates[:, :, None], 0.0), axis=1)
    earlier = (
        jnp.arange(token_index, dtype=jnp.int32)[:, None]
        > jnp.arange(token_index, dtype=jnp.int32)[None, :]
    ).astype(jnp.float32)
    rank = jnp.dot(earlier, picks, precision=lax.Precision.HIGHEST).astype(jnp.int32)
    place = jnp.arange(capacity, dtype=jnp.int32)
    select = (picks[None, :, :] > 0) & (rank[None, :, :] == place[:, None, None])
    select = jnp.transpose(select, (2, 0, 1))
    select2 = jnp.broadcast_to(
        select[:, None], (n_experts, 2, capacity, token_index)
    ).reshape(2 * n_experts * capacity, token_index)
    weight = jnp.where(
        jnp.transpose(select, (2, 0, 1))[:, :, None, :],
        gate_of[:, :, None, None],
        0.0,
    )
    weight = jnp.broadcast_to(weight, (token_index, n_experts, 2, capacity))
    chunks = 2
    part = capacity // chunks
    select2 = select2.reshape(2 * n_experts, capacity, token_index)
    moe = resid_f
    for c in range(chunks):
        picked_rows = select2[:, c * part:(c + 1) * part].reshape(-1, token_index)
        outgoing = jnp.dot(
            picked_rows.astype(jnp.bfloat16), normed, preferred_element_type=jnp.float32
        ).astype(jnp.bfloat16)
        outgoing = outgoing.reshape(2 * n_experts, part, D)
        rows = lax.all_to_all(outgoing, ("req", "exp"), split_axis=0, concat_axis=0, tiled=True)
        flat_rows = rows.reshape(-1, D)
        gate_part = jnp.dot(flat_rows, w_gate[0], preferred_element_type=jnp.float32)
        up_part = jnp.dot(flat_rows, w_up[0], preferred_element_type=jnp.float32)
        inner = (jax.nn.silu(gate_part) * up_part).astype(jnp.bfloat16)
        returned = lax.all_to_all(
            jnp.dot(inner, w_down[0], preferred_element_type=jnp.float32)
            .astype(jnp.bfloat16)
            .reshape(rows.shape),
            ("req", "exp"),
            split_axis=0,
            concat_axis=0,
            tiled=True,
        ).reshape(-1, D)
        chunk_weight = weight[:, :, :, c * part:(c + 1) * part].reshape(token_index, -1)
        high = chunk_weight.astype(jnp.bfloat16)
        low = (chunk_weight - high.astype(jnp.float32)).astype(jnp.bfloat16)
        both = jnp.dot(
            jnp.concatenate([high, low], axis=0), returned, preferred_element_type=jnp.float32
        )
        moe = moe + both[:token_index] + both[token_index:]
    return moe.astype(jnp.bfloat16)


def solution(mesh):
    placed = (
        P(("req", "exp"), None),
        P(("req", "exp"), None),
        P(("req", "exp"), None),
        P("req", None),
        P("req", None, None),
        P("req", None, None),
        P(),
        P(),
        P(("req", "exp"), None),
        P(("req", "exp"), None, None),
        P(("req", "exp"), None, None),
        P(("req", "exp"), None, None),
    )
    return jax.shard_map(
        on_device, mesh=mesh, in_specs=placed, out_specs=P(("req", "exp"), None), check_vma=False
    )
```
